128 devices in a mesh: seq: 32 (over z, y, core), tp: 4 (over x).
Axes of the slice: x: 4, y: 4, z: 4, core: 2. Of those that a mesh axis runs over, the one named last changes fastest.
Arguments:
- tokens: bfloat16 [16384, 1408], P('seq'), may hold values from -70 to 70
- group_image: int32 [4096], P('seq'), may hold values from 0 to 31, never falling along the last dimension, each value on 1 to 512 neighbouring positions
- image_slot: int32 [32], replicated, may hold values from 0 to 31, each once
- attention_gain: float32 [1408], replicated, may hold values from 0.1 to 1.9
- query_weight: bfloat16 [1408, 1408], P(None, 'tp'), may hold values from -1.11930376 to 1.11930376
- key_weight: bfloat16 [1408, 1408], P(None, 'tp'), may hold values from -1.11930376 to 1.11930376
- value_weight: bfloat16 [1408, 1408], P(None, 'tp'), may hold values from -1.25 to 1.25
- output_weight: bfloat16 [1408, 1408], P('tp'), may hold values from -0.15625 to 0.15625
- feedforward_gain: float32 [1408], replicated, may hold values from 0.1 to 1.9
- up_weight: bfloat16 [1408, 6144], P(None, 'tp'), may hold values from -0.15625 to 0.15625
- down_weight: bfloat16 [6144, 1408], P('tp'), may hold values from -0.078125 to 0.078125
- merge_gain: float32 [1408], replicated, may hold values from 0.1 to 1.9
- merge_weight: bfloat16 [5632, 3584], P(None, 'tp'), may hold values from -0.078125 to 0.078125
Outputs:
- merged_rows: bfloat16 [32, 512, 3584], P('seq', None, 'tp')
The draws below stay inside these ranges and needn't reach their ends.
Inputs may be any that keep to these rules, and one draw needn't show every extreme that they name: `group_image`: images are numbered in the order of their groups, each covers consecutive groups, 1 to 512 of them, and one covers exactly 512.
All inputs are finite; a program needn't handle non-finite values.
Results may differ from the reference program's by a relative error of at most 0.012.
Values may be sent and summed in bfloat16 or wider, within the bound.
No kernel may reach another device: no remote copies, remote signals or barrier semaphores. Data moves between devices by JAX's collectives and lax.ppermute only.
A program may use at most 192 MiB of HBM per device.

```python
import math
import jax
import jax.numpy as jnp
import numpy as np
from jax import lax

D = 1408
HEADS = 16
HD = 88
FF = 6144
OUT = 3584
REACH = 4
TOK_DEV = 512
TOKENS = 16384
GROUPS = 4096
NIMG = 32
MOSTG = 512
N_SEQ = 32


def draw_tokens(key, part):
    normal_part = jnp.clip(jax.random.normal(jax.random.fold_in(key, 1), (TOKENS, D), jnp.float32), -6.0, 6.0)
    return normal_part.astype(jnp.bfloat16)


def query_key(key, which):
    private = jnp.clip(jax.random.normal(jax.random.fold_in(key, 12 + which), (D, D), jnp.float32), -6.0, 6.0)
    matrix = 1.5 * private
    return (matrix * D ** (-0.5)).astype(jnp.bfloat16)


def draw_query_weight(key, part):
    return query_key(key, 0)


def draw_key_weight(key, part):
    return query_key(key, 1)


def steps_of(own_key, shape, cuts, smallest, top_value):
    level, own = 1.0, jax.random.fold_in(own_key, 6)
    for position, shards_of in cuts:
        steps = jnp.exp(jax.random.uniform(jax.random.fold_in(own, position), (shards_of,), jnp.float32, smallest / len(cuts), top_value / len(cuts)))
        level = level * jnp.repeat(steps, shape[position] // shards_of).reshape([-1 if axis == position else 1 for axis in range(len(shape))])
    return level


def split_up(amount, total, limit, slope):
    loads = [(1 << 20) // math.isqrt(rank ** slope) + 1 for rank in range(2, amount + 1)]
    rest, given = total - limit - (amount - 1), [1] * (amount - 1)
    while rest > 0:
        free = [i for i in range(amount - 1) if given[i] < limit]
        mass, budget = sum([loads[i] for i in free]), rest
        for i in free:
            more = min(limit - given[i], max(1, budget * loads[i] // mass), rest)
            given[i] = given[i] + more
            rest = rest - more
    return np.array([limit] + given)


def uneven(rng, amount, total, most, slope):
    if amount == 2:
        one = jax.random.randint(rng, (), max(1, total - most), min(most, total - 1) + 1)
        return jnp.stack([one, total - one])
    tallies = jnp.asarray(split_up(amount, total, most, slope), jnp.int32)
    couples = (amount - 1) // 2
    donor, taker = tallies[1:1 + 2 * couples:2], tallies[2:2 + 2 * couples:2]
    slack = jnp.minimum(donor - 1, most - taker)
    shifted = jax.random.randint(jax.random.fold_in(rng, 1), (couples,), 0, 1 << 20) % (slack + 1)
    tallies = tallies.at[1:1 + 2 * couples:2].set(donor - shifted).at[2:2 + 2 * couples:2].set(taker + shifted)
    return tallies[jax.random.permutation(jax.random.fold_in(rng, 2), amount)]


def normal_values(stream_key, dims, width, reach, cuts=(), kind=jnp.bfloat16):
    gain = steps_of(stream_key, dims, cuts, -0.22, 0.18) if cuts else 1.0
    drawn = jax.random.normal(stream_key, dims, jnp.float32) * width * gain
    return jnp.minimum(jnp.maximum(drawn, -reach), reach).astype(kind)


def setup_inputs(seed: int = 0) -> dict:
    streams_of = jax.random.split(jax.random.key(seed), 14)
    return {
        "tokens": draw_tokens(jax.random.fold_in(streams_of[13], 71), 0),
        "group_image": jnp.searchsorted(jnp.cumsum(uneven(streams_of[1], NIMG, GROUPS, MOSTG, 2)), jnp.arange(GROUPS), side="right").astype(jnp.int32),
        "image_slot": jax.random.permutation(streams_of[2], NIMG).astype(jnp.int32),
        "attention_gain": jnp.clip(1.0 + 0.18 * jax.random.normal(streams_of[3], (D,), jnp.float32), 0.1, 1.9),
        "query_weight": draw_query_weight(jax.random.fold_in(streams_of[13], 71), 0),
        "key_weight": draw_key_weight(jax.random.fold_in(streams_of[13], 71), 0),
        "value_weight": normal_values(streams_of[6], (D, D), (D // 64) ** -0.5, 1.25, ((1, 4),)),
        "output_weight": normal_values(streams_of[7], (D, D), D ** -0.5, 0.15625, ((0, 4),)),
        "feedforward_gain": jnp.clip(1.0 + 0.18 * jax.random.normal(streams_of[8], (D,), jnp.float32), 0.1, 1.9),
        "up_weight": normal_values(streams_of[9], (D, FF), D ** -0.5, 0.15625, ((1, 4),)),
        "down_weight": normal_values(streams_of[10], (FF, D), FF ** -0.5, 0.078125, ((0, 4),)),
        "merge_gain": jnp.clip(1.0 + 0.18 * jax.random.normal(streams_of[11], (D,), jnp.float32), 0.1, 1.9),
        "merge_weight": normal_values(streams_of[12], (4 * D, OUT), (4 * D) ** -0.5, 0.078125, ((1, 4),)),
    }


epsilon = 1e-06
masked_score = -1e+30

def layer_norm(hidden, norm_gain):
    row_mean = lax.optimization_barrier(jnp.mean(hidden, axis=1, keepdims=True))
    square = lax.optimization_barrier(jnp.mean(hidden * hidden, axis=1, keepdims=True))
    return ((hidden - row_mean) * lax.rsqrt(square - row_mean * row_mean + epsilon) * norm_gain).astype(jnp.bfloat16)

def reference(tokens, group_image, image_slot, attention_gain, query_weight, key_weight, value_weight, output_weight, feedforward_gain, up_weight, down_weight, merge_gain, merge_weight):
    token_image = jnp.repeat(group_image, 4)
    residual = tokens.astype(jnp.float32)
    normed = layer_norm(residual, attention_gain)
    queries = jnp.dot(normed, query_weight, preferred_element_type=jnp.float32).astype(jnp.bfloat16).reshape(TOKENS, HEADS, HD)
    key_rows = jnp.dot(normed, key_weight, preferred_element_type=jnp.float32).astype(jnp.bfloat16).reshape(TOKENS, HEADS, HD)
    value_rows = jnp.dot(normed, value_weight, preferred_element_type=jnp.float32).astype(jnp.bfloat16).reshape(TOKENS, HEADS, HD)
    reach_rows = REACH * TOK_DEV
    window = (2 * REACH + 1) * TOK_DEV
    zero_pad = jnp.zeros((reach_rows, HEADS, HD), jnp.bfloat16)
    key_padded = jnp.concatenate([zero_pad, key_rows, zero_pad], axis=0)
    value_padded = jnp.concatenate([zero_pad, value_rows, zero_pad], axis=0)
    image_pad = jnp.full((reach_rows,), -1, jnp.int32)
    image_padded = jnp.concatenate([image_pad, token_image, image_pad], axis=0)
    score_scale = HD ** (-0.5)

    def attend(block_index):
        first_row = (block_index * TOK_DEV).astype(jnp.int32)
        query_block = lax.dynamic_slice_in_dim(queries, first_row, TOK_DEV, 0).astype(jnp.float32)
        key_block = lax.dynamic_slice_in_dim(key_padded, first_row, window, 0).astype(jnp.float32)
        value_block = lax.dynamic_slice_in_dim(value_padded, first_row, window, 0).astype(jnp.float32)
        query_image = lax.dynamic_slice_in_dim(token_image, first_row, TOK_DEV, 0)
        key_image = lax.dynamic_slice_in_dim(image_padded, first_row, window, 0)
        scores = jnp.einsum('qhd,khd->hqk', query_block, key_block) * score_scale
        same_image = query_image[:, None] == key_image[None, :]
        scores = jnp.where(same_image[None], scores, masked_score)
        row_best = lax.optimization_barrier(jnp.max(scores, axis=2, keepdims=True))
        weights = jnp.exp(scores - row_best)
        row_total = lax.optimization_barrier(jnp.sum(weights, axis=2))
        rounded = lax.optimization_barrier(weights.astype(jnp.bfloat16)).astype(jnp.float32)
        weighted = jnp.einsum('hqk,khd->qhd', rounded, value_block)
        return (weighted / jnp.transpose(row_total)[:, :, None]).astype(jnp.bfloat16).reshape(TOK_DEV, D)
    context = lax.map(attend, jnp.arange(N_SEQ, dtype=jnp.int32)).reshape(TOKENS, D)
    after_attention = residual + jnp.dot(context, output_weight, preferred_element_type=jnp.float32)
    normed_two = layer_norm(after_attention, feedforward_gain)
    hidden_units = jax.nn.gelu(jnp.dot(normed_two, up_weight, preferred_element_type=jnp.float32), approximate=False).astype(jnp.bfloat16)
    after_feedforward = after_attention + jnp.dot(hidden_units, down_weight, preferred_element_type=jnp.float32)
    normed_three = layer_norm(after_feedforward, merge_gain)
    grouped = normed_three.reshape(TOKENS // 4, 4 * D)
    projected = jnp.dot(grouped, merge_weight, preferred_element_type=jnp.float32).astype(jnp.bfloat16)
    image_ids = jnp.arange(NIMG, dtype=jnp.int32)
    onehot = (group_image[:, None] == image_ids[None, :]).astype(jnp.int32)
    counts = lax.optimization_barrier(jnp.sum(onehot, axis=0)).astype(jnp.int32)
    starts = (jnp.cumsum(counts) - counts).astype(jnp.int32)
    padded = jnp.concatenate([projected, jnp.zeros((MOSTG, OUT), jnp.bfloat16)], axis=0)

    def take_block(first_row, group_count):
        own_block = lax.dynamic_slice_in_dim(padded, first_row, MOSTG, 0)
        kept_rows = jnp.arange(MOSTG, dtype=jnp.int32) < group_count
        return jnp.where(kept_rows[:, None], own_block, jnp.zeros_like(own_block))
    blocks = jax.vmap(take_block)(starts, counts)
    return jnp.zeros((NIMG, MOSTG, OUT), jnp.bfloat16).at[image_slot].set(blocks)
```

```python
import jax
import jax.numpy as jnp
from jax import lax
from jax.sharding import PartitionSpec as P

D = 1408
HD = 88
REACH = 4


epsilon = 1e-06
masked_score = -1e30


def shifted(value, axis, steps):
    count = lax.axis_size(axis)
    initial, last = (max(0, -steps), min(count, count - steps))
    return lax.ppermute(value, axis, [(source, source + steps) for source in range(initial, last)])


def finish_norm(hidden, row_mean, square, norm_gain):
    return (
        (hidden - row_mean) * lax.rsqrt(square - row_mean * row_mean + epsilon) * norm_gain
    ).astype(jnp.bfloat16)


def full_norm(hidden, norm_gain):
    row_mean = jnp.mean(hidden, axis=1, keepdims=True)
    square = jnp.mean(hidden * hidden, axis=1, keepdims=True)
    return finish_norm(hidden, row_mean, square, norm_gain)


def sum_rows(partial_value):
    return lax.psum(partial_value, "tp")


def attend_window(query_heads, key_heads, value_heads, query_image, key_image):
    scores = jnp.einsum(
        "qhd,khd->hqk", query_heads, key_heads, preferred_element_type=jnp.float32
    ) * HD ** (-0.5)
    same_image = query_image[:, None] == key_image[None, :]
    scores = jnp.where(same_image[None], scores, masked_score)
    row_best = jnp.max(scores, axis=2, keepdims=True)
    weights = jnp.exp(scores - row_best)
    row_total = jnp.sum(weights, axis=2)
    weighted = jnp.einsum(
        "hqk,khd->qhd",
        weights.astype(jnp.bfloat16),
        value_heads,
        preferred_element_type=jnp.float32,
    )
    return weighted / jnp.transpose(row_total)[:, :, None]


def image_of_groups(groups, starts, group_total):
    inside = (groups >= 0) & (groups < group_total)
    image = jnp.sum((starts[None, :] <= groups[:, None]).astype(jnp.int32), axis=1) - 1
    return jnp.where(inside, image, -1)


def route_to_owners(projected, starts, counts, image_slot, device, seq_count):
    group_rows, out_cols = projected.shape
    per_pair = group_rows // seq_count
    spread = projected.reshape(per_pair, seq_count, out_cols).transpose(1, 0, 2)
    spread = lax.all_to_all(spread, "seq", split_axis=0, concat_axis=0, tiled=True)
    held = spread.reshape(group_rows, out_cols)
    image_count = image_slot.shape[0]
    most_rows = REACH * group_rows
    per_owner = most_rows // seq_count
    image_ids = jnp.arange(image_count, dtype=jnp.int32)
    owners = jnp.arange(seq_count, dtype=jnp.int32)
    owned_image = jnp.sum(
        jnp.where(image_slot[None, :] == owners[:, None], image_ids[None, :], 0), axis=1
    )
    owner_start = starts[owned_image]
    owner_count = counts[owned_image]
    first_pos = jnp.mod(device - owner_start, seq_count)
    first_row = (owner_start + first_pos - device) // seq_count
    steps = jnp.arange(per_owner, dtype=jnp.int32)
    rows = first_row[:, None] + steps[None, :]
    valid = (first_pos[:, None] + seq_count * steps[None, :]) < owner_count[:, None]
    rows = jnp.clip(rows, 0, group_rows - 1)
    outgoing = jnp.take(held, rows.reshape(-1), axis=0).reshape(seq_count, per_owner, out_cols)
    outgoing = jnp.where(valid[:, :, None], outgoing, jnp.zeros((), outgoing.dtype))
    received = lax.all_to_all(outgoing, "seq", split_axis=0, concat_axis=0, tiled=True)
    own_image = jnp.sum(jnp.where(image_slot == device, image_ids, 0))
    own_start = starts[own_image]
    order = jnp.mod(own_start + jnp.arange(seq_count, dtype=jnp.int32), seq_count)
    placed = jnp.take(received, order, axis=0).transpose(1, 0, 2)
    return placed.reshape(most_rows, out_cols)


def shards(
    tokens,
    group_image,
    image_slot,
    attention_gain,
    query_weight,
    key_weight,
    value_weight,
    output_weight,
    feedforward_gain,
    up_weight,
    down_weight,
    merge_gain,
    merge_weight,
):
    device = lax.axis_index("seq")
    seq_count = lax.axis_size("seq")
    token_rows = tokens.shape[0]
    group_rows = group_image.shape[0]
    group_total = group_rows * seq_count
    image_count = image_slot.shape[0]
    image_ids = jnp.arange(image_count, dtype=jnp.int32)
    local_counts = jnp.sum(
        (group_image[:, None] == image_ids[None, :]).astype(jnp.int32), axis=0
    )
    counts = lax.psum(local_counts, "seq")
    starts = jnp.cumsum(counts) - counts
    query_image = jnp.repeat(group_image, 4)
    residual = tokens.astype(jnp.float32)
    normed = full_norm(residual, attention_gain)
    head_count = query_weight.shape[1] // HD
    queries = jnp.dot(normed, query_weight, preferred_element_type=jnp.float32).astype(jnp.bfloat16)
    key_rows = jnp.dot(normed, key_weight, preferred_element_type=jnp.float32).astype(jnp.bfloat16)
    value_rows = jnp.dot(normed, value_weight, preferred_element_type=jnp.float32).astype(
        jnp.bfloat16
    )
    query_heads = queries.reshape(token_rows, head_count, HD)
    key_value = jnp.stack([key_rows, value_rows])
    arrived = []
    for offset in range(REACH, -REACH - 1, -1):
        if offset == 0:
            arrived.append(key_value)
        else:
            arrived.append(shifted(key_value, "seq", offset))
    window = jnp.concatenate(arrived, axis=1)
    window_groups = (device - REACH) * group_rows + jnp.arange(
        (2 * REACH + 1) * group_rows, dtype=jnp.int32
    )
    key_image = jnp.repeat(image_of_groups(window_groups, starts, group_total), 4)
    context = attend_window(
        query_heads,
        window[0].reshape(-1, head_count, HD),
        window[1].reshape(-1, head_count, HD),
        query_image,
        key_image,
    )
    context = context.astype(jnp.bfloat16).reshape(token_rows, head_count * HD)
    attention_part = jnp.dot(context, output_weight, preferred_element_type=jnp.float32)
    after_attention = residual + sum_rows(attention_part)
    normed_two = full_norm(after_attention, feedforward_gain)
    hidden_units = jax.nn.gelu(
        jnp.dot(normed_two, up_weight, preferred_element_type=jnp.float32), approximate=False
    ).astype(jnp.bfloat16)
    after_feedforward = after_attention + sum_rows(
        jnp.dot(hidden_units, down_weight, preferred_element_type=jnp.float32)
    )
    normed_three = full_norm(after_feedforward, merge_gain)
    grouped = normed_three.reshape(group_rows, 4 * D)
    projected = jnp.dot(grouped, merge_weight, preferred_element_type=jnp.float32).astype(
        jnp.bfloat16
    )
    return route_to_owners(projected, starts, counts, image_slot, device, seq_count)[None]


def solution(mesh):
    return jax.shard_map(
        shards,
        mesh=mesh,
        in_specs=(
            P("seq", None),
            P("seq"),
            P(),
            P(),
            P(None, "tp"),
            P(None, "tp"),
            P(None, "tp"),
            P("tp", None),
            P(),
            P(None, "tp"),
            P("tp", None),
            P(),
            P(None, "tp"),
        ),
        out_specs=P("seq", None, "tp"),
        check_vma=False,
    )
```

```python
import jax
import jax.numpy as jnp
from jax import lax
from jax.sharding import PartitionSpec as P

D = 1408
HD = 88
REACH = 4


epsilon = 1e-06
masked_score = -1e30


def shifted(value, axis, steps):
    count = lax.axis_size(axis)
    initial, last = (max(0, -steps), min(count, count - steps))
    return lax.ppermute(value, axis, [(source, source + steps) for source in range(initial, last)])


def finish_norm(hidden, row_mean, square, norm_gain):
    return (
        (hidden - row_mean) * lax.rsqrt(square - row_mean * row_mean + epsilon) * norm_gain
    ).astype(jnp.bfloat16)


def full_norm(hidden, norm_gain):
    row_mean = jnp.mean(hidden, axis=1, keepdims=True)
    square = jnp.mean(hidden * hidden, axis=1, keepdims=True)
    return finish_norm(hidden, row_mean, square, norm_gain)


def sum_rows(partial_value):
    tp_count = lax.axis_size("tp")
    rows, cols = partial_value.shape
    pieces = partial_value.astype(jnp.bfloat16).reshape(tp_count, rows // tp_count, cols)
    pieces = lax.all_to_all(pieces, "tp", split_axis=0, concat_axis=0, tiled=True)
    return jnp.sum(pieces.astype(jnp.float32), axis=0)


def gather_rows(row_block):
    return lax.all_gather(row_block, "tp", axis=0, tiled=True)


def attend_window(query_heads, key_heads, value_heads, query_image, key_image):
    scores = jnp.einsum(
        "qhd,khd->hqk", query_heads, key_heads, preferred_element_type=jnp.float32
    ) * HD ** (-0.5)
    same_image = query_image[:, None] == key_image[None, :]
    scores = jnp.where(same_image[None], scores, masked_score)
    row_best = jnp.max(scores, axis=2, keepdims=True)
    weights = jnp.exp(scores - row_best)
    row_total = jnp.sum(weights, axis=2)
    weighted = jnp.einsum(
        "hqk,khd->qhd",
        weights.astype(jnp.bfloat16),
        value_heads,
        preferred_element_type=jnp.float32,
    )
    return weighted / jnp.transpose(row_total)[:, :, None]


def image_of_groups(groups, starts, group_total):
    inside = (groups >= 0) & (groups < group_total)
    image = jnp.sum((starts[None, :] <= groups[:, None]).astype(jnp.int32), axis=1) - 1
    return jnp.where(inside, image, -1)


def route_to_owners(projected, starts, counts, image_slot, device, seq_count):
    group_rows, out_cols = projected.shape
    per_pair = group_rows // seq_count
    spread = projected.reshape(per_pair, seq_count, out_cols).transpose(1, 0, 2)
    spread = lax.all_to_all(spread, "seq", split_axis=0, concat_axis=0, tiled=True)
    held = spread.reshape(group_rows, out_cols)
    image_count = image_slot.shape[0]
    most_rows = REACH * group_rows
    per_owner = most_rows // seq_count
    image_ids = jnp.arange(image_count, dtype=jnp.int32)
    owners = jnp.arange(seq_count, dtype=jnp.int32)
    owned_image = jnp.sum(
        jnp.where(image_slot[None, :] == owners[:, None], image_ids[None, :], 0), axis=1
    )
    owner_start = starts[owned_image]
    owner_count = counts[owned_image]
    first_pos = jnp.mod(device - owner_start, seq_count)
    first_row = (owner_start + first_pos - device) // seq_count
    steps = jnp.arange(per_owner, dtype=jnp.int32)
    rows = first_row[:, None] + steps[None, :]
    valid = (first_pos[:, None] + seq_count * steps[None, :]) < owner_count[:, None]
    rows = jnp.clip(rows, 0, group_rows - 1)
    outgoing = jnp.take(held, rows.reshape(-1), axis=0).reshape(seq_count, per_owner, out_cols)
    outgoing = jnp.where(valid[:, :, None], outgoing, jnp.zeros((), outgoing.dtype))
    received = lax.all_to_all(outgoing, "seq", split_axis=0, concat_axis=0, tiled=True)
    own_image = jnp.sum(jnp.where(image_slot == device, image_ids, 0))
    own_start = starts[own_image]
    order = jnp.mod(own_start + jnp.arange(seq_count, dtype=jnp.int32), seq_count)
    placed = jnp.take(received, order, axis=0).transpose(1, 0, 2)
    return placed.reshape(most_rows, out_cols)


def shards(
    tokens,
    group_image,
    image_slot,
    attention_gain,
    query_weight,
    key_weight,
    value_weight,
    output_weight,
    feedforward_gain,
    up_weight,
    down_weight,
    merge_gain,
    merge_weight,
):
    device = lax.axis_index("seq")
    seq_count = lax.axis_size("seq")
    token_rows = tokens.shape[0]
    group_rows = group_image.shape[0]
    group_total = group_rows * seq_count
    image_count = image_slot.shape[0]
    image_ids = jnp.arange(image_count, dtype=jnp.int32)
    local_counts = jnp.sum(
        (group_image[:, None] == image_ids[None, :]).astype(jnp.int32), axis=0
    )
    every_count = lax.all_to_all(
        jnp.broadcast_to(local_counts[None, :], (seq_count, image_count)),
        "seq",
        split_axis=0,
        concat_axis=0,
        tiled=True,
    )
    counts = jnp.sum(every_count, axis=0)
    starts = jnp.cumsum(counts) - counts
    query_image = jnp.repeat(group_image, 4)
    residual = tokens.astype(jnp.float32)
    normed = full_norm(residual, attention_gain)
    head_count = query_weight.shape[1] // HD
    queries = jnp.dot(normed, query_weight, preferred_element_type=jnp.float32).astype(jnp.bfloat16)
    key_rows = jnp.dot(normed, key_weight, preferred_element_type=jnp.float32).astype(jnp.bfloat16)
    value_rows = jnp.dot(normed, value_weight, preferred_element_type=jnp.float32).astype(
        jnp.bfloat16
    )
    query_heads = queries.reshape(token_rows, head_count, HD)
    key_value = jnp.stack([key_rows, value_rows])
    arrived = []
    for offset in range(REACH, -REACH - 1, -1):
        if offset == 0:
            arrived.append(key_value)
        else:
            arrived.append(shifted(key_value, "seq", offset))
    window = jnp.concatenate(arrived, axis=1)
    window_groups = (device - REACH) * group_rows + jnp.arange(
        (2 * REACH + 1) * group_rows, dtype=jnp.int32
    )
    key_image = jnp.repeat(image_of_groups(window_groups, starts, group_total), 4)
    context = attend_window(
        query_heads,
        window[0].reshape(-1, head_count, HD),
        window[1].reshape(-1, head_count, HD),
        query_image,
        key_image,
    )
    context = context.astype(jnp.bfloat16).reshape(token_rows, head_count * HD)
    attention_part = jnp.dot(context, output_weight, preferred_element_type=jnp.float32)
    tp_count = lax.axis_size("tp")
    own_rows = token_rows // tp_count
    own_residual = lax.dynamic_slice_in_dim(residual, lax.axis_index("tp") * own_rows, own_rows, 0)
    after_attention = own_residual + sum_rows(attention_part)
    normed_two = gather_rows(full_norm(after_attention, feedforward_gain))
    hidden_units = jax.nn.gelu(
        jnp.dot(normed_two, up_weight, preferred_element_type=jnp.float32), approximate=False
    ).astype(jnp.bfloat16)
    after_feedforward = after_attention + sum_rows(
        jnp.dot(hidden_units, down_weight, preferred_element_type=jnp.float32)
    )
    normed_three = gather_rows(full_norm(after_feedforward, merge_gain))
    grouped = normed_three.reshape(group_rows, 4 * D)
    projected = jnp.dot(grouped, merge_weight, preferred_element_type=jnp.float32).astype(
        jnp.bfloat16
    )
    return route_to_owners(projected, starts, counts, image_slot, device, seq_count)[None]


def solution(mesh):
    return jax.shard_map(
        shards,
        mesh=mesh,
        in_specs=(
            P("seq", None),
            P("seq"),
            P(),
            P(),
            P(None, "tp"),
            P(None, "tp"),
            P(None, "tp"),
            P("tp", None),
            P(),
            P(None, "tp"),
            P("tp", None),
            P(),
            P(None, "tp"),
        ),
        out_specs=P("seq", None, "tp"),
        check_vma=False,
    )
```

```python
import jax
import jax.numpy as jnp
from jax import lax
from jax.sharding import PartitionSpec as P

D = 1408
HD = 88
REACH = 4


epsilon = 1e-06
masked_score = -1e30


def shifted(value, axis, steps):
    count = lax.axis_size(axis)
    initial, last = (max(0, -steps), min(count, count - steps))
    return lax.ppermute(value, axis, [(source, source + steps) for source in range(initial, last)])


def finish_norm(hidden, row_mean, square, norm_gain):
    return (
        (hidden - row_mean) * lax.rsqrt(square - row_mean * row_mean + epsilon) * norm_gain
    ).astype(jnp.bfloat16)


def full_norm(hidden, norm_gain):
    row_mean = jnp.mean(hidden, axis=1, keepdims=True)
    square = jnp.mean(hidden * hidden, axis=1, keepdims=True)
    return finish_norm(hidden, row_mean, square, norm_gain)


def sum_rows(partial_value):
    tp_count = lax.axis_size("tp")
    rows, cols = partial_value.shape
    pieces = partial_value.astype(jnp.bfloat16).reshape(tp_count, rows // tp_count, cols)
    pieces = lax.all_to_all(pieces, "tp", split_axis=0, concat_axis=0, tiled=True)
    return jnp.sum(pieces.astype(jnp.float32), axis=0)


def gather_rows(row_block):
    tp_count = lax.axis_size("tp")
    copies = jnp.broadcast_to(row_block[None], (tp_count,) + row_block.shape)
    copies = lax.all_to_all(copies, "tp", split_axis=0, concat_axis=0, tiled=True)
    return copies.reshape(tp_count * row_block.shape[0], row_block.shape[1])


def attend_window(query_heads, key_heads, value_heads, query_image, key_image):
    scores = jnp.einsum(
        "qhd,khd->hqk", query_heads, key_heads, preferred_element_type=jnp.float32
    ) * HD ** (-0.5)
    same_image = query_image[:, None] == key_image[None, :]
    scores = jnp.where(same_image[None], scores, masked_score)
    row_best = jnp.max(scores, axis=2, keepdims=True)
    weights = jnp.exp(scores - row_best)
    row_total = jnp.sum(weights, axis=2)
    weighted = jnp.einsum(
        "hqk,khd->qhd",
        weights.astype(jnp.bfloat16),
        value_heads,
        preferred_element_type=jnp.float32,
    )
    return weighted / jnp.transpose(row_total)[:, :, None]


def image_of_groups(groups, starts, group_total):
    inside = (groups >= 0) & (groups < group_total)
    image = jnp.sum((starts[None, :] <= groups[:, None]).astype(jnp.int32), axis=1) - 1
    return jnp.where(inside, image, -1)


def route_to_owners(projected, starts, counts, image_slot, device, seq_count):
    group_rows, out_cols = projected.shape
    per_pair = group_rows // seq_count
    spread = projected.reshape(per_pair, seq_count, out_cols).transpose(1, 0, 2)
    spread = lax.all_to_all(spread, "seq", split_axis=0, concat_axis=0, tiled=True)
    held = spread.reshape(group_rows, out_cols)
    image_count = image_slot.shape[0]
    most_rows = REACH * group_rows
    per_owner = most_rows // seq_count
    image_ids = jnp.arange(image_count, dtype=jnp.int32)
    owners = jnp.arange(seq_count, dtype=jnp.int32)
    owned_image = jnp.sum(
        jnp.where(image_slot[None, :] == owners[:, None], image_ids[None, :], 0), axis=1
    )
    owner_start = starts[owned_image]
    owner_count = counts[owned_image]
    first_pos = jnp.mod(device - owner_start, seq_count)
    first_row = (owner_start + first_pos - device) // seq_count
    steps = jnp.arange(per_owner, dtype=jnp.int32)
    rows = first_row[:, None] + steps[None, :]
    valid = (first_pos[:, None] + seq_count * steps[None, :]) < owner_count[:, None]
    rows = jnp.clip(rows, 0, group_rows - 1)
    outgoing = jnp.take(held, rows.reshape(-1), axis=0).reshape(seq_count, per_owner, out_cols)
    outgoing = jnp.where(valid[:, :, None], outgoing, jnp.zeros((), outgoing.dtype))
    received = lax.all_to_all(outgoing, "seq", split_axis=0, concat_axis=0, tiled=True)
    own_image = jnp.sum(jnp.where(image_slot == device, image_ids, 0))
    own_start = starts[own_image]
    order = jnp.mod(own_start + jnp.arange(seq_count, dtype=jnp.int32), seq_count)
    placed = jnp.take(received, order, axis=0).transpose(1, 0, 2)
    return placed.reshape(most_rows, out_cols)


def shards(
    tokens,
    group_image,
    image_slot,
    attention_gain,
    query_weight,
    key_weight,
    value_weight,
    output_weight,
    feedforward_gain,
    up_weight,
    down_weight,
    merge_gain,
    merge_weight,
):
    device = lax.axis_index("seq")
    seq_count = lax.axis_size("seq")
    token_rows = tokens.shape[0]
    group_rows = group_image.shape[0]
    group_total = group_rows * seq_count
    image_count = image_slot.shape[0]
    image_ids = jnp.arange(image_count, dtype=jnp.int32)
    local_counts = jnp.sum(
        (group_image[:, None] == image_ids[None, :]).astype(jnp.int32), axis=0
    )
    every_count = lax.all_to_all(
        jnp.broadcast_to(local_counts[None, :], (seq_count, image_count)),
        "seq",
        split_axis=0,
        concat_axis=0,
        tiled=True,
    )
    counts = jnp.sum(every_count, axis=0)
    starts = jnp.cumsum(counts) - counts
    query_image = jnp.repeat(group_image, 4)
    residual = tokens.astype(jnp.float32)
    normed = full_norm(residual, attention_gain)
    head_count = query_weight.shape[1] // HD
    queries = jnp.dot(normed, query_weight, preferred_element_type=jnp.float32).astype(jnp.bfloat16)
    key_rows = jnp.dot(normed, key_weight, preferred_element_type=jnp.float32).astype(jnp.bfloat16)
    value_rows = jnp.dot(normed, value_weight, preferred_element_type=jnp.float32).astype(
        jnp.bfloat16
    )
    query_heads = queries.reshape(token_rows, head_count, HD)
    key_value = jnp.stack([key_rows, value_rows])
    counts, key_value = lax.optimization_barrier((counts, key_value))
    arrived = []
    for offset in range(REACH, -REACH - 1, -1):
        if offset == 0:
            arrived.append(key_value)
        else:
            arrived.append(shifted(key_value, "seq", offset))
    window = jnp.concatenate(arrived, axis=1)
    window_groups = (device - REACH) * group_rows + jnp.arange(
        (2 * REACH + 1) * group_rows, dtype=jnp.int32
    )
    key_image = jnp.repeat(image_of_groups(window_groups, starts, group_total), 4)
    context = attend_window(
        query_heads,
        window[0].reshape(-1, head_count, HD),
        window[1].reshape(-1, head_count, HD),
        query_image,
        key_image,
    )
    context = context.astype(jnp.bfloat16).reshape(token_rows, head_count * HD)
    attention_part = jnp.dot(context, output_weight, preferred_element_type=jnp.float32)
    tp_count = lax.axis_size("tp")
    own_rows = token_rows // tp_count
    own_residual = lax.dynamic_slice_in_dim(residual, lax.axis_index("tp") * own_rows, own_rows, 0)
    after_attention = own_residual + sum_rows(attention_part)
    normed_two = gather_rows(full_norm(after_attention, feedforward_gain))
    hidden_units = jax.nn.gelu(
        jnp.dot(normed_two, up_weight, preferred_element_type=jnp.float32), approximate=False
    ).astype(jnp.bfloat16)
    after_feedforward = after_attention + sum_rows(
        jnp.dot(hidden_units, down_weight, preferred_element_type=jnp.float32)
    )
    normed_three = gather_rows(full_norm(after_feedforward, merge_gain))
    grouped = normed_three.reshape(group_rows, 4 * D)
    projected = jnp.dot(grouped, merge_weight, preferred_element_type=jnp.float32).astype(
        jnp.bfloat16
    )
    return route_to_owners(projected, starts, counts, image_slot, device, seq_count)[None]


def solution(mesh):
    return jax.shard_map(
        shards,
        mesh=mesh,
        in_specs=(
            P("seq", None),
            P("seq"),
            P(),
            P(),
            P(None, "tp"),
            P(None, "tp"),
            P(None, "tp"),
            P("tp", None),
            P(),
            P(None, "tp"),
            P("tp", None),
            P(),
            P(None, "tp"),
        ),
        out_specs=P("seq", None, "tp"),
        check_vma=False,
    )
```

```python
import jax
import jax.numpy as jnp
from jax import lax
from jax.sharding import PartitionSpec as P

D = 1408
HD = 88
REACH = 4


epsilon = 1e-06
masked_score = -1e30


def shifted(value, axis, steps):
    count = lax.axis_size(axis)
    initial, last = (max(0, -steps), min(count, count - steps))
    return lax.ppermute(value, axis, [(source, source + steps) for source in range(initial, last)])


def finish_norm(hidden, row_mean, square, norm_gain):
    return (
        (hidden - row_mean) * lax.rsqrt(square - row_mean * row_mean + epsilon) * norm_gain
    ).astype(jnp.bfloat16)


def full_norm(hidden, norm_gain):
    row_mean = jnp.mean(hidden, axis=1, keepdims=True)
    square = jnp.mean(hidden * hidden, axis=1, keepdims=True)
    return finish_norm(hidden, row_mean, square, norm_gain)


def sum_rows(partial_value):
    tp_count = lax.axis_size("tp")
    rows, cols = partial_value.shape
    pieces = partial_value.astype(jnp.bfloat16).reshape(tp_count, rows // tp_count, cols)
    pieces = lax.all_to_all(pieces, "tp", split_axis=0, concat_axis=0, tiled=True)
    return jnp.sum(pieces.astype(jnp.float32), axis=0)


def gather_rows(row_block):
    tp_count = lax.axis_size("tp")
    copies = jnp.broadcast_to(row_block[None], (tp_count,) + row_block.shape)
    copies = lax.all_to_all(copies, "tp", split_axis=0, concat_axis=0, tiled=True)
    return copies.reshape(tp_count * row_block.shape[0], row_block.shape[1])


def block_scores(query_heads, key_heads, query_image, key_image):
    scores = jnp.einsum(
        "qhd,khd->hqk", query_heads, key_heads, preferred_element_type=jnp.float32
    ) * HD ** (-0.5)
    same_image = query_image[:, None] == key_image[None, :]
    return jnp.where(same_image[None], scores, masked_score)


def block_values(weights, value_heads):
    return jnp.einsum(
        "hqk,khd->hqd",
        weights.astype(jnp.bfloat16),
        value_heads,
        preferred_element_type=jnp.float32,
    )


def attend_own_block(query_heads, key_heads, value_heads, query_image, key_image):
    scores = block_scores(query_heads, key_heads, query_image, key_image)
    row_best = jnp.max(scores, axis=2, keepdims=True)
    weights = jnp.exp(scores - row_best)
    row_total = jnp.sum(weights, axis=2, keepdims=True)
    return row_best, row_total, block_values(weights, value_heads)


def attend_more(state, query_heads, key_heads, value_heads, query_image, key_image):
    row_best, row_total, weighted = state
    scores = block_scores(query_heads, key_heads, query_image, key_image)
    new_best = jnp.maximum(row_best, jnp.max(scores, axis=2, keepdims=True))
    rescale = jnp.exp(row_best - new_best)
    weights = jnp.exp(scores - new_best)
    row_total = row_total * rescale + jnp.sum(weights, axis=2, keepdims=True)
    weighted = weighted * rescale + block_values(weights, value_heads)
    return new_best, row_total, weighted


def image_of_groups(groups, starts, group_total):
    inside = (groups >= 0) & (groups < group_total)
    image = jnp.sum((starts[None, :] <= groups[:, None]).astype(jnp.int32), axis=1) - 1
    return jnp.where(inside, image, -1)


def route_to_owners(projected, starts, counts, image_slot, device, seq_count):
    group_rows, out_cols = projected.shape
    per_pair = group_rows // seq_count
    spread = projected.reshape(per_pair, seq_count, out_cols).transpose(1, 0, 2)
    spread = lax.all_to_all(spread, "seq", split_axis=0, concat_axis=0, tiled=True)
    held = spread.reshape(group_rows, out_cols)
    image_count = image_slot.shape[0]
    most_rows = REACH * group_rows
    per_owner = most_rows // seq_count
    image_ids = jnp.arange(image_count, dtype=jnp.int32)
    owners = jnp.arange(seq_count, dtype=jnp.int32)
    owned_image = jnp.sum(
        jnp.where(image_slot[None, :] == owners[:, None], image_ids[None, :], 0), axis=1
    )
    owner_start = starts[owned_image]
    owner_count = counts[owned_image]
    first_pos = jnp.mod(device - owner_start, seq_count)
    first_row = (owner_start + first_pos - device) // seq_count
    steps = jnp.arange(per_owner, dtype=jnp.int32)
    rows = first_row[:, None] + steps[None, :]
    valid = (first_pos[:, None] + seq_count * steps[None, :]) < owner_count[:, None]
    rows = jnp.clip(rows, 0, group_rows - 1)
    outgoing = jnp.take(held, rows.reshape(-1), axis=0).reshape(seq_count, per_owner, out_cols)
    outgoing = jnp.where(valid[:, :, None], outgoing, jnp.zeros((), outgoing.dtype))
    received = lax.all_to_all(outgoing, "seq", split_axis=0, concat_axis=0, tiled=True)
    own_image = jnp.sum(jnp.where(image_slot == device, image_ids, 0))
    own_start = starts[own_image]
    order = jnp.mod(own_start + jnp.arange(seq_count, dtype=jnp.int32), seq_count)
    placed = jnp.take(received, order, axis=0).transpose(1, 0, 2)
    return placed.reshape(most_rows, out_cols)


def shards(
    tokens,
    group_image,
    image_slot,
    attention_gain,
    query_weight,
    key_weight,
    value_weight,
    output_weight,
    feedforward_gain,
    up_weight,
    down_weight,
    merge_gain,
    merge_weight,
):
    device = lax.axis_index("seq")
    seq_count = lax.axis_size("seq")
    token_rows = tokens.shape[0]
    group_rows = group_image.shape[0]
    group_total = group_rows * seq_count
    image_count = image_slot.shape[0]
    image_ids = jnp.arange(image_count, dtype=jnp.int32)
    local_counts = jnp.sum(
        (group_image[:, None] == image_ids[None, :]).astype(jnp.int32), axis=0
    )
    every_count = lax.all_to_all(
        jnp.broadcast_to(local_counts[None, :], (seq_count, image_count)),
        "seq",
        split_axis=0,
        concat_axis=0,
        tiled=True,
    )
    counts = jnp.sum(every_count, axis=0)
    query_image = jnp.repeat(group_image, 4)
    residual = tokens.astype(jnp.float32)
    normed = full_norm(residual, attention_gain)
    head_count = query_weight.shape[1] // HD
    queries = jnp.dot(normed, query_weight, preferred_element_type=jnp.float32).astype(jnp.bfloat16)
    key_rows = jnp.dot(normed, key_weight, preferred_element_type=jnp.float32).astype(jnp.bfloat16)
    value_rows = jnp.dot(normed, value_weight, preferred_element_type=jnp.float32).astype(
        jnp.bfloat16
    )
    query_heads = queries.reshape(token_rows, head_count, HD)
    key_value = jnp.stack([key_rows, value_rows])
    counts, key_value = lax.optimization_barrier((counts, key_value))
    starts = jnp.cumsum(counts) - counts

    def images_of_block(source):
        groups = source * group_rows + jnp.arange(group_rows, dtype=jnp.int32)
        return jnp.repeat(image_of_groups(groups, starts, group_total), 4)

    state = attend_own_block(
        query_heads,
        key_value[0].reshape(token_rows, head_count, HD),
        key_value[1].reshape(token_rows, head_count, HD),
        query_image,
        query_image,
    )
    from_left, from_right = key_value, key_value
    for step in range(1, REACH + 1):
        from_left = shifted(from_left, "seq", 1)
        from_right = shifted(from_right, "seq", -1)
        for block, source, needed in (
            (from_left, device - step, lambda k: k[-1] == query_image[0]),
            (from_right, device + step, lambda k: k[0] == query_image[-1]),
        ):
            key_image = images_of_block(source)
            state = lax.cond(
                needed(key_image),
                lambda st, blk, kim: attend_more(
                    st,
                    query_heads,
                    blk[0].reshape(token_rows, head_count, HD),
                    blk[1].reshape(token_rows, head_count, HD),
                    query_image,
                    kim,
                ),
                lambda st, blk, kim: st,
                state,
                block,
                key_image,
            )
    row_best, row_total, weighted = state
    context = jnp.transpose(weighted / row_total, (1, 0, 2))
    context = context.astype(jnp.bfloat16).reshape(token_rows, head_count * HD)
    attention_part = jnp.dot(context, output_weight, preferred_element_type=jnp.float32)
    tp_count = lax.axis_size("tp")
    own_rows = token_rows // tp_count
    own_residual = lax.dynamic_slice_in_dim(residual, lax.axis_index("tp") * own_rows, own_rows, 0)
    after_attention = own_residual + sum_rows(attention_part)
    normed_two = gather_rows(full_norm(after_attention, feedforward_gain))
    hidden_units = jax.nn.gelu(
        jnp.dot(normed_two, up_weight, preferred_element_type=jnp.float32), approximate=False
    ).astype(jnp.bfloat16)
    after_feedforward = after_attention + sum_rows(
        jnp.dot(hidden_units, down_weight, preferred_element_type=jnp.float32)
    )
    normed_three = gather_rows(full_norm(after_feedforward, merge_gain))
    grouped = normed_three.reshape(group_rows, 4 * D)
    projected = jnp.dot(grouped, merge_weight, preferred_element_type=jnp.float32).astype(
        jnp.bfloat16
    )
    return route_to_owners(projected, starts, counts, image_slot, device, seq_count)[None]


def solution(mesh):
    return jax.shard_map(
        shards,
        mesh=mesh,
        in_specs=(
            P("seq", None),
            P("seq"),
            P(),
            P(),
            P(None, "tp"),
            P(None, "tp"),
            P(None, "tp"),
            P("tp", None),
            P(),
            P(None, "tp"),
            P("tp", None),
            P(),
            P(None, "tp"),
        ),
        out_specs=P("seq", None, "tp"),
        check_vma=False,
    )
```

```python
import jax
import jax.numpy as jnp
from jax import lax
from jax.sharding import PartitionSpec as P

D = 1408
HD = 88
REACH = 4


epsilon = 1e-06
masked_score = -1e30


def shifted(value, axis, steps):
    count = lax.axis_size(axis)
    initial, last = (max(0, -steps), min(count, count - steps))
    return lax.ppermute(value, axis, [(source, source + steps) for source in range(initial, last)])


def finish_norm(hidden, row_mean, square, norm_gain):
    return (
        (hidden - row_mean) * lax.rsqrt(square - row_mean * row_mean + epsilon) * norm_gain
    ).astype(jnp.bfloat16)


def full_norm(hidden, norm_gain):
    row_mean = jnp.mean(hidden, axis=1, keepdims=True)
    square = jnp.mean(hidden * hidden, axis=1, keepdims=True)
    return finish_norm(hidden, row_mean, square, norm_gain)


def tp_shift(value, steps):
    count = lax.axis_size("tp")
    return lax.ppermute(value, "tp", [(u, (u + steps) % count) for u in range(count)])


def sum_rows(partial_value):
    tp_count = lax.axis_size("tp")
    me = lax.axis_index("tp")
    rows, cols = partial_value.shape
    pieces = partial_value.astype(jnp.bfloat16).reshape(tp_count, rows // tp_count, cols)
    total = lax.dynamic_index_in_dim(pieces, me, 0, keepdims=False).astype(jnp.float32)
    for steps in range(1, tp_count):
        outgoing = lax.dynamic_index_in_dim(pieces, (me + steps) % tp_count, 0, keepdims=False)
        total = total + tp_shift(outgoing, steps).astype(jnp.float32)
    return total


def gather_rows(row_block):
    tp_count = lax.axis_size("tp")
    me = lax.axis_index("tp")
    arrived = [row_block] + [tp_shift(row_block, steps) for steps in range(1, tp_count)]
    order = (me - jnp.arange(tp_count, dtype=jnp.int32)) % tp_count
    placed = jnp.take(jnp.stack(arrived), order, axis=0)
    return placed.reshape(tp_count * row_block.shape[0], row_block.shape[1])


def block_scores(query_heads, key_heads, query_image, key_image):
    scores = jnp.einsum(
        "qhd,khd->hqk", query_heads, key_heads, preferred_element_type=jnp.float32
    ) * HD ** (-0.5)
    same_image = query_image[:, None] == key_image[None, :]
    return jnp.where(same_image[None], scores, masked_score)


def block_values(weights, value_heads):
    return jnp.einsum(
        "hqk,khd->hqd",
        weights.astype(jnp.bfloat16),
        value_heads,
        preferred_element_type=jnp.float32,
    )


def attend_own_block(query_heads, key_heads, value_heads, query_image, key_image):
    scores = block_scores(query_heads, key_heads, query_image, key_image)
    row_best = jnp.max(scores, axis=2, keepdims=True)
    weights = jnp.exp(scores - row_best)
    row_total = jnp.sum(weights, axis=2, keepdims=True)
    return row_best, row_total, block_values(weights, value_heads)


def attend_more(state, query_heads, key_heads, value_heads, query_image, key_image):
    row_best, row_total, weighted = state
    scores = block_scores(query_heads, key_heads, query_image, key_image)
    new_best = jnp.maximum(row_best, jnp.max(scores, axis=2, keepdims=True))
    rescale = jnp.exp(row_best - new_best)
    weights = jnp.exp(scores - new_best)
    row_total = row_total * rescale + jnp.sum(weights, axis=2, keepdims=True)
    weighted = weighted * rescale + block_values(weights, value_heads)
    return new_best, row_total, weighted


def image_of_groups(groups, starts, group_total):
    inside = (groups >= 0) & (groups < group_total)
    image = jnp.sum((starts[None, :] <= groups[:, None]).astype(jnp.int32), axis=1) - 1
    return jnp.where(inside, image, -1)


def route_to_owners(projected, starts, counts, image_slot, device, seq_count):
    group_rows, out_cols = projected.shape
    per_pair = group_rows // seq_count
    spread = projected.reshape(per_pair, seq_count, out_cols).transpose(1, 0, 2)
    spread = lax.all_to_all(spread, "seq", split_axis=0, concat_axis=0, tiled=True)
    held = spread.reshape(group_rows, out_cols)
    image_count = image_slot.shape[0]
    most_rows = REACH * group_rows
    per_owner = most_rows // seq_count
    image_ids = jnp.arange(image_count, dtype=jnp.int32)
    owners = jnp.arange(seq_count, dtype=jnp.int32)
    owned_image = jnp.sum(
        jnp.where(image_slot[None, :] == owners[:, None], image_ids[None, :], 0), axis=1
    )
    owner_start = starts[owned_image]
    owner_count = counts[owned_image]
    first_pos = jnp.mod(device - owner_start, seq_count)
    first_row = (owner_start + first_pos - device) // seq_count
    steps = jnp.arange(per_owner, dtype=jnp.int32)
    rows = first_row[:, None] + steps[None, :]
    valid = (first_pos[:, None] + seq_count * steps[None, :]) < owner_count[:, None]
    rows = jnp.clip(rows, 0, group_rows - 1)
    outgoing = jnp.take(held, rows.reshape(-1), axis=0).reshape(seq_count, per_owner, out_cols)
    outgoing = jnp.where(valid[:, :, None], outgoing, jnp.zeros((), outgoing.dtype))
    received = lax.all_to_all(outgoing, "seq", split_axis=0, concat_axis=0, tiled=True)
    own_image = jnp.sum(jnp.where(image_slot == device, image_ids, 0))
    own_start = starts[own_image]
    order = jnp.mod(own_start + jnp.arange(seq_count, dtype=jnp.int32), seq_count)
    placed = jnp.take(received, order, axis=0).transpose(1, 0, 2)
    return placed.reshape(most_rows, out_cols)


def shards(
    tokens,
    group_image,
    image_slot,
    attention_gain,
    query_weight,
    key_weight,
    value_weight,
    output_weight,
    feedforward_gain,
    up_weight,
    down_weight,
    merge_gain,
    merge_weight,
):
    device = lax.axis_index("seq")
    seq_count = lax.axis_size("seq")
    token_rows = tokens.shape[0]
    group_rows = group_image.shape[0]
    group_total = group_rows * seq_count
    image_count = image_slot.shape[0]
    image_ids = jnp.arange(image_count, dtype=jnp.int32)
    local_counts = jnp.sum(
        (group_image[:, None] == image_ids[None, :]).astype(jnp.int32), axis=0
    )
    every_count = lax.all_to_all(
        jnp.broadcast_to(local_counts[None, :], (seq_count, image_count)),
        "seq",
        split_axis=0,
        concat_axis=0,
        tiled=True,
    )
    counts = jnp.sum(every_count, axis=0)
    query_image = jnp.repeat(group_image, 4)
    residual = tokens.astype(jnp.float32)
    normed = full_norm(residual, attention_gain)
    head_count = query_weight.shape[1] // HD
    queries = jnp.dot(normed, query_weight, preferred_element_type=jnp.float32).astype(jnp.bfloat16)
    key_rows = jnp.dot(normed, key_weight, preferred_element_type=jnp.float32).astype(jnp.bfloat16)
    value_rows = jnp.dot(normed, value_weight, preferred_element_type=jnp.float32).astype(
        jnp.bfloat16
    )
    query_heads = queries.reshape(token_rows, head_count, HD)
    key_value = jnp.stack([key_rows, value_rows])
    counts, key_value = lax.optimization_barrier((counts, key_value))
    starts = jnp.cumsum(counts) - counts

    def images_of_block(source):
        groups = source * group_rows + jnp.arange(group_rows, dtype=jnp.int32)
        return jnp.repeat(image_of_groups(groups, starts, group_total), 4)

    state = attend_own_block(
        query_heads,
        key_value[0].reshape(token_rows, head_count, HD),
        key_value[1].reshape(token_rows, head_count, HD),
        query_image,
        query_image,
    )
    from_left, from_right = key_value, key_value
    for step in range(1, REACH + 1):
        from_left = shifted(from_left, "seq", 1)
        from_right = shifted(from_right, "seq", -1)
        for block, source, needed in (
            (from_left, device - step, lambda k: k[-1] == query_image[0]),
            (from_right, device + step, lambda k: k[0] == query_image[-1]),
        ):
            key_image = images_of_block(source)
            state = lax.cond(
                needed(key_image),
                lambda st, blk, kim: attend_more(
                    st,
                    query_heads,
                    blk[0].reshape(token_rows, head_count, HD),
                    blk[1].reshape(token_rows, head_count, HD),
                    query_image,
                    kim,
                ),
                lambda st, blk, kim: st,
                state,
                block,
                key_image,
            )
    row_best, row_total, weighted = state
    context = jnp.transpose(weighted / row_total, (1, 0, 2))
    context = context.astype(jnp.bfloat16).reshape(token_rows, head_count * HD)
    attention_part = jnp.dot(context, output_weight, preferred_element_type=jnp.float32)
    tp_count = lax.axis_size("tp")
    own_rows = token_rows // tp_count
    own_residual = lax.dynamic_slice_in_dim(residual, lax.axis_index("tp") * own_rows, own_rows, 0)
    after_attention = own_residual + sum_rows(attention_part)
    normed_two = gather_rows(full_norm(after_attention, feedforward_gain))
    hidden_units = jax.nn.gelu(
        jnp.dot(normed_two, up_weight, preferred_element_type=jnp.float32), approximate=False
    ).astype(jnp.bfloat16)
    after_feedforward = after_attention + sum_rows(
        jnp.dot(hidden_units, down_weight, preferred_element_type=jnp.float32)
    )
    normed_three = gather_rows(full_norm(after_feedforward, merge_gain))
    grouped = normed_three.reshape(group_rows, 4 * D)
    projected = jnp.dot(grouped, merge_weight, preferred_element_type=jnp.float32).astype(
        jnp.bfloat16
    )
    return route_to_owners(projected, starts, counts, image_slot, device, seq_count)[None]


def solution(mesh):
    return jax.shard_map(
        shards,
        mesh=mesh,
        in_specs=(
            P("seq", None),
            P("seq"),
            P(),
            P(),
            P(None, "tp"),
            P(None, "tp"),
            P(None, "tp"),
            P("tp", None),
            P(),
            P(None, "tp"),
            P("tp", None),
            P(),
            P(None, "tp"),
        ),
        out_specs=P("seq", None, "tp"),
        check_vma=False,
    )
```

```python
import jax
import jax.numpy as jnp
from jax import lax
from jax.sharding import PartitionSpec as P

D = 1408
HD = 88
REACH = 4


epsilon = 1e-06
masked_score = -1e30


def shifted(value, axis, steps):
    count = lax.axis_size(axis)
    initial, last = (max(0, -steps), min(count, count - steps))
    return lax.ppermute(value, axis, [(source, source + steps) for source in range(initial, last)])


def finish_norm(hidden, row_mean, square, norm_gain):
    return (
        (hidden - row_mean) * lax.rsqrt(square - row_mean * row_mean + epsilon) * norm_gain
    ).astype(jnp.bfloat16)


def full_norm(hidden, norm_gain):
    row_mean = jnp.mean(hidden, axis=1, keepdims=True)
    square = jnp.mean(hidden * hidden, axis=1, keepdims=True)
    return finish_norm(hidden, row_mean, square, norm_gain)


def tp_shift(value, steps):
    count = lax.axis_size("tp")
    return lax.ppermute(value, "tp", [(u, (u + steps) % count) for u in range(count)])


def sum_rows(partial_value):
    tp_count = lax.axis_size("tp")
    me = lax.axis_index("tp")
    rows, cols = partial_value.shape
    pieces = partial_value.astype(jnp.bfloat16).reshape(tp_count, rows // tp_count, cols)
    total = lax.dynamic_index_in_dim(pieces, me, 0, keepdims=False).astype(jnp.float32)
    for steps in range(1, tp_count):
        outgoing = lax.dynamic_index_in_dim(pieces, (me + steps) % tp_count, 0, keepdims=False)
        total = total + tp_shift(outgoing, steps).astype(jnp.float32)
    return total


def gather_rows(row_block):
    tp_count = lax.axis_size("tp")
    me = lax.axis_index("tp")
    arrived = [row_block] + [tp_shift(row_block, steps) for steps in range(1, tp_count)]
    order = (me - jnp.arange(tp_count, dtype=jnp.int32)) % tp_count
    placed = jnp.take(jnp.stack(arrived), order, axis=0)
    return placed.reshape(tp_count * row_block.shape[0], row_block.shape[1])


def block_scores(query_heads, key_heads, query_image, key_image):
    scores = jnp.einsum(
        "qhd,khd->hqk", query_heads, key_heads, preferred_element_type=jnp.float32
    ) * HD ** (-0.5)
    same_image = query_image[:, None] == key_image[None, :]
    return jnp.where(same_image[None], scores, masked_score)


def block_values(weights, value_heads):
    return jnp.einsum(
        "hqk,khd->hqd",
        weights.astype(jnp.bfloat16),
        value_heads,
        preferred_element_type=jnp.float32,
    )


def attend_own_block(query_heads, key_heads, value_heads, query_image, key_image):
    scores = block_scores(query_heads, key_heads, query_image, key_image)
    row_best = jnp.max(scores, axis=2, keepdims=True)
    weights = jnp.exp(scores - row_best)
    row_total = jnp.sum(weights, axis=2, keepdims=True)
    return row_best, row_total, block_values(weights, value_heads)


def attend_more(state, query_heads, key_heads, value_heads, query_image, key_image):
    row_best, row_total, weighted = state
    scores = block_scores(query_heads, key_heads, query_image, key_image)
    new_best = jnp.maximum(row_best, jnp.max(scores, axis=2, keepdims=True))
    rescale = jnp.exp(row_best - new_best)
    weights = jnp.exp(scores - new_best)
    row_total = row_total * rescale + jnp.sum(weights, axis=2, keepdims=True)
    weighted = weighted * rescale + block_values(weights, value_heads)
    return new_best, row_total, weighted


def image_of_groups(groups, starts, group_total):
    inside = (groups >= 0) & (groups < group_total)
    image = jnp.sum((starts[None, :] <= groups[:, None]).astype(jnp.int32), axis=1) - 1
    return jnp.where(inside, image, -1)


def route_to_owners(held, starts, counts, image_slot, device, seq_count):
    group_rows, out_cols = held.shape
    image_count = image_slot.shape[0]
    most_rows = REACH * group_rows
    per_owner = most_rows // seq_count
    image_ids = jnp.arange(image_count, dtype=jnp.int32)
    owners = jnp.arange(seq_count, dtype=jnp.int32)
    owned_image = jnp.sum(
        jnp.where(image_slot[None, :] == owners[:, None], image_ids[None, :], 0), axis=1
    )
    owner_start = starts[owned_image]
    owner_count = counts[owned_image]
    first_pos = jnp.mod(device - owner_start, seq_count)
    first_row = (owner_start + first_pos - device) // seq_count
    steps = jnp.arange(per_owner, dtype=jnp.int32)
    rows = first_row[:, None] + steps[None, :]
    valid = (first_pos[:, None] + seq_count * steps[None, :]) < owner_count[:, None]
    rows = jnp.clip(rows, 0, group_rows - 1)
    outgoing = jnp.take(held, rows.reshape(-1), axis=0).reshape(seq_count, per_owner, out_cols)
    outgoing = jnp.where(valid[:, :, None], outgoing, jnp.zeros((), outgoing.dtype))
    received = lax.all_to_all(outgoing, "seq", split_axis=0, concat_axis=0, tiled=True)
    own_image = jnp.sum(jnp.where(image_slot == device, image_ids, 0))
    own_start = starts[own_image]
    order = jnp.mod(own_start + jnp.arange(seq_count, dtype=jnp.int32), seq_count)
    placed = jnp.take(received, order, axis=0).transpose(1, 0, 2)
    return placed.reshape(most_rows, out_cols)


def shards(
    tokens,
    group_image,
    image_slot,
    attention_gain,
    query_weight,
    key_weight,
    value_weight,
    output_weight,
    feedforward_gain,
    up_weight,
    down_weight,
    merge_gain,
    merge_weight,
):
    device = lax.axis_index("seq")
    seq_count = lax.axis_size("seq")
    token_rows = tokens.shape[0]
    group_rows = group_image.shape[0]
    group_total = group_rows * seq_count
    image_count = image_slot.shape[0]
    image_ids = jnp.arange(image_count, dtype=jnp.int32)
    local_counts = jnp.sum(
        (group_image[:, None] == image_ids[None, :]).astype(jnp.int32), axis=0
    )
    every_count = lax.all_to_all(
        jnp.broadcast_to(local_counts[None, :], (seq_count, image_count)),
        "seq",
        split_axis=0,
        concat_axis=0,
        tiled=True,
    )
    counts = jnp.sum(every_count, axis=0)
    query_image = jnp.repeat(group_image, 4)
    residual = tokens.astype(jnp.float32)
    normed = full_norm(residual, attention_gain)
    head_count = query_weight.shape[1] // HD
    queries = jnp.dot(normed, query_weight, preferred_element_type=jnp.float32).astype(jnp.bfloat16)
    key_rows = jnp.dot(normed, key_weight, preferred_element_type=jnp.float32).astype(jnp.bfloat16)
    value_rows = jnp.dot(normed, value_weight, preferred_element_type=jnp.float32).astype(
        jnp.bfloat16
    )
    query_heads = queries.reshape(token_rows, head_count, HD)
    key_value = jnp.stack([key_rows, value_rows])
    counts, key_value = lax.optimization_barrier((counts, key_value))
    starts = jnp.cumsum(counts) - counts

    def images_of_block(source):
        groups = source * group_rows + jnp.arange(group_rows, dtype=jnp.int32)
        return jnp.repeat(image_of_groups(groups, starts, group_total), 4)

    state = attend_own_block(
        query_heads,
        key_value[0].reshape(token_rows, head_count, HD),
        key_value[1].reshape(token_rows, head_count, HD),
        query_image,
        query_image,
    )
    from_left, from_right = key_value, key_value
    for step in range(1, REACH + 1):
        from_left = shifted(from_left, "seq", 1)
        from_right = shifted(from_right, "seq", -1)
        for block, source, needed in (
            (from_left, device - step, lambda k: k[-1] == query_image[0]),
            (from_right, device + step, lambda k: k[0] == query_image[-1]),
        ):
            key_image = images_of_block(source)
            state = lax.cond(
                needed(key_image),
                lambda st, blk, kim: attend_more(
                    st,
                    query_heads,
                    blk[0].reshape(token_rows, head_count, HD),
                    blk[1].reshape(token_rows, head_count, HD),
                    query_image,
                    kim,
                ),
                lambda st, blk, kim: st,
                state,
                block,
                key_image,
            )
    row_best, row_total, weighted = state
    context = jnp.transpose(weighted / row_total, (1, 0, 2))
    context = context.astype(jnp.bfloat16).reshape(token_rows, head_count * HD)
    attention_part = jnp.dot(context, output_weight, preferred_element_type=jnp.float32)
    tp_count = lax.axis_size("tp")
    own_rows = token_rows // tp_count
    own_residual = lax.dynamic_slice_in_dim(residual, lax.axis_index("tp") * own_rows, own_rows, 0)
    after_attention = own_residual + sum_rows(attention_part)
    normed_two = gather_rows(full_norm(after_attention, feedforward_gain))
    hidden_units = jax.nn.gelu(
        jnp.dot(normed_two, up_weight, preferred_element_type=jnp.float32), approximate=False
    ).astype(jnp.bfloat16)
    after_feedforward = after_attention + sum_rows(
        jnp.dot(hidden_units, down_weight, preferred_element_type=jnp.float32)
    )
    normed_three = full_norm(after_feedforward, merge_gain)
    own_groups = normed_three.reshape(own_rows // 4, 4 * D)
    copies = jnp.repeat(own_groups, tp_count, axis=0)
    held_groups = lax.all_to_all(copies, ("seq", "tp"), split_axis=0, concat_axis=0, tiled=True)
    projected = jnp.dot(held_groups, merge_weight, preferred_element_type=jnp.float32).astype(
        jnp.bfloat16
    )
    return route_to_owners(projected, starts, counts, image_slot, device, seq_count)[None]


def solution(mesh):
    return jax.shard_map(
        shards,
        mesh=mesh,
        in_specs=(
            P("seq", None),
            P("seq"),
            P(),
            P(),
            P(None, "tp"),
            P(None, "tp"),
            P(None, "tp"),
            P("tp", None),
            P(),
            P(None, "tp"),
            P("tp", None),
            P(),
            P(None, "tp"),
        ),
        out_specs=P("seq", None, "tp"),
        check_vma=False,
    )
```

```python
import jax
import jax.numpy as jnp
from jax import lax
from jax.sharding import PartitionSpec as P

D = 1408
HD = 88
REACH = 4


epsilon = 1e-06
masked_score = -1e30


def shifted(value, axis, steps):
    count = lax.axis_size(axis)
    initial, last = (max(0, -steps), min(count, count - steps))
    return lax.ppermute(value, axis, [(source, source + steps) for source in range(initial, last)])


def finish_norm(hidden, row_mean, square, norm_gain):
    return (
        (hidden - row_mean) * lax.rsqrt(square - row_mean * row_mean + epsilon) * norm_gain
    ).astype(jnp.bfloat16)


def full_norm(hidden, norm_gain):
    row_mean = jnp.mean(hidden, axis=1, keepdims=True)
    square = jnp.mean(hidden * hidden, axis=1, keepdims=True)
    return finish_norm(hidden, row_mean, square, norm_gain)


def tp_shift(value, steps):
    count = lax.axis_size("tp")
    return lax.ppermute(value, "tp", [(u, (u + steps) % count) for u in range(count)])


def sum_rows(partial_value):
    tp_count = lax.axis_size("tp")
    me = lax.axis_index("tp")
    rows, cols = partial_value.shape
    pieces = partial_value.astype(jnp.bfloat16).reshape(tp_count, rows // tp_count, cols)
    total = lax.dynamic_index_in_dim(pieces, me, 0, keepdims=False).astype(jnp.float32)
    for steps in range(1, tp_count):
        outgoing = lax.dynamic_index_in_dim(pieces, (me + steps) % tp_count, 0, keepdims=False)
        total = total + tp_shift(outgoing, steps).astype(jnp.float32)
    return total


def gather_rows(row_block):
    tp_count = lax.axis_size("tp")
    me = lax.axis_index("tp")
    arrived = [row_block] + [tp_shift(row_block, steps) for steps in range(1, tp_count)]
    order = (me - jnp.arange(tp_count, dtype=jnp.int32)) % tp_count
    placed = jnp.take(jnp.stack(arrived), order, axis=0)
    return placed.reshape(tp_count * row_block.shape[0], row_block.shape[1])


def block_scores(query_heads, key_heads, query_image, key_image):
    scores = jnp.einsum(
        "qhd,khd->hqk", query_heads, key_heads, preferred_element_type=jnp.float32
    ) * HD ** (-0.5)
    same_image = query_image[:, None] == key_image[None, :]
    return jnp.where(same_image[None], scores, masked_score)


def block_values(weights, value_heads):
    return jnp.einsum(
        "hqk,khd->hqd",
        weights.astype(jnp.bfloat16),
        value_heads,
        preferred_element_type=jnp.float32,
    )


def attend_own_block(query_heads, key_heads, value_heads, query_image, key_image):
    scores = block_scores(query_heads, key_heads, query_image, key_image)
    row_best = jnp.max(scores, axis=2, keepdims=True)
    weights = jnp.exp(scores - row_best)
    row_total = jnp.sum(weights, axis=2, keepdims=True)
    return row_best, row_total, block_values(weights, value_heads)


def attend_more(state, query_heads, key_heads, value_heads, query_image, key_image):
    row_best, row_total, weighted = state
    scores = block_scores(query_heads, key_heads, query_image, key_image)
    new_best = jnp.maximum(row_best, jnp.max(scores, axis=2, keepdims=True))
    rescale = jnp.exp(row_best - new_best)
    weights = jnp.exp(scores - new_best)
    row_total = row_total * rescale + jnp.sum(weights, axis=2, keepdims=True)
    weighted = weighted * rescale + block_values(weights, value_heads)
    return new_best, row_total, weighted


def image_of_groups(groups, starts, group_total):
    inside = (groups >= 0) & (groups < group_total)
    image = jnp.sum((starts[None, :] <= groups[:, None]).astype(jnp.int32), axis=1) - 1
    return jnp.where(inside, image, -1)


def route_to_owners(projected, starts, counts, image_slot, device, seq_count):
    group_rows, out_cols = projected.shape
    per_pair = group_rows // seq_count
    spread = projected.reshape(per_pair, seq_count, out_cols).transpose(1, 0, 2)
    spread = lax.all_to_all(spread, "seq", split_axis=0, concat_axis=0, tiled=True)
    held = spread.reshape(group_rows, out_cols)
    image_count = image_slot.shape[0]
    most_rows = REACH * group_rows
    per_owner = most_rows // seq_count
    image_ids = jnp.arange(image_count, dtype=jnp.int32)
    owners = jnp.arange(seq_count, dtype=jnp.int32)
    owned_image = jnp.sum(
        jnp.where(image_slot[None, :] == owners[:, None], image_ids[None, :], 0), axis=1
    )
    owner_start = starts[owned_image]
    owner_count = counts[owned_image]
    first_pos = jnp.mod(device - owner_start, seq_count)
    first_row = (owner_start + first_pos - device) // seq_count
    steps = jnp.arange(per_owner, dtype=jnp.int32)
    rows = first_row[:, None] + steps[None, :]
    valid = (first_pos[:, None] + seq_count * steps[None, :]) < owner_count[:, None]
    rows = jnp.clip(rows, 0, group_rows - 1)
    outgoing = jnp.take(held, rows.reshape(-1), axis=0).reshape(seq_count, per_owner, out_cols)
    outgoing = jnp.where(valid[:, :, None], outgoing, jnp.zeros((), outgoing.dtype))
    received = lax.all_to_all(outgoing, "seq", split_axis=0, concat_axis=0, tiled=True)
    own_image = jnp.sum(jnp.where(image_slot == device, image_ids, 0))
    own_start = starts[own_image]
    order = jnp.mod(own_start + jnp.arange(seq_count, dtype=jnp.int32), seq_count)
    placed = jnp.take(received, order, axis=0).transpose(1, 0, 2)
    return placed.reshape(most_rows, out_cols)


def shards(
    tokens,
    group_image,
    image_slot,
    attention_gain,
    query_weight,
    key_weight,
    value_weight,
    output_weight,
    feedforward_gain,
    up_weight,
    down_weight,
    merge_gain,
    merge_weight,
):
    device = lax.axis_index("seq")
    seq_count = lax.axis_size("seq")
    token_rows = tokens.shape[0]
    group_rows = group_image.shape[0]
    group_total = group_rows * seq_count
    image_count = image_slot.shape[0]
    image_ids = jnp.arange(image_count, dtype=jnp.int32)
    local_counts = jnp.sum(
        (group_image[:, None] == image_ids[None, :]).astype(jnp.int32), axis=0
    )
    every_count = lax.all_to_all(
        jnp.broadcast_to(local_counts[None, :], (seq_count, image_count)),
        "seq",
        split_axis=0,
        concat_axis=0,
        tiled=True,
    )
    counts = jnp.sum(every_count, axis=0)
    query_image = jnp.repeat(group_image, 4)
    residual = tokens.astype(jnp.float32)
    normed = full_norm(residual, attention_gain)
    head_count = query_weight.shape[1] // HD
    queries = jnp.dot(normed, query_weight, preferred_element_type=jnp.float32).astype(jnp.bfloat16)
    key_rows = jnp.dot(normed, key_weight, preferred_element_type=jnp.float32).astype(jnp.bfloat16)
    value_rows = jnp.dot(normed, value_weight, preferred_element_type=jnp.float32).astype(
        jnp.bfloat16
    )
    query_heads = queries.reshape(token_rows, head_count, HD)
    key_value = jnp.stack([key_rows, value_rows])
    counts, key_value = lax.optimization_barrier((counts, key_value))
    starts = jnp.cumsum(counts) - counts

    def images_of_block(source):
        groups = source * group_rows + jnp.arange(group_rows, dtype=jnp.int32)
        return jnp.repeat(image_of_groups(groups, starts, group_total), 4)

    state = attend_own_block(
        query_heads,
        key_value[0].reshape(token_rows, head_count, HD),
        key_value[1].reshape(token_rows, head_count, HD),
        query_image,
        query_image,
    )
    near = {step: shifted(key_value, "seq", step) for step in (1, -1, 2, -2)}
    far = {
        3: shifted(near[2], "seq", 1),
        -3: shifted(near[-2], "seq", -1),
        4: shifted(near[2], "seq", 2),
        -4: shifted(near[-2], "seq", -2),
    }
    arrived = {**near, **far}
    for step in (1, -1, 2, -2, 3, -3, 4, -4):
        block = arrived[step]
        source = device - step
        if step > 0:
            needed = lambda k: k[-1] == query_image[0]
        else:
            needed = lambda k: k[0] == query_image[-1]
        key_image = images_of_block(source)
        state = lax.cond(
            needed(key_image),
            lambda st, blk, kim: attend_more(
                st,
                query_heads,
                blk[0].reshape(token_rows, head_count, HD),
                blk[1].reshape(token_rows, head_count, HD),
                query_image,
                kim,
            ),
            lambda st, blk, kim: st,
            state,
            block,
            key_image,
        )
    row_best, row_total, weighted = state
    context = jnp.transpose(weighted / row_total, (1, 0, 2))
    context = context.astype(jnp.bfloat16).reshape(token_rows, head_count * HD)
    attention_part = jnp.dot(context, output_weight, preferred_element_type=jnp.float32)
    tp_count = lax.axis_size("tp")
    own_rows = token_rows // tp_count
    own_residual = lax.dynamic_slice_in_dim(residual, lax.axis_index("tp") * own_rows, own_rows, 0)
    after_attention = own_residual + sum_rows(attention_part)
    normed_two = gather_rows(full_norm(after_attention, feedforward_gain))
    hidden_units = jax.nn.gelu(
        jnp.dot(normed_two, up_weight, preferred_element_type=jnp.float32), approximate=False
    ).astype(jnp.bfloat16)
    after_feedforward = after_attention + sum_rows(
        jnp.dot(hidden_units, down_weight, preferred_element_type=jnp.float32)
    )
    normed_three = gather_rows(full_norm(after_feedforward, merge_gain))
    grouped = normed_three.reshape(group_rows, 4 * D)
    projected = jnp.dot(grouped, merge_weight, preferred_element_type=jnp.float32).astype(
        jnp.bfloat16
    )
    return route_to_owners(projected, starts, counts, image_slot, device, seq_count)[None]


def solution(mesh):
    return jax.shard_map(
        shards,
        mesh=mesh,
        in_specs=(
            P("seq", None),
            P("seq"),
            P(),
            P(),
            P(None, "tp"),
            P(None, "tp"),
            P(None, "tp"),
            P("tp", None),
            P(),
            P(None, "tp"),
            P("tp", None),
            P(),
            P(None, "tp"),
        ),
        out_specs=P("seq", None, "tp"),
        check_vma=False,
    )
```

```python
import jax
import jax.numpy as jnp
from jax import lax
from jax.sharding import PartitionSpec as P

D = 1408
HD = 88
REACH = 4


epsilon = 1e-06
masked_score = -1e30


def shifted(value, axis, steps):
    count = lax.axis_size(axis)
    initial, last = (max(0, -steps), min(count, count - steps))
    return lax.ppermute(value, axis, [(source, source + steps) for source in range(initial, last)])


def finish_norm(hidden, row_mean, square, norm_gain):
    return (
        (hidden - row_mean) * lax.rsqrt(square - row_mean * row_mean + epsilon) * norm_gain
    ).astype(jnp.bfloat16)


def full_norm(hidden, norm_gain):
    row_mean = jnp.mean(hidden, axis=1, keepdims=True)
    square = jnp.mean(hidden * hidden, axis=1, keepdims=True)
    return finish_norm(hidden, row_mean, square, norm_gain)


def tp_shift(value, steps):
    count = lax.axis_size("tp")
    return lax.ppermute(value, "tp", [(u, (u + steps) % count) for u in range(count)])


def sum_rows(partial_value):
    tp_count = lax.axis_size("tp")
    me = lax.axis_index("tp")
    rows, cols = partial_value.shape
    pieces = partial_value.astype(jnp.bfloat16).reshape(tp_count, rows // tp_count, cols)
    total = lax.dynamic_index_in_dim(pieces, me, 0, keepdims=False).astype(jnp.float32)
    for steps in range(1, tp_count):
        outgoing = lax.dynamic_index_in_dim(pieces, (me + steps) % tp_count, 0, keepdims=False)
        total = total + tp_shift(outgoing, steps).astype(jnp.float32)
    return total


def gather_rows(row_block):
    tp_count = lax.axis_size("tp")
    me = lax.axis_index("tp")
    arrived = [row_block] + [tp_shift(row_block, steps) for steps in range(1, tp_count)]
    order = (me - jnp.arange(tp_count, dtype=jnp.int32)) % tp_count
    placed = jnp.take(jnp.stack(arrived), order, axis=0)
    return placed.reshape(tp_count * row_block.shape[0], row_block.shape[1])


def block_scores(query_heads, key_heads, query_image, key_image):
    scores = jnp.einsum(
        "qhd,khd->hqk", query_heads, key_heads, preferred_element_type=jnp.float32
    ) * HD ** (-0.5)
    same_image = query_image[:, None] == key_image[None, :]
    return jnp.where(same_image[None], scores, masked_score)


def block_values(weights, value_heads):
    return jnp.einsum(
        "hqk,khd->hqd",
        weights.astype(jnp.bfloat16),
        value_heads,
        preferred_element_type=jnp.float32,
    )


def attend_own_block(query_heads, key_heads, value_heads, query_image, key_image):
    scores = block_scores(query_heads, key_heads, query_image, key_image)
    row_best = jnp.max(scores, axis=2, keepdims=True)
    weights = jnp.exp(scores - row_best)
    row_total = jnp.sum(weights, axis=2, keepdims=True)
    return row_best, row_total, block_values(weights, value_heads)


def attend_more(state, query_heads, key_heads, value_heads, query_image, key_image):
    row_best, row_total, weighted = state
    scores = block_scores(query_heads, key_heads, query_image, key_image)
    new_best = jnp.maximum(row_best, jnp.max(scores, axis=2, keepdims=True))
    rescale = jnp.exp(row_best - new_best)
    weights = jnp.exp(scores - new_best)
    row_total = row_total * rescale + jnp.sum(weights, axis=2, keepdims=True)
    weighted = weighted * rescale + block_values(weights, value_heads)
    return new_best, row_total, weighted


def image_of_groups(groups, starts, group_total):
    inside = (groups >= 0) & (groups < group_total)
    image = jnp.sum((starts[None, :] <= groups[:, None]).astype(jnp.int32), axis=1) - 1
    return jnp.where(inside, image, -1)


def route_to_owners(projected, starts, counts, image_slot, device, seq_count):
    group_rows, out_cols = projected.shape
    per_pair = group_rows // seq_count
    spread = projected.reshape(per_pair, seq_count, out_cols).transpose(1, 0, 2)
    spread = lax.all_to_all(spread, "seq", split_axis=0, concat_axis=0, tiled=True)
    held = spread.reshape(group_rows, out_cols)
    image_count = image_slot.shape[0]
    most_rows = REACH * group_rows
    per_owner = most_rows // seq_count
    image_ids = jnp.arange(image_count, dtype=jnp.int32)
    owners = jnp.arange(seq_count, dtype=jnp.int32)
    owned_image = jnp.sum(
        jnp.where(image_slot[None, :] == owners[:, None], image_ids[None, :], 0), axis=1
    )
    owner_start = starts[owned_image]
    owner_count = counts[owned_image]
    first_pos = jnp.mod(device - owner_start, seq_count)
    first_row = (owner_start + first_pos - device) // seq_count
    steps = jnp.arange(per_owner, dtype=jnp.int32)
    rows = first_row[:, None] + steps[None, :]
    valid = (first_pos[:, None] + seq_count * steps[None, :]) < owner_count[:, None]
    rows = jnp.clip(rows, 0, group_rows - 1)
    outgoing = jnp.take(held, rows.reshape(-1), axis=0).reshape(seq_count, per_owner, out_cols)
    outgoing = jnp.where(valid[:, :, None], outgoing, jnp.zeros((), outgoing.dtype))
    received = lax.all_to_all(outgoing, "seq", split_axis=0, concat_axis=0, tiled=True)
    own_image = jnp.sum(jnp.where(image_slot == device, image_ids, 0))
    own_start = starts[own_image]
    order = jnp.mod(own_start + jnp.arange(seq_count, dtype=jnp.int32), seq_count)
    placed = jnp.take(received, order, axis=0).transpose(1, 0, 2)
    return placed.reshape(most_rows, out_cols)


def shards(
    tokens,
    group_image,
    image_slot,
    attention_gain,
    query_weight,
    key_weight,
    value_weight,
    output_weight,
    feedforward_gain,
    up_weight,
    down_weight,
    merge_gain,
    merge_weight,
):
    device = lax.axis_index("seq")
    seq_count = lax.axis_size("seq")
    token_rows = tokens.shape[0]
    group_rows = group_image.shape[0]
    group_total = group_rows * seq_count
    image_count = image_slot.shape[0]
    image_ids = jnp.arange(image_count, dtype=jnp.int32)
    local_counts = jnp.sum(
        (group_image[:, None] == image_ids[None, :]).astype(jnp.int32), axis=0
    )
    every_count = lax.all_to_all(
        jnp.broadcast_to(local_counts[None, :], (seq_count, image_count)),
        "seq",
        split_axis=0,
        concat_axis=0,
        tiled=True,
    )
    counts = jnp.sum(every_count, axis=0)
    query_image = jnp.repeat(group_image, 4)
    residual = tokens.astype(jnp.float32)
    normed = full_norm(residual, attention_gain)
    head_count = query_weight.shape[1] // HD
    queries = jnp.dot(normed, query_weight, preferred_element_type=jnp.float32).astype(jnp.bfloat16)
    key_rows = jnp.dot(normed, key_weight, preferred_element_type=jnp.float32).astype(jnp.bfloat16)
    value_rows = jnp.dot(normed, value_weight, preferred_element_type=jnp.float32).astype(
        jnp.bfloat16
    )
    query_heads = queries.reshape(token_rows, head_count, HD)
    key_value = jnp.stack([key_rows, value_rows])
    counts, key_value = lax.optimization_barrier((counts, key_value))
    starts = jnp.cumsum(counts) - counts

    def images_of_block(source):
        groups = source * group_rows + jnp.arange(group_rows, dtype=jnp.int32)
        return jnp.repeat(image_of_groups(groups, starts, group_total), 4)

    state = attend_own_block(
        query_heads,
        key_value[0].reshape(token_rows, head_count, HD),
        key_value[1].reshape(token_rows, head_count, HD),
        query_image,
        query_image,
    )
    near = {step: shifted(key_value, "seq", step) for step in (1, -1, 2, -2)}
    tie = (state[1][0, 0, 0] < 0.0).astype(jnp.bfloat16)
    second_left, second_right = near[2] + tie, near[-2] + tie
    far = {
        3: shifted(second_left, "seq", 1),
        -3: shifted(second_right, "seq", -1),
        4: shifted(second_left, "seq", 2),
        -4: shifted(second_right, "seq", -2),
    }
    arrived = {**near, **far}
    for step in (1, -1, 2, -2, 3, -3, 4, -4):
        block = arrived[step]
        source = device - step
        if step > 0:
            needed = lambda k: k[-1] == query_image[0]
        else:
            needed = lambda k: k[0] == query_image[-1]
        key_image = images_of_block(source)
        state = lax.cond(
            needed(key_image),
            lambda st, blk, kim: attend_more(
                st,
                query_heads,
                blk[0].reshape(token_rows, head_count, HD),
                blk[1].reshape(token_rows, head_count, HD),
                query_image,
                kim,
            ),
            lambda st, blk, kim: st,
            state,
            block,
            key_image,
        )
    row_best, row_total, weighted = state
    context = jnp.transpose(weighted / row_total, (1, 0, 2))
    context = context.astype(jnp.bfloat16).reshape(token_rows, head_count * HD)
    attention_part = jnp.dot(context, output_weight, preferred_element_type=jnp.float32)
    tp_count = lax.axis_size("tp")
    own_rows = token_rows // tp_count
    own_residual = lax.dynamic_slice_in_dim(residual, lax.axis_index("tp") * own_rows, own_rows, 0)
    after_attention = own_residual + sum_rows(attention_part)
    normed_two = gather_rows(full_norm(after_attention, feedforward_gain))
    hidden_units = jax.nn.gelu(
        jnp.dot(normed_two, up_weight, preferred_element_type=jnp.float32), approximate=False
    ).astype(jnp.bfloat16)
    after_feedforward = after_attention + sum_rows(
        jnp.dot(hidden_units, down_weight, preferred_element_type=jnp.float32)
    )
    normed_three = gather_rows(full_norm(after_feedforward, merge_gain))
    grouped = normed_three.reshape(group_rows, 4 * D)
    projected = jnp.dot(grouped, merge_weight, preferred_element_type=jnp.float32).astype(
        jnp.bfloat16
    )
    return route_to_owners(projected, starts, counts, image_slot, device, seq_count)[None]


def solution(mesh):
    return jax.shard_map(
        shards,
        mesh=mesh,
        in_specs=(
            P("seq", None),
            P("seq"),
            P(),
            P(),
            P(None, "tp"),
            P(None, "tp"),
            P(None, "tp"),
            P("tp", None),
            P(),
            P(None, "tp"),
            P("tp", None),
            P(),
            P(None, "tp"),
        ),
        out_specs=P("seq", None, "tp"),
        check_vma=False,
    )
```

```python
import jax
import jax.numpy as jnp
from jax import lax
from jax.sharding import PartitionSpec as P

D = 1408
HD = 88
REACH = 4


epsilon = 1e-06
masked_score = -1e30


def shifted(value, axis, steps):
    count = lax.axis_size(axis)
    initial, last = (max(0, -steps), min(count, count - steps))
    return lax.ppermute(value, axis, [(source, source + steps) for source in range(initial, last)])


def finish_norm(hidden, row_mean, square, norm_gain):
    return (
        (hidden - row_mean) * lax.rsqrt(square - row_mean * row_mean + epsilon) * norm_gain
    ).astype(jnp.bfloat16)


def full_norm(hidden, norm_gain):
    row_mean = jnp.mean(hidden, axis=1, keepdims=True)
    square = jnp.mean(hidden * hidden, axis=1, keepdims=True)
    return finish_norm(hidden, row_mean, square, norm_gain)


def tp_shift(value, steps):
    count = lax.axis_size("tp")
    return lax.ppermute(value, "tp", [(u, (u + steps) % count) for u in range(count)])


def sum_rows(partial_value):
    tp_count = lax.axis_size("tp")
    me = lax.axis_index("tp")
    rows, cols = partial_value.shape
    pieces = partial_value.astype(jnp.bfloat16).reshape(tp_count, rows // tp_count, cols)
    total = lax.dynamic_index_in_dim(pieces, me, 0, keepdims=False).astype(jnp.float32)
    for steps in range(1, tp_count):
        outgoing = lax.dynamic_index_in_dim(pieces, (me + steps) % tp_count, 0, keepdims=False)
        total = total + tp_shift(outgoing, steps).astype(jnp.float32)
    return total


def gather_rows(row_block):
    tp_count = lax.axis_size("tp")
    me = lax.axis_index("tp")
    arrived = [row_block] + [tp_shift(row_block, steps) for steps in range(1, tp_count)]
    order = (me - jnp.arange(tp_count, dtype=jnp.int32)) % tp_count
    placed = jnp.take(jnp.stack(arrived), order, axis=0)
    return placed.reshape(tp_count * row_block.shape[0], row_block.shape[1])


def block_scores(query_heads, key_heads, query_image, key_image):
    scores = jnp.einsum(
        "qhd,khd->hqk", query_heads, key_heads, preferred_element_type=jnp.float32
    ) * HD ** (-0.5)
    same_image = query_image[:, None] == key_image[None, :]
    return jnp.where(same_image[None], scores, masked_score)


def block_values(weights, value_heads):
    return jnp.einsum(
        "hqk,khd->hqd",
        weights.astype(jnp.bfloat16),
        value_heads,
        preferred_element_type=jnp.float32,
    )


def attend_own_block(query_heads, key_heads, value_heads, query_image, key_image):
    scores = block_scores(query_heads, key_heads, query_image, key_image)
    row_best = jnp.max(scores, axis=2, keepdims=True)
    weights = jnp.exp(scores - row_best)
    row_total = jnp.sum(weights, axis=2, keepdims=True)
    return row_best, row_total, block_values(weights, value_heads)


def attend_more(state, query_heads, key_heads, value_heads, query_image, key_image):
    row_best, row_total, weighted = state
    scores = block_scores(query_heads, key_heads, query_image, key_image)
    new_best = jnp.maximum(row_best, jnp.max(scores, axis=2, keepdims=True))
    rescale = jnp.exp(row_best - new_best)
    weights = jnp.exp(scores - new_best)
    row_total = row_total * rescale + jnp.sum(weights, axis=2, keepdims=True)
    weighted = weighted * rescale + block_values(weights, value_heads)
    return new_best, row_total, weighted


def image_of_groups(groups, starts, group_total):
    inside = (groups >= 0) & (groups < group_total)
    image = jnp.sum((starts[None, :] <= groups[:, None]).astype(jnp.int32), axis=1) - 1
    return jnp.where(inside, image, -1)


def route_to_owners(projected, starts, counts, image_slot, device, seq_count):
    group_rows, out_cols = projected.shape
    per_pair = group_rows // seq_count
    spread = projected.reshape(per_pair, seq_count, out_cols).transpose(1, 0, 2)
    spread = lax.all_to_all(spread, "seq", split_axis=0, concat_axis=0, tiled=True)
    held = spread.reshape(group_rows, out_cols)
    image_count = image_slot.shape[0]
    most_rows = REACH * group_rows
    per_owner = most_rows // seq_count
    image_ids = jnp.arange(image_count, dtype=jnp.int32)
    owners = jnp.arange(seq_count, dtype=jnp.int32)
    owned_image = jnp.sum(
        jnp.where(image_slot[None, :] == owners[:, None], image_ids[None, :], 0), axis=1
    )
    owner_start = starts[owned_image]
    owner_count = counts[owned_image]
    first_pos = jnp.mod(device - owner_start, seq_count)
    first_row = (owner_start + first_pos - device) // seq_count
    steps = jnp.arange(per_owner, dtype=jnp.int32)
    rows = first_row[:, None] + steps[None, :]
    valid = (first_pos[:, None] + seq_count * steps[None, :]) < owner_count[:, None]
    rows = jnp.clip(rows, 0, group_rows - 1)
    outgoing = jnp.take(held, rows.reshape(-1), axis=0).reshape(seq_count, per_owner, out_cols)
    outgoing = jnp.where(valid[:, :, None], outgoing, jnp.zeros((), outgoing.dtype))
    received = lax.all_to_all(outgoing, "seq", split_axis=0, concat_axis=0, tiled=True)
    own_image = jnp.sum(jnp.where(image_slot == device, image_ids, 0))
    own_start = starts[own_image]
    order = jnp.mod(own_start + jnp.arange(seq_count, dtype=jnp.int32), seq_count)
    placed = jnp.take(received, order, axis=0).transpose(1, 0, 2)
    return placed.reshape(most_rows, out_cols)


def shards(
    tokens,
    group_image,
    image_slot,
    attention_gain,
    query_weight,
    key_weight,
    value_weight,
    output_weight,
    feedforward_gain,
    up_weight,
    down_weight,
    merge_gain,
    merge_weight,
):
    device = lax.axis_index("seq")
    seq_count = lax.axis_size("seq")
    token_rows = tokens.shape[0]
    group_rows = group_image.shape[0]
    group_total = group_rows * seq_count
    image_count = image_slot.shape[0]
    image_ids = jnp.arange(image_count, dtype=jnp.int32)
    local_counts = jnp.sum(
        (group_image[:, None] == image_ids[None, :]).astype(jnp.int32), axis=0
    )
    query_image = jnp.repeat(group_image, 4)
    residual = tokens.astype(jnp.float32)
    normed = full_norm(residual, attention_gain)
    head_count = query_weight.shape[1] // HD
    queries = jnp.dot(normed, query_weight, preferred_element_type=jnp.float32).astype(jnp.bfloat16)
    key_rows = jnp.dot(normed, key_weight, preferred_element_type=jnp.float32).astype(jnp.bfloat16)
    value_rows = jnp.dot(normed, value_weight, preferred_element_type=jnp.float32).astype(
        jnp.bfloat16
    )
    query_heads = queries.reshape(token_rows, head_count, HD)
    id_rows = jnp.zeros((2, 8, key_rows.shape[1]), jnp.bfloat16)
    id_rows = id_rows.at[:, 0, :group_rows].set(group_image.astype(jnp.bfloat16))
    key_value = jnp.concatenate([jnp.stack([key_rows, value_rows]), id_rows], axis=1)

    def images_of_block(source, block):
        present = (source >= 0) & (source < seq_count)
        images = block[0, token_rows, :group_rows].astype(jnp.int32)
        return jnp.repeat(jnp.where(present, images, -1), 4)

    state = attend_own_block(
        query_heads,
        key_value[0, :token_rows].reshape(token_rows, head_count, HD),
        key_value[1, :token_rows].reshape(token_rows, head_count, HD),
        query_image,
        query_image,
    )
    near = {step: shifted(key_value, "seq", step) for step in (1, -1, 2, -2)}
    far = {
        3: shifted(near[2], "seq", 1),
        -3: shifted(near[-2], "seq", -1),
        4: shifted(near[2], "seq", 2),
        -4: shifted(near[-2], "seq", -2),
    }
    arrived = {**near, **far}
    for step in (1, -1, 2, -2, 3, -3, 4, -4):
        block = arrived[step]
        source = device - step
        if step > 0:
            needed = lambda k: k[-1] == query_image[0]
        else:
            needed = lambda k: k[0] == query_image[-1]
        key_image = images_of_block(source, block)
        state = lax.cond(
            needed(key_image),
            lambda st, blk, kim: attend_more(
                st,
                query_heads,
                blk[0, :token_rows].reshape(token_rows, head_count, HD),
                blk[1, :token_rows].reshape(token_rows, head_count, HD),
                query_image,
                kim,
            ),
            lambda st, blk, kim: st,
            state,
            block,
            key_image,
        )
    row_best, row_total, weighted = state
    tie = (row_total[0, 0, 0] < 0.0).astype(jnp.int32)
    every_count = lax.all_to_all(
        jnp.broadcast_to(local_counts[None, :] + tie, (seq_count, image_count)),
        "seq",
        split_axis=0,
        concat_axis=0,
        tiled=True,
    )
    counts = jnp.sum(every_count, axis=0)
    starts = jnp.cumsum(counts) - counts
    context = jnp.transpose(weighted / row_total, (1, 0, 2))
    context = context.astype(jnp.bfloat16).reshape(token_rows, head_count * HD)
    attention_part = jnp.dot(context, output_weight, preferred_element_type=jnp.float32)
    tp_count = lax.axis_size("tp")
    own_rows = token_rows // tp_count
    own_residual = lax.dynamic_slice_in_dim(residual, lax.axis_index("tp") * own_rows, own_rows, 0)
    after_attention = own_residual + sum_rows(attention_part)
    normed_two = gather_rows(full_norm(after_attention, feedforward_gain))
    hidden_units = jax.nn.gelu(
        jnp.dot(normed_two, up_weight, preferred_element_type=jnp.float32), approximate=False
    ).astype(jnp.bfloat16)
    after_feedforward = after_attention + sum_rows(
        jnp.dot(hidden_units, down_weight, preferred_element_type=jnp.float32)
    )
    normed_three = gather_rows(full_norm(after_feedforward, merge_gain))
    grouped = normed_three.reshape(group_rows, 4 * D)
    projected = jnp.dot(grouped, merge_weight, preferred_element_type=jnp.float32).astype(
        jnp.bfloat16
    )
    return route_to_owners(projected, starts, counts, image_slot, device, seq_count)[None]


def solution(mesh):
    return jax.shard_map(
        shards,
        mesh=mesh,
        in_specs=(
            P("seq", None),
            P("seq"),
            P(),
            P(),
            P(None, "tp"),
            P(None, "tp"),
            P(None, "tp"),
            P("tp", None),
            P(),
            P(None, "tp"),
            P("tp", None),
            P(),
            P(None, "tp"),
        ),
        out_specs=P("seq", None, "tp"),
        check_vma=False,
    )
```

```python
import jax
import jax.numpy as jnp
from jax import lax
from jax.sharding import PartitionSpec as P

D = 1408
HD = 88
REACH = 4


epsilon = 1e-06
masked_score = -1e30


def shifted(value, axis, steps):
    count = lax.axis_size(axis)
    initial, last = (max(0, -steps), min(count, count - steps))
    return lax.ppermute(value, axis, [(source, source + steps) for source in range(initial, last)])


def finish_norm(hidden, row_mean, square, norm_gain):
    return (
        (hidden - row_mean) * lax.rsqrt(square - row_mean * row_mean + epsilon) * norm_gain
    ).astype(jnp.bfloat16)


def full_norm(hidden, norm_gain):
    row_mean = jnp.mean(hidden, axis=1, keepdims=True)
    square = jnp.mean(hidden * hidden, axis=1, keepdims=True)
    return finish_norm(hidden, row_mean, square, norm_gain)


def tp_shift(value, steps):
    count = lax.axis_size("tp")
    return lax.ppermute(value, "tp", [(u, (u + steps) % count) for u in range(count)])


def sum_rows(partial_value):
    tp_count = lax.axis_size("tp")
    me = lax.axis_index("tp")
    rows, cols = partial_value.shape
    pieces = partial_value.astype(jnp.bfloat16).reshape(tp_count, rows // tp_count, cols)
    total = lax.dynamic_index_in_dim(pieces, me, 0, keepdims=False).astype(jnp.float32)
    for steps in range(1, tp_count):
        outgoing = lax.dynamic_index_in_dim(pieces, (me + steps) % tp_count, 0, keepdims=False)
        total = total + tp_shift(outgoing, steps).astype(jnp.float32)
    return total


def gather_rows(row_block):
    tp_count = lax.axis_size("tp")
    me = lax.axis_index("tp")
    arrived = [row_block] + [tp_shift(row_block, steps) for steps in range(1, tp_count)]
    order = (me - jnp.arange(tp_count, dtype=jnp.int32)) % tp_count
    placed = jnp.take(jnp.stack(arrived), order, axis=0)
    return placed.reshape(tp_count * row_block.shape[0], row_block.shape[1])


def block_scores(query_heads, key_heads, query_image, key_image):
    scores = jnp.einsum(
        "qhd,khd->hqk", query_heads, key_heads, preferred_element_type=jnp.float32
    ) * HD ** (-0.5)
    same_image = query_image[:, None] == key_image[None, :]
    return jnp.where(same_image[None], scores, masked_score)


def block_values(weights, value_heads):
    return jnp.einsum(
        "hqk,khd->hqd",
        weights.astype(jnp.bfloat16),
        value_heads,
        preferred_element_type=jnp.float32,
    )


def attend_own_block(query_heads, key_heads, value_heads, query_image, key_image):
    scores = block_scores(query_heads, key_heads, query_image, key_image)
    row_best = jnp.max(scores, axis=2, keepdims=True)
    weights = jnp.exp(scores - row_best)
    row_total = jnp.sum(weights, axis=2, keepdims=True)
    return row_best, row_total, block_values(weights, value_heads)


def attend_more(state, query_heads, key_heads, value_heads, query_image, key_image):
    row_best, row_total, weighted = state
    scores = block_scores(query_heads, key_heads, query_image, key_image)
    new_best = jnp.maximum(row_best, jnp.max(scores, axis=2, keepdims=True))
    rescale = jnp.exp(row_best - new_best)
    weights = jnp.exp(scores - new_best)
    row_total = row_total * rescale + jnp.sum(weights, axis=2, keepdims=True)
    weighted = weighted * rescale + block_values(weights, value_heads)
    return new_best, row_total, weighted


def image_of_groups(groups, starts, group_total):
    inside = (groups >= 0) & (groups < group_total)
    image = jnp.sum((starts[None, :] <= groups[:, None]).astype(jnp.int32), axis=1) - 1
    return jnp.where(inside, image, -1)


def route_to_owners(projected, starts, counts, image_slot, device, seq_count):
    group_rows, out_cols = projected.shape
    per_pair = group_rows // seq_count
    spread = projected.reshape(per_pair, seq_count, out_cols).transpose(1, 0, 2)
    spread = lax.all_to_all(spread, "seq", split_axis=0, concat_axis=0, tiled=True)
    held = spread.reshape(group_rows, out_cols)
    image_count = image_slot.shape[0]
    most_rows = REACH * group_rows
    per_owner = most_rows // seq_count
    image_ids = jnp.arange(image_count, dtype=jnp.int32)
    owners = jnp.arange(seq_count, dtype=jnp.int32)
    owned_image = jnp.sum(
        jnp.where(image_slot[None, :] == owners[:, None], image_ids[None, :], 0), axis=1
    )
    owner_start = starts[owned_image]
    owner_count = counts[owned_image]
    first_pos = jnp.mod(device - owner_start, seq_count)
    first_row = (owner_start + first_pos - device) // seq_count
    steps = jnp.arange(per_owner, dtype=jnp.int32)
    rows = first_row[:, None] + steps[None, :]
    valid = (first_pos[:, None] + seq_count * steps[None, :]) < owner_count[:, None]
    rows = jnp.clip(rows, 0, group_rows - 1)
    outgoing = jnp.take(held, rows.reshape(-1), axis=0).reshape(seq_count, per_owner, out_cols)
    outgoing = jnp.where(valid[:, :, None], outgoing, jnp.zeros((), outgoing.dtype))
    received = lax.all_to_all(outgoing, "seq", split_axis=0, concat_axis=0, tiled=True)
    own_image = jnp.sum(jnp.where(image_slot == device, image_ids, 0))
    own_start = starts[own_image]
    order = jnp.mod(own_start + jnp.arange(seq_count, dtype=jnp.int32), seq_count)
    placed = jnp.take(received, order, axis=0).transpose(1, 0, 2)
    return placed.reshape(most_rows, out_cols)


def shards(
    tokens,
    group_image,
    image_slot,
    attention_gain,
    query_weight,
    key_weight,
    value_weight,
    output_weight,
    feedforward_gain,
    up_weight,
    down_weight,
    merge_gain,
    merge_weight,
):
    device = lax.axis_index("seq")
    seq_count = lax.axis_size("seq")
    token_rows = tokens.shape[0]
    group_rows = group_image.shape[0]
    group_total = group_rows * seq_count
    image_count = image_slot.shape[0]
    image_ids = jnp.arange(image_count, dtype=jnp.int32)
    local_counts = jnp.sum(
        (group_image[:, None] == image_ids[None, :]).astype(jnp.int32), axis=0
    )
    every_count = lax.all_to_all(
        jnp.broadcast_to(local_counts[None, :], (seq_count, image_count)),
        "seq",
        split_axis=0,
        concat_axis=0,
        tiled=True,
    )
    counts = jnp.sum(every_count, axis=0)
    query_image = jnp.repeat(group_image, 4)
    residual = tokens.astype(jnp.float32)
    normed = full_norm(residual, attention_gain)
    head_count = query_weight.shape[1] // HD
    queries = jnp.dot(normed, query_weight, preferred_element_type=jnp.float32).astype(jnp.bfloat16)
    key_rows = jnp.dot(normed, key_weight, preferred_element_type=jnp.float32).astype(jnp.bfloat16)
    value_rows = jnp.dot(normed, value_weight, preferred_element_type=jnp.float32).astype(
        jnp.bfloat16
    )
    query_heads = queries.reshape(token_rows, head_count, HD)
    key_value = jnp.stack([key_rows, value_rows])
    counts, key_value = lax.optimization_barrier((counts, key_value))
    starts = jnp.cumsum(counts) - counts

    def images_of_block(source):
        groups = source * group_rows + jnp.arange(group_rows, dtype=jnp.int32)
        return jnp.repeat(image_of_groups(groups, starts, group_total), 4)

    state = attend_own_block(
        query_heads,
        key_value[0].reshape(token_rows, head_count, HD),
        key_value[1].reshape(token_rows, head_count, HD),
        query_image,
        query_image,
    )
    near = {step: shifted(key_value, "seq", step) for step in (1, -1, 2, -2)}
    far = {
        3: shifted(near[2], "seq", 1),
        -3: shifted(near[-2], "seq", -1),
        4: shifted(near[2], "seq", 2),
        -4: shifted(near[-2], "seq", -2),
    }
    arrived = {**near, **far}
    for step in (1, -1, 2, -2, 3, -3, 4, -4):
        block = arrived[step]
        source = device - step
        if step > 0:
            needed = lambda k: k[-1] == query_image[0]
        else:
            needed = lambda k: k[0] == query_image[-1]
        key_image = images_of_block(source)
        state = lax.cond(
            needed(key_image),
            lambda st, blk, kim: attend_more(
                st,
                query_heads,
                blk[0].reshape(token_rows, head_count, HD),
                blk[1].reshape(token_rows, head_count, HD),
                query_image,
                kim,
            ),
            lambda st, blk, kim: st,
            state,
            block,
            key_image,
        )
    row_best, row_total, weighted = state
    context = jnp.transpose(weighted / row_total, (1, 0, 2))
    context = context.astype(jnp.bfloat16).reshape(token_rows, head_count * HD)
    attention_part = jnp.dot(context, output_weight, preferred_element_type=jnp.float32)
    tp_count = lax.axis_size("tp")
    own_rows = token_rows // tp_count
    own_residual = lax.dynamic_slice_in_dim(residual, lax.axis_index("tp") * own_rows, own_rows, 0)
    after_attention = own_residual + sum_rows(attention_part)
    normed_two = gather_rows(full_norm(after_attention, feedforward_gain))
    hidden_units = jax.nn.gelu(
        jnp.dot(normed_two, up_weight, preferred_element_type=jnp.float32), approximate=False
    ).astype(jnp.bfloat16)
    hidden_units = lax.optimization_barrier(hidden_units)
    after_feedforward = after_attention + sum_rows(
        jnp.dot(hidden_units, down_weight, preferred_element_type=jnp.float32)
    )
    normed_three = gather_rows(full_norm(after_feedforward, merge_gain))
    grouped = normed_three.reshape(group_rows, 4 * D)
    projected = jnp.dot(grouped, merge_weight, preferred_element_type=jnp.float32).astype(
        jnp.bfloat16
    )
    return route_to_owners(projected, starts, counts, image_slot, device, seq_count)[None]


def solution(mesh):
    return jax.shard_map(
        shards,
        mesh=mesh,
        in_specs=(
            P("seq", None),
            P("seq"),
            P(),
            P(),
            P(None, "tp"),
            P(None, "tp"),
            P(None, "tp"),
            P("tp", None),
            P(),
            P(None, "tp"),
            P("tp", None),
            P(),
            P(None, "tp"),
        ),
        out_specs=P("seq", None, "tp"),
        check_vma=False,
    )
```

```python
import jax
import jax.numpy as jnp
from jax import lax
from jax.sharding import PartitionSpec as P

D = 1408
HD = 88
REACH = 4


epsilon = 1e-06
masked_score = -1e30


def shifted(value, axis, steps):
    count = lax.axis_size(axis)
    initial, last = (max(0, -steps), min(count, count - steps))
    return lax.ppermute(value, axis, [(source, source + steps) for source in range(initial, last)])


def finish_norm(hidden, row_mean, square, norm_gain):
    return (
        (hidden - row_mean) * lax.rsqrt(square - row_mean * row_mean + epsilon) * norm_gain
    ).astype(jnp.bfloat16)


def full_norm(hidden, norm_gain):
    row_mean = jnp.mean(hidden, axis=1, keepdims=True)
    square = jnp.mean(hidden * hidden, axis=1, keepdims=True)
    return finish_norm(hidden, row_mean, square, norm_gain)


def tp_shift(value, steps):
    count = lax.axis_size("tp")
    return lax.ppermute(value, "tp", [(u, (u + steps) % count) for u in range(count)])


def sum_rows(partial_value):
    tp_count = lax.axis_size("tp")
    me = lax.axis_index("tp")
    rows, cols = partial_value.shape
    pieces = partial_value.astype(jnp.bfloat16).reshape(tp_count, rows // tp_count, cols)
    total = lax.dynamic_index_in_dim(pieces, me, 0, keepdims=False).astype(jnp.float32)
    for steps in range(1, tp_count):
        outgoing = lax.dynamic_index_in_dim(pieces, (me + steps) % tp_count, 0, keepdims=False)
        total = total + tp_shift(outgoing, steps).astype(jnp.float32)
    return total


def gather_rows(row_block):
    tp_count = lax.axis_size("tp")
    me = lax.axis_index("tp")
    arrived = [row_block] + [tp_shift(row_block, steps) for steps in range(1, tp_count)]
    order = (me - jnp.arange(tp_count, dtype=jnp.int32)) % tp_count
    placed = jnp.take(jnp.stack(arrived), order, axis=0)
    return placed.reshape(tp_count * row_block.shape[0], row_block.shape[1])


def block_scores(query_heads, key_heads, query_image, key_image):
    scores = jnp.einsum(
        "qhd,khd->hqk", query_heads, key_heads, preferred_element_type=jnp.float32
    ) * HD ** (-0.5)
    same_image = query_image[:, None] == key_image[None, :]
    return jnp.where(same_image[None], scores, masked_score)


def block_values(weights, value_heads):
    return jnp.einsum(
        "hqk,khd->hqd",
        weights.astype(jnp.bfloat16),
        value_heads,
        preferred_element_type=jnp.float32,
    )


def attend_own_block(query_heads, key_heads, value_heads, query_image, key_image):
    scores = block_scores(query_heads, key_heads, query_image, key_image)
    row_best = jnp.max(scores, axis=2, keepdims=True)
    weights = jnp.exp(scores - row_best)
    row_total = jnp.sum(weights, axis=2, keepdims=True)
    return row_best, row_total, block_values(weights, value_heads)


def attend_more(state, query_heads, key_heads, value_heads, query_image, key_image):
    row_best, row_total, weighted = state
    scores = block_scores(query_heads, key_heads, query_image, key_image)
    new_best = jnp.maximum(row_best, jnp.max(scores, axis=2, keepdims=True))
    rescale = jnp.exp(row_best - new_best)
    weights = jnp.exp(scores - new_best)
    row_total = row_total * rescale + jnp.sum(weights, axis=2, keepdims=True)
    weighted = weighted * rescale + block_values(weights, value_heads)
    return new_best, row_total, weighted


def image_of_groups(groups, starts, group_total):
    inside = (groups >= 0) & (groups < group_total)
    image = jnp.sum((starts[None, :] <= groups[:, None]).astype(jnp.int32), axis=1) - 1
    return jnp.where(inside, image, -1)


def route_to_owners(projected, starts, counts, image_slot, device, seq_count):
    group_rows, out_cols = projected.shape
    per_pair = group_rows // seq_count
    spread = projected.reshape(per_pair, seq_count, out_cols).transpose(1, 0, 2)
    spread = lax.all_to_all(spread, "seq", split_axis=0, concat_axis=0, tiled=True)
    held = spread.reshape(group_rows, out_cols)
    image_count = image_slot.shape[0]
    most_rows = REACH * group_rows
    per_owner = most_rows // seq_count
    image_ids = jnp.arange(image_count, dtype=jnp.int32)
    owners = jnp.arange(seq_count, dtype=jnp.int32)
    owned_image = jnp.sum(
        jnp.where(image_slot[None, :] == owners[:, None], image_ids[None, :], 0), axis=1
    )
    owner_start = starts[owned_image]
    owner_count = counts[owned_image]
    first_pos = jnp.mod(device - owner_start, seq_count)
    first_row = (owner_start + first_pos - device) // seq_count
    steps = jnp.arange(per_owner, dtype=jnp.int32)
    rows = first_row[:, None] + steps[None, :]
    valid = (first_pos[:, None] + seq_count * steps[None, :]) < owner_count[:, None]
    rows = jnp.clip(rows, 0, group_rows - 1)
    outgoing = jnp.take(held, rows.reshape(-1), axis=0).reshape(seq_count, per_owner, out_cols)
    outgoing = jnp.where(valid[:, :, None], outgoing, jnp.zeros((), outgoing.dtype))
    received = lax.all_to_all(outgoing, "seq", split_axis=0, concat_axis=0, tiled=True)
    own_image = jnp.sum(jnp.where(image_slot == device, image_ids, 0))
    own_start = starts[own_image]
    order = jnp.mod(own_start + jnp.arange(seq_count, dtype=jnp.int32), seq_count)
    placed = jnp.take(received, order, axis=0).transpose(1, 0, 2)
    return placed.reshape(most_rows, out_cols)


def shards(
    tokens,
    group_image,
    image_slot,
    attention_gain,
    query_weight,
    key_weight,
    value_weight,
    output_weight,
    feedforward_gain,
    up_weight,
    down_weight,
    merge_gain,
    merge_weight,
):
    device = lax.axis_index("seq")
    seq_count = lax.axis_size("seq")
    token_rows = tokens.shape[0]
    group_rows = group_image.shape[0]
    group_total = group_rows * seq_count
    image_count = image_slot.shape[0]
    image_ids = jnp.arange(image_count, dtype=jnp.int32)
    local_counts = jnp.sum(
        (group_image[:, None] == image_ids[None, :]).astype(jnp.int32), axis=0
    )
    every_count = lax.all_to_all(
        jnp.broadcast_to(local_counts[None, :], (seq_count, image_count)),
        "seq",
        split_axis=0,
        concat_axis=0,
        tiled=True,
    )
    counts = jnp.sum(every_count, axis=0)
    query_image = jnp.repeat(group_image, 4)
    residual = tokens.astype(jnp.float32)
    normed = full_norm(residual, attention_gain)
    head_count = query_weight.shape[1] // HD
    queries = jnp.dot(normed, query_weight, preferred_element_type=jnp.float32).astype(jnp.bfloat16)
    key_rows = jnp.dot(normed, key_weight, preferred_element_type=jnp.float32).astype(jnp.bfloat16)
    value_rows = jnp.dot(normed, value_weight, preferred_element_type=jnp.float32).astype(
        jnp.bfloat16
    )
    query_heads = queries.reshape(token_rows, head_count, HD)
    key_value = jnp.stack([key_rows, value_rows])
    counts, key_value = lax.optimization_barrier((counts, key_value))
    starts = jnp.cumsum(counts) - counts

    def images_of_block(source):
        groups = source * group_rows + jnp.arange(group_rows, dtype=jnp.int32)
        return jnp.repeat(image_of_groups(groups, starts, group_total), 4)

    state = attend_own_block(
        query_heads,
        key_value[0].reshape(token_rows, head_count, HD),
        key_value[1].reshape(token_rows, head_count, HD),
        query_image,
        query_image,
    )
    near = {step: shifted(key_value, "seq", step) for step in (1, -1, 2, -2)}
    far = {
        3: shifted(near[2], "seq", 1),
        -3: shifted(near[-2], "seq", -1),
        4: shifted(near[2], "seq", 2),
        -4: shifted(near[-2], "seq", -2),
    }
    arrived = {**near, **far}
    for step in (1, -1, 2, -2, 3, -3, 4, -4):
        block = arrived[step]
        source = device - step
        if step > 0:
            needed = lambda k: k[-1] == query_image[0]
        else:
            needed = lambda k: k[0] == query_image[-1]
        key_image = images_of_block(source)
        state = lax.cond(
            needed(key_image),
            lambda st, blk, kim: attend_more(
                st,
                query_heads,
                blk[0].reshape(token_rows, head_count, HD),
                blk[1].reshape(token_rows, head_count, HD),
                query_image,
                kim,
            ),
            lambda st, blk, kim: st,
            state,
            block,
            key_image,
        )
    row_best, row_total, weighted = state
    context = jnp.transpose(weighted / row_total, (1, 0, 2))
    context = context.astype(jnp.bfloat16).reshape(token_rows, head_count * HD)
    attention_part = jnp.dot(context, output_weight, preferred_element_type=jnp.float32)
    tp_count = lax.axis_size("tp")
    own_rows = token_rows // tp_count
    own_residual = lax.dynamic_slice_in_dim(residual, lax.axis_index("tp") * own_rows, own_rows, 0)
    after_attention = own_residual + sum_rows(attention_part)
    me = lax.axis_index("tp")

    def feed_forward(rows):
        hidden = jax.nn.gelu(
            jnp.dot(rows, up_weight, preferred_element_type=jnp.float32), approximate=False
        ).astype(jnp.bfloat16)
        return jnp.dot(hidden, down_weight, preferred_element_type=jnp.float32)

    normed_two = full_norm(after_attention, feedforward_gain)
    visiting = [tp_shift(normed_two, steps) for steps in range(1, tp_count)]
    ff_total = feed_forward(normed_two)
    for steps, rows in zip(range(1, tp_count), visiting):
        returned = tp_shift(feed_forward(rows).astype(jnp.bfloat16), -steps)
        ff_total = ff_total + returned.astype(jnp.float32)
    after_feedforward = after_attention + ff_total
    normed_three = full_norm(after_feedforward, merge_gain)
    own_groups = normed_three.reshape(own_rows // 4, 4 * D)

    def merge(groups):
        return jnp.dot(groups, merge_weight, preferred_element_type=jnp.float32).astype(
            jnp.bfloat16
        )

    merged = [merge(own_groups)] + [
        merge(tp_shift(own_groups, steps)) for steps in range(1, tp_count)
    ]
    order = (me - jnp.arange(tp_count, dtype=jnp.int32)) % tp_count
    projected = jnp.take(jnp.stack(merged), order, axis=0).reshape(group_rows, -1)
    return route_to_owners(projected, starts, counts, image_slot, device, seq_count)[None]


def solution(mesh):
    return jax.shard_map(
        shards,
        mesh=mesh,
        in_specs=(
            P("seq", None),
            P("seq"),
            P(),
            P(),
            P(None, "tp"),
            P(None, "tp"),
            P(None, "tp"),
            P("tp", None),
            P(),
            P(None, "tp"),
            P("tp", None),
            P(),
            P(None, "tp"),
        ),
        out_specs=P("seq", None, "tp"),
        check_vma=False,
    )
```

```python
import jax
import jax.numpy as jnp
from jax import lax
from jax.sharding import PartitionSpec as P

D = 1408
HD = 88
REACH = 4


epsilon = 1e-06
masked_score = -1e30


def shifted(value, axis, steps):
    count = lax.axis_size(axis)
    initial, last = (max(0, -steps), min(count, count - steps))
    return lax.ppermute(value, axis, [(source, source + steps) for source in range(initial, last)])


def finish_norm(hidden, row_mean, square, norm_gain):
    return (
        (hidden - row_mean) * lax.rsqrt(square - row_mean * row_mean + epsilon) * norm_gain
    ).astype(jnp.bfloat16)


def full_norm(hidden, norm_gain):
    row_mean = jnp.mean(hidden, axis=1, keepdims=True)
    square = jnp.mean(hidden * hidden, axis=1, keepdims=True)
    return finish_norm(hidden, row_mean, square, norm_gain)


def tp_shift(value, steps):
    count = lax.axis_size("tp")
    return lax.ppermute(value, "tp", [(u, (u + steps) % count) for u in range(count)])


def sum_rows(partial_value):
    tp_count = lax.axis_size("tp")
    me = lax.axis_index("tp")
    rows, cols = partial_value.shape
    pieces = partial_value.astype(jnp.bfloat16).reshape(tp_count, rows // tp_count, cols)
    total = lax.dynamic_index_in_dim(pieces, me, 0, keepdims=False).astype(jnp.float32)
    for steps in range(1, tp_count):
        outgoing = lax.dynamic_index_in_dim(pieces, (me + steps) % tp_count, 0, keepdims=False)
        total = total + tp_shift(outgoing, steps).astype(jnp.float32)
    return total


def gather_rows(row_block):
    tp_count = lax.axis_size("tp")
    me = lax.axis_index("tp")
    arrived = [row_block] + [tp_shift(row_block, steps) for steps in range(1, tp_count)]
    order = (me - jnp.arange(tp_count, dtype=jnp.int32)) % tp_count
    placed = jnp.take(jnp.stack(arrived), order, axis=0)
    return placed.reshape(tp_count * row_block.shape[0], row_block.shape[1])


def block_scores(query_heads, key_heads, query_image, key_image):
    scores = jnp.einsum(
        "qhd,khd->hqk", query_heads, key_heads, preferred_element_type=jnp.float32
    ) * HD ** (-0.5)
    same_image = query_image[:, None] == key_image[None, :]
    return jnp.where(same_image[None], scores, masked_score)


def block_values(weights, value_heads):
    return jnp.einsum(
        "hqk,khd->hqd",
        weights.astype(jnp.bfloat16),
        value_heads,
        preferred_element_type=jnp.float32,
    )


def attend_own_block(query_heads, key_heads, value_heads, query_image, key_image):
    scores = block_scores(query_heads, key_heads, query_image, key_image)
    row_best = jnp.max(scores, axis=2, keepdims=True)
    weights = jnp.exp(scores - row_best)
    row_total = jnp.sum(weights, axis=2, keepdims=True)
    return row_best, row_total, block_values(weights, value_heads)


def attend_more(state, query_heads, key_heads, value_heads, query_image, key_image):
    row_best, row_total, weighted = state
    scores = block_scores(query_heads, key_heads, query_image, key_image)
    new_best = jnp.maximum(row_best, jnp.max(scores, axis=2, keepdims=True))
    rescale = jnp.exp(row_best - new_best)
    weights = jnp.exp(scores - new_best)
    row_total = row_total * rescale + jnp.sum(weights, axis=2, keepdims=True)
    weighted = weighted * rescale + block_values(weights, value_heads)
    return new_best, row_total, weighted


def image_of_groups(groups, starts, group_total):
    inside = (groups >= 0) & (groups < group_total)
    image = jnp.sum((starts[None, :] <= groups[:, None]).astype(jnp.int32), axis=1) - 1
    return jnp.where(inside, image, -1)


def route_to_owners(projected, starts, counts, image_slot, device, seq_count):
    group_rows, out_cols = projected.shape
    per_pair = group_rows // seq_count
    spread = projected.reshape(per_pair, seq_count, out_cols).transpose(1, 0, 2)
    spread = lax.all_to_all(spread, "seq", split_axis=0, concat_axis=0, tiled=True)
    held = spread.reshape(group_rows, out_cols)
    image_count = image_slot.shape[0]
    most_rows = REACH * group_rows
    per_owner = most_rows // seq_count
    image_ids = jnp.arange(image_count, dtype=jnp.int32)
    owners = jnp.arange(seq_count, dtype=jnp.int32)
    owned_image = jnp.sum(
        jnp.where(image_slot[None, :] == owners[:, None], image_ids[None, :], 0), axis=1
    )
    owner_start = starts[owned_image]
    owner_count = counts[owned_image]
    first_pos = jnp.mod(device - owner_start, seq_count)
    first_row = (owner_start + first_pos - device) // seq_count
    steps = jnp.arange(per_owner, dtype=jnp.int32)
    rows = first_row[:, None] + steps[None, :]
    valid = (first_pos[:, None] + seq_count * steps[None, :]) < owner_count[:, None]
    rows = jnp.clip(rows, 0, group_rows - 1)
    outgoing = jnp.take(held, rows.reshape(-1), axis=0).reshape(seq_count, per_owner, out_cols)
    outgoing = jnp.where(valid[:, :, None], outgoing, jnp.zeros((), outgoing.dtype))
    received = lax.all_to_all(outgoing, "seq", split_axis=0, concat_axis=0, tiled=True)
    own_image = jnp.sum(jnp.where(image_slot == device, image_ids, 0))
    own_start = starts[own_image]
    order = jnp.mod(own_start + jnp.arange(seq_count, dtype=jnp.int32), seq_count)
    placed = jnp.take(received, order, axis=0).transpose(1, 0, 2)
    return placed.reshape(most_rows, out_cols)


def shards(
    tokens,
    group_image,
    image_slot,
    attention_gain,
    query_weight,
    key_weight,
    value_weight,
    output_weight,
    feedforward_gain,
    up_weight,
    down_weight,
    merge_gain,
    merge_weight,
):
    device = lax.axis_index("seq")
    seq_count = lax.axis_size("seq")
    token_rows = tokens.shape[0]
    group_rows = group_image.shape[0]
    group_total = group_rows * seq_count
    image_count = image_slot.shape[0]
    image_ids = jnp.arange(image_count, dtype=jnp.int32)
    local_counts = jnp.sum(
        (group_image[:, None] == image_ids[None, :]).astype(jnp.int32), axis=0
    )
    every_count = lax.all_to_all(
        jnp.broadcast_to(local_counts[None, :], (seq_count, image_count)),
        "seq",
        split_axis=0,
        concat_axis=0,
        tiled=True,
    )
    counts = jnp.sum(every_count, axis=0)
    query_image = jnp.repeat(group_image, 4)
    residual = tokens.astype(jnp.float32)
    normed = full_norm(residual, attention_gain)
    head_count = query_weight.shape[1] // HD
    queries = jnp.dot(normed, query_weight, preferred_element_type=jnp.float32).astype(jnp.bfloat16)
    key_rows = jnp.dot(normed, key_weight, preferred_element_type=jnp.float32).astype(jnp.bfloat16)
    value_rows = jnp.dot(normed, value_weight, preferred_element_type=jnp.float32).astype(
        jnp.bfloat16
    )
    query_heads = queries.reshape(token_rows, head_count, HD)
    key_value = jnp.stack([key_rows, value_rows])
    counts, key_value = lax.optimization_barrier((counts, key_value))
    starts = jnp.cumsum(counts) - counts

    def images_of_block(source):
        groups = source * group_rows + jnp.arange(group_rows, dtype=jnp.int32)
        return jnp.repeat(image_of_groups(groups, starts, group_total), 4)

    state = attend_own_block(
        query_heads,
        key_value[0].reshape(token_rows, head_count, HD),
        key_value[1].reshape(token_rows, head_count, HD),
        query_image,
        query_image,
    )
    near = {step: shifted(key_value, "seq", step) for step in (1, -1, 2, -2)}
    far = {
        3: shifted(near[2], "seq", 1),
        -3: shifted(near[-2], "seq", -1),
        4: shifted(near[2], "seq", 2),
        -4: shifted(near[-2], "seq", -2),
    }
    arrived = {**near, **far}
    for step in (1, -1, 2, -2, 3, -3, 4, -4):
        block = arrived[step]
        source = device - step
        if step > 0:
            needed = lambda k: k[-1] == query_image[0]
        else:
            needed = lambda k: k[0] == query_image[-1]
        key_image = images_of_block(source)
        state = lax.cond(
            needed(key_image),
            lambda st, blk, kim: attend_more(
                st,
                query_heads,
                blk[0].reshape(token_rows, head_count, HD),
                blk[1].reshape(token_rows, head_count, HD),
                query_image,
                kim,
            ),
            lambda st, blk, kim: st,
            state,
            block,
            key_image,
        )
    row_best, row_total, weighted = state
    context = jnp.transpose(weighted / row_total, (1, 0, 2))
    context = context.astype(jnp.bfloat16).reshape(token_rows, head_count * HD)
    attention_part = jnp.dot(context, output_weight, preferred_element_type=jnp.float32)
    tp_count = lax.axis_size("tp")
    own_rows = token_rows // tp_count
    own_residual = lax.dynamic_slice_in_dim(residual, lax.axis_index("tp") * own_rows, own_rows, 0)
    after_attention = own_residual + sum_rows(attention_part)
    me = lax.axis_index("tp")

    def feed_forward(rows):
        hidden = jax.nn.gelu(
            jnp.dot(rows, up_weight, preferred_element_type=jnp.float32), approximate=False
        ).astype(jnp.bfloat16)
        return jnp.dot(hidden, down_weight, preferred_element_type=jnp.float32)

    normed_two = full_norm(after_attention, feedforward_gain)
    visiting = [tp_shift(normed_two, steps) for steps in range(1, tp_count)]
    ff_total = feed_forward(normed_two)
    own_done = (ff_total[0, 0] != ff_total[0, 0]).astype(jnp.bfloat16)
    visiting[0] = visiting[0] + own_done
    for steps, rows in zip(range(1, tp_count), visiting):
        returned = tp_shift(feed_forward(rows).astype(jnp.bfloat16), -steps)
        ff_total = ff_total + returned.astype(jnp.float32)
    after_feedforward = after_attention + ff_total
    normed_three = full_norm(after_feedforward, merge_gain)
    own_groups = normed_three.reshape(own_rows // 4, 4 * D)

    def merge(groups):
        return jnp.dot(groups, merge_weight, preferred_element_type=jnp.float32).astype(
            jnp.bfloat16
        )

    merged = [merge(own_groups)] + [
        merge(tp_shift(own_groups, steps)) for steps in range(1, tp_count)
    ]
    order = (me - jnp.arange(tp_count, dtype=jnp.int32)) % tp_count
    projected = jnp.take(jnp.stack(merged), order, axis=0).reshape(group_rows, -1)
    return route_to_owners(projected, starts, counts, image_slot, device, seq_count)[None]


def solution(mesh):
    return jax.shard_map(
        shards,
        mesh=mesh,
        in_specs=(
            P("seq", None),
            P("seq"),
            P(),
            P(),
            P(None, "tp"),
            P(None, "tp"),
            P(None, "tp"),
            P("tp", None),
            P(),
            P(None, "tp"),
            P("tp", None),
            P(),
            P(None, "tp"),
        ),
        out_specs=P("seq", None, "tp"),
        check_vma=False,
    )
```

```python
import jax
import jax.numpy as jnp
from jax import lax
from jax.sharding import PartitionSpec as P

D = 1408
HD = 88
REACH = 4


epsilon = 1e-06
masked_score = -1e30


def shifted(value, axis, steps):
    count = lax.axis_size(axis)
    initial, last = (max(0, -steps), min(count, count - steps))
    return lax.ppermute(value, axis, [(source, source + steps) for source in range(initial, last)])


def finish_norm(hidden, row_mean, square, norm_gain):
    return (
        (hidden - row_mean) * lax.rsqrt(square - row_mean * row_mean + epsilon) * norm_gain
    ).astype(jnp.bfloat16)


def full_norm(hidden, norm_gain):
    row_mean = jnp.mean(hidden, axis=1, keepdims=True)
    square = jnp.mean(hidden * hidden, axis=1, keepdims=True)
    return finish_norm(hidden, row_mean, square, norm_gain)


def tp_shift(value, steps):
    count = lax.axis_size("tp")
    return lax.ppermute(value, "tp", [(u, (u + steps) % count) for u in range(count)])


def sum_rows(partial_value):
    tp_count = lax.axis_size("tp")
    me = lax.axis_index("tp")
    rows, cols = partial_value.shape
    pieces = partial_value.astype(jnp.bfloat16).reshape(tp_count, rows // tp_count, cols)
    total = lax.dynamic_index_in_dim(pieces, me, 0, keepdims=False).astype(jnp.float32)
    for steps in range(1, tp_count):
        outgoing = lax.dynamic_index_in_dim(pieces, (me + steps) % tp_count, 0, keepdims=False)
        total = total + tp_shift(outgoing, steps).astype(jnp.float32)
    return total


def gather_rows(row_block):
    tp_count = lax.axis_size("tp")
    me = lax.axis_index("tp")
    arrived = [row_block] + [tp_shift(row_block, steps) for steps in range(1, tp_count)]
    order = (me - jnp.arange(tp_count, dtype=jnp.int32)) % tp_count
    placed = jnp.take(jnp.stack(arrived), order, axis=0)
    return placed.reshape(tp_count * row_block.shape[0], row_block.shape[1])


def block_scores(query_heads, key_heads, query_image, key_image):
    scores = jnp.einsum(
        "qhd,khd->hqk", query_heads, key_heads, preferred_element_type=jnp.float32
    ) * HD ** (-0.5)
    same_image = query_image[:, None] == key_image[None, :]
    return jnp.where(same_image[None], scores, masked_score)


def block_values(weights, value_heads):
    return jnp.einsum(
        "hqk,khd->hqd",
        weights.astype(jnp.bfloat16),
        value_heads,
        preferred_element_type=jnp.float32,
    )


def attend_own_block(query_heads, key_heads, value_heads, query_image, key_image):
    scores = block_scores(query_heads, key_heads, query_image, key_image)
    row_best = jnp.max(scores, axis=2, keepdims=True)
    weights = jnp.exp(scores - row_best)
    row_total = jnp.sum(weights, axis=2, keepdims=True)
    return row_best, row_total, block_values(weights, value_heads)


def attend_more(state, query_heads, key_heads, value_heads, query_image, key_image):
    row_best, row_total, weighted = state
    scores = block_scores(query_heads, key_heads, query_image, key_image)
    new_best = jnp.maximum(row_best, jnp.max(scores, axis=2, keepdims=True))
    rescale = jnp.exp(row_best - new_best)
    weights = jnp.exp(scores - new_best)
    row_total = row_total * rescale + jnp.sum(weights, axis=2, keepdims=True)
    weighted = weighted * rescale + block_values(weights, value_heads)
    return new_best, row_total, weighted


def image_of_groups(groups, starts, group_total):
    inside = (groups >= 0) & (groups < group_total)
    image = jnp.sum((starts[None, :] <= groups[:, None]).astype(jnp.int32), axis=1) - 1
    return jnp.where(inside, image, -1)


def route_to_owners(projected, starts, counts, image_slot, device, seq_count):
    group_rows, out_cols = projected.shape
    per_pair = group_rows // seq_count
    spread = projected.reshape(per_pair, seq_count, out_cols).transpose(1, 0, 2)
    spread = lax.all_to_all(spread, "seq", split_axis=0, concat_axis=0, tiled=True)
    held = spread.reshape(group_rows, out_cols)
    image_count = image_slot.shape[0]
    most_rows = REACH * group_rows
    per_owner = most_rows // seq_count
    image_ids = jnp.arange(image_count, dtype=jnp.int32)
    owners = jnp.arange(seq_count, dtype=jnp.int32)
    owned_image = jnp.sum(
        jnp.where(image_slot[None, :] == owners[:, None], image_ids[None, :], 0), axis=1
    )
    owner_start = starts[owned_image]
    owner_count = counts[owned_image]
    first_pos = jnp.mod(device - owner_start, seq_count)
    first_row = (owner_start + first_pos - device) // seq_count
    steps = jnp.arange(per_owner, dtype=jnp.int32)
    rows = first_row[:, None] + steps[None, :]
    valid = (first_pos[:, None] + seq_count * steps[None, :]) < owner_count[:, None]
    rows = jnp.clip(rows, 0, group_rows - 1)
    outgoing = jnp.take(held, rows.reshape(-1), axis=0).reshape(seq_count, per_owner, out_cols)
    outgoing = jnp.where(valid[:, :, None], outgoing, jnp.zeros((), outgoing.dtype))
    received = lax.all_to_all(outgoing, "seq", split_axis=0, concat_axis=0, tiled=True)
    own_image = jnp.sum(jnp.where(image_slot == device, image_ids, 0))
    own_start = starts[own_image]
    order = jnp.mod(own_start + jnp.arange(seq_count, dtype=jnp.int32), seq_count)
    placed = jnp.take(received, order, axis=0).transpose(1, 0, 2)
    return placed.reshape(most_rows, out_cols)


def shards(
    tokens,
    group_image,
    image_slot,
    attention_gain,
    query_weight,
    key_weight,
    value_weight,
    output_weight,
    feedforward_gain,
    up_weight,
    down_weight,
    merge_gain,
    merge_weight,
):
    device = lax.axis_index("seq")
    seq_count = lax.axis_size("seq")
    token_rows = tokens.shape[0]
    group_rows = group_image.shape[0]
    group_total = group_rows * seq_count
    image_count = image_slot.shape[0]
    image_ids = jnp.arange(image_count, dtype=jnp.int32)
    local_counts = jnp.sum(
        (group_image[:, None] == image_ids[None, :]).astype(jnp.int32), axis=0
    )
    every_count = lax.all_to_all(
        jnp.broadcast_to(local_counts[None, :], (seq_count, image_count)),
        "seq",
        split_axis=0,
        concat_axis=0,
        tiled=True,
    )
    counts = jnp.sum(every_count, axis=0)
    query_image = jnp.repeat(group_image, 4)
    residual = tokens.astype(jnp.float32)
    normed = full_norm(residual, attention_gain)
    head_count = query_weight.shape[1] // HD
    queries = jnp.dot(normed, query_weight, preferred_element_type=jnp.float32).astype(jnp.bfloat16)
    key_rows = jnp.dot(normed, key_weight, preferred_element_type=jnp.float32).astype(jnp.bfloat16)
    value_rows = jnp.dot(normed, value_weight, preferred_element_type=jnp.float32).astype(
        jnp.bfloat16
    )
    query_heads = queries.reshape(token_rows, head_count, HD)
    output_rows_of_peer = [None] + [
        tp_shift(output_weight, steps) for steps in range(1, lax.axis_size("tp"))
    ]
    key_value = jnp.stack([key_rows, value_rows])
    counts, key_value = lax.optimization_barrier((counts, key_value))
    starts = jnp.cumsum(counts) - counts

    def images_of_block(source):
        groups = source * group_rows + jnp.arange(group_rows, dtype=jnp.int32)
        return jnp.repeat(image_of_groups(groups, starts, group_total), 4)

    state = attend_own_block(
        query_heads,
        key_value[0].reshape(token_rows, head_count, HD),
        key_value[1].reshape(token_rows, head_count, HD),
        query_image,
        query_image,
    )
    near = {step: shifted(key_value, "seq", step) for step in (1, -1, 2, -2)}
    far = {
        3: shifted(near[2], "seq", 1),
        -3: shifted(near[-2], "seq", -1),
        4: shifted(near[2], "seq", 2),
        -4: shifted(near[-2], "seq", -2),
    }
    arrived = {**near, **far}
    for step in (1, -1, 2, -2, 3, -3, 4, -4):
        block = arrived[step]
        source = device - step
        if step > 0:
            needed = lambda k: k[-1] == query_image[0]
        else:
            needed = lambda k: k[0] == query_image[-1]
        key_image = images_of_block(source)
        state = lax.cond(
            needed(key_image),
            lambda st, blk, kim: attend_more(
                st,
                query_heads,
                blk[0].reshape(token_rows, head_count, HD),
                blk[1].reshape(token_rows, head_count, HD),
                query_image,
                kim,
            ),
            lambda st, blk, kim: st,
            state,
            block,
            key_image,
        )
    row_best, row_total, weighted = state
    context = jnp.transpose(weighted / row_total, (1, 0, 2))
    context = context.astype(jnp.bfloat16).reshape(token_rows, head_count * HD)
    tp_count = lax.axis_size("tp")
    own_rows = token_rows // tp_count
    me = lax.axis_index("tp")
    own_residual = lax.dynamic_slice_in_dim(residual, me * own_rows, own_rows, 0)
    context_pieces = context.reshape(tp_count, own_rows, head_count * HD)
    attention_out = jnp.dot(
        context_pieces[me], output_weight, preferred_element_type=jnp.float32
    )
    for steps in range(1, tp_count):
        outgoing = lax.dynamic_index_in_dim(
            context_pieces, (me + steps) % tp_count, 0, keepdims=False
        )
        attention_out = attention_out + jnp.dot(
            tp_shift(outgoing, steps),
            output_rows_of_peer[steps],
            preferred_element_type=jnp.float32,
        )
    after_attention = own_residual + attention_out

    def feed_forward(rows):
        hidden = jax.nn.gelu(
            jnp.dot(rows, up_weight, preferred_element_type=jnp.float32), approximate=False
        ).astype(jnp.bfloat16)
        return jnp.dot(hidden, down_weight, preferred_element_type=jnp.float32)

    normed_two = full_norm(after_attention, feedforward_gain)
    visiting = [tp_shift(normed_two, steps) for steps in range(1, tp_count)]
    ff_total = feed_forward(normed_two)
    own_done = (ff_total[0, 0] != ff_total[0, 0]).astype(jnp.bfloat16)
    visiting[0] = visiting[0] + own_done
    for steps, rows in zip(range(1, tp_count), visiting):
        returned = tp_shift(feed_forward(rows).astype(jnp.bfloat16), -steps)
        ff_total = ff_total + returned.astype(jnp.float32)
    after_feedforward = after_attention + ff_total
    normed_three = full_norm(after_feedforward, merge_gain)
    own_groups = normed_three.reshape(own_rows // 4, 4 * D)

    def merge(groups):
        return jnp.dot(groups, merge_weight, preferred_element_type=jnp.float32).astype(
            jnp.bfloat16
        )

    merged = [merge(own_groups)] + [
        merge(tp_shift(own_groups, steps)) for steps in range(1, tp_count)
    ]
    order = (me - jnp.arange(tp_count, dtype=jnp.int32)) % tp_count
    projected = jnp.take(jnp.stack(merged), order, axis=0).reshape(group_rows, -1)
    return route_to_owners(projected, starts, counts, image_slot, device, seq_count)[None]


def solution(mesh):
    return jax.shard_map(
        shards,
        mesh=mesh,
        in_specs=(
            P("seq", None),
            P("seq"),
            P(),
            P(),
            P(None, "tp"),
            P(None, "tp"),
            P(None, "tp"),
            P("tp", None),
            P(),
            P(None, "tp"),
            P("tp", None),
            P(),
            P(None, "tp"),
        ),
        out_specs=P("seq", None, "tp"),
        check_vma=False,
    )
```

```python
import jax
import jax.numpy as jnp
from jax import lax
from jax.sharding import PartitionSpec as P

D = 1408
HD = 88
REACH = 4


epsilon = 1e-06
masked_score = -1e30


def shifted(value, axis, steps):
    count = lax.axis_size(axis)
    initial, last = (max(0, -steps), min(count, count - steps))
    return lax.ppermute(value, axis, [(source, source + steps) for source in range(initial, last)])


def finish_norm(hidden, row_mean, square, norm_gain):
    return (
        (hidden - row_mean) * lax.rsqrt(square - row_mean * row_mean + epsilon) * norm_gain
    ).astype(jnp.bfloat16)


def full_norm(hidden, norm_gain):
    row_mean = jnp.mean(hidden, axis=1, keepdims=True)
    square = jnp.mean(hidden * hidden, axis=1, keepdims=True)
    return finish_norm(hidden, row_mean, square, norm_gain)


def tp_shift(value, steps):
    count = lax.axis_size("tp")
    return lax.ppermute(value, "tp", [(u, (u + steps) % count) for u in range(count)])


def sum_rows(partial_value):
    tp_count = lax.axis_size("tp")
    me = lax.axis_index("tp")
    rows, cols = partial_value.shape
    pieces = partial_value.astype(jnp.bfloat16).reshape(tp_count, rows // tp_count, cols)
    total = lax.dynamic_index_in_dim(pieces, me, 0, keepdims=False).astype(jnp.float32)
    for steps in range(1, tp_count):
        outgoing = lax.dynamic_index_in_dim(pieces, (me + steps) % tp_count, 0, keepdims=False)
        total = total + tp_shift(outgoing, steps).astype(jnp.float32)
    return total


def gather_rows(row_block):
    tp_count = lax.axis_size("tp")
    me = lax.axis_index("tp")
    arrived = [row_block] + [tp_shift(row_block, steps) for steps in range(1, tp_count)]
    order = (me - jnp.arange(tp_count, dtype=jnp.int32)) % tp_count
    placed = jnp.take(jnp.stack(arrived), order, axis=0)
    return placed.reshape(tp_count * row_block.shape[0], row_block.shape[1])


def block_scores(query_heads, key_heads, query_image, key_image):
    scores = jnp.einsum(
        "qhd,khd->hqk", query_heads, key_heads, preferred_element_type=jnp.float32
    ) * HD ** (-0.5)
    same_image = query_image[:, None] == key_image[None, :]
    return jnp.where(same_image[None], scores, masked_score)


def block_values(weights, value_heads):
    return jnp.einsum(
        "hqk,khd->hqd",
        weights.astype(jnp.bfloat16),
        value_heads,
        preferred_element_type=jnp.float32,
    )


def attend_own_block(query_heads, key_heads, value_heads, query_image, key_image):
    scores = block_scores(query_heads, key_heads, query_image, key_image)
    row_best = jnp.max(scores, axis=2, keepdims=True)
    weights = jnp.exp(scores - row_best)
    row_total = jnp.sum(weights, axis=2, keepdims=True)
    return row_best, row_total, block_values(weights, value_heads)


def attend_more(state, query_heads, key_heads, value_heads, query_image, key_image):
    row_best, row_total, weighted = state
    scores = block_scores(query_heads, key_heads, query_image, key_image)
    new_best = jnp.maximum(row_best, jnp.max(scores, axis=2, keepdims=True))
    rescale = jnp.exp(row_best - new_best)
    weights = jnp.exp(scores - new_best)
    row_total = row_total * rescale + jnp.sum(weights, axis=2, keepdims=True)
    weighted = weighted * rescale + block_values(weights, value_heads)
    return new_best, row_total, weighted


def image_of_groups(groups, starts, group_total):
    inside = (groups >= 0) & (groups < group_total)
    image = jnp.sum((starts[None, :] <= groups[:, None]).astype(jnp.int32), axis=1) - 1
    return jnp.where(inside, image, -1)


def route_to_owners(projected, starts, counts, image_slot, device, seq_count):
    group_rows, out_cols = projected.shape
    per_pair = group_rows // seq_count
    spread = projected.reshape(per_pair, seq_count, out_cols).transpose(1, 0, 2)
    spread = lax.all_to_all(spread, "seq", split_axis=0, concat_axis=0, tiled=True)
    held = spread.reshape(group_rows, out_cols)
    image_count = image_slot.shape[0]
    most_rows = REACH * group_rows
    per_owner = most_rows // seq_count
    image_ids = jnp.arange(image_count, dtype=jnp.int32)
    owners = jnp.arange(seq_count, dtype=jnp.int32)
    owned_image = jnp.sum(
        jnp.where(image_slot[None, :] == owners[:, None], image_ids[None, :], 0), axis=1
    )
    owner_start = starts[owned_image]
    owner_count = counts[owned_image]
    first_pos = jnp.mod(device - owner_start, seq_count)
    first_row = (owner_start + first_pos - device) // seq_count
    steps = jnp.arange(per_owner, dtype=jnp.int32)
    rows = first_row[:, None] + steps[None, :]
    valid = (first_pos[:, None] + seq_count * steps[None, :]) < owner_count[:, None]
    rows = jnp.clip(rows, 0, group_rows - 1)
    outgoing = jnp.take(held, rows.reshape(-1), axis=0).reshape(seq_count, per_owner, out_cols)
    outgoing = jnp.where(valid[:, :, None], outgoing, jnp.zeros((), outgoing.dtype))
    received = lax.all_to_all(outgoing, "seq", split_axis=0, concat_axis=0, tiled=True)
    own_image = jnp.sum(jnp.where(image_slot == device, image_ids, 0))
    own_start = starts[own_image]
    order = jnp.mod(own_start + jnp.arange(seq_count, dtype=jnp.int32), seq_count)
    placed = jnp.take(received, order, axis=0).transpose(1, 0, 2)
    return placed.reshape(most_rows, out_cols)


def shards(
    tokens,
    group_image,
    image_slot,
    attention_gain,
    query_weight,
    key_weight,
    value_weight,
    output_weight,
    feedforward_gain,
    up_weight,
    down_weight,
    merge_gain,
    merge_weight,
):
    device = lax.axis_index("seq")
    seq_count = lax.axis_size("seq")
    token_rows = tokens.shape[0]
    group_rows = group_image.shape[0]
    group_total = group_rows * seq_count
    image_count = image_slot.shape[0]
    image_ids = jnp.arange(image_count, dtype=jnp.int32)
    local_counts = jnp.sum(
        (group_image[:, None] == image_ids[None, :]).astype(jnp.int32), axis=0
    )
    every_count = lax.all_to_all(
        jnp.broadcast_to(local_counts[None, :], (seq_count, image_count)),
        "seq",
        split_axis=0,
        concat_axis=0,
        tiled=True,
    )
    counts = jnp.sum(every_count, axis=0)
    query_image = jnp.repeat(group_image, 4)
    residual = tokens.astype(jnp.float32)
    normed = full_norm(residual, attention_gain)
    head_count = query_weight.shape[1] // HD
    queries = jnp.dot(normed, query_weight, preferred_element_type=jnp.float32).astype(jnp.bfloat16)
    key_rows = jnp.dot(normed, key_weight, preferred_element_type=jnp.float32).astype(jnp.bfloat16)
    value_rows = jnp.dot(normed, value_weight, preferred_element_type=jnp.float32).astype(
        jnp.bfloat16
    )
    query_heads = queries.reshape(token_rows, head_count, HD)
    key_value = jnp.stack([key_rows, value_rows])
    counts, key_value = lax.optimization_barrier((counts, key_value))
    starts = jnp.cumsum(counts) - counts

    def images_of_block(source):
        groups = source * group_rows + jnp.arange(group_rows, dtype=jnp.int32)
        return jnp.repeat(image_of_groups(groups, starts, group_total), 4)

    near = {step: shifted(key_value, "seq", step) for step in (1, -1, 2, -2)}
    far = {
        3: shifted(near[2], "seq", 1),
        -3: shifted(near[-2], "seq", -1),
        4: shifted(near[2], "seq", 2),
        -4: shifted(near[-2], "seq", -2),
    }
    arrived = {**near, **far}
    tp_count = lax.axis_size("tp")
    own_rows = token_rows // tp_count
    me = lax.axis_index("tp")
    own_keys = key_value[0].reshape(token_rows, head_count, HD)
    own_values = key_value[1].reshape(token_rows, head_count, HD)

    def attend_rows(pieces):
        rows = jnp.concatenate(
            [piece * own_rows + jnp.arange(own_rows, dtype=jnp.int32) for piece in pieces]
        )
        queries_here = jnp.take(query_heads, rows, axis=0)
        images_here = jnp.take(query_image, rows)
        state = attend_own_block(queries_here, own_keys, own_values, images_here, query_image)
        for step in (1, -1, 2, -2, 3, -3, 4, -4):
            block = arrived[step]
            key_image = images_of_block(device - step)
            if step > 0:
                needed = key_image[-1] == jnp.min(images_here)
            else:
                needed = key_image[0] == jnp.max(images_here)
            state = lax.cond(
                needed,
                lambda st, blk, kim: attend_more(
                    st,
                    queries_here,
                    blk[0].reshape(token_rows, head_count, HD),
                    blk[1].reshape(token_rows, head_count, HD),
                    images_here,
                    kim,
                ),
                lambda st, blk, kim: st,
                state,
                block,
                key_image,
            )
        row_best, row_total, weighted = state
        context = jnp.transpose(weighted / row_total, (1, 0, 2)).astype(jnp.bfloat16)
        context = context.reshape(rows.shape[0], head_count * HD)
        return jnp.dot(context, output_weight, preferred_element_type=jnp.float32)

    first = attend_rows([(me + 1) % tp_count, (me + 2) % tp_count])
    attention_sum = [
        tp_shift(first[:own_rows].astype(jnp.bfloat16), 1),
        tp_shift(first[own_rows:].astype(jnp.bfloat16), 2),
    ]
    second = attend_rows([(me + 3) % tp_count, me])
    attention_sum.append(tp_shift(second[:own_rows].astype(jnp.bfloat16), 3))
    attention_out = second[own_rows:]
    for piece in attention_sum:
        attention_out = attention_out + piece.astype(jnp.float32)
    own_residual = lax.dynamic_slice_in_dim(residual, me * own_rows, own_rows, 0)
    after_attention = own_residual + attention_out

    def feed_forward(rows):
        hidden = jax.nn.gelu(
            jnp.dot(rows, up_weight, preferred_element_type=jnp.float32), approximate=False
        ).astype(jnp.bfloat16)
        return jnp.dot(hidden, down_weight, preferred_element_type=jnp.float32)

    normed_two = full_norm(after_attention, feedforward_gain)
    visiting = [tp_shift(normed_two, steps) for steps in range(1, tp_count)]
    ff_total = feed_forward(normed_two)
    for steps, rows in zip(range(1, tp_count), visiting):
        returned = tp_shift(feed_forward(rows).astype(jnp.bfloat16), -steps)
        ff_total = ff_total + returned.astype(jnp.float32)
    after_feedforward = after_attention + ff_total
    normed_three = full_norm(after_feedforward, merge_gain)
    own_groups = normed_three.reshape(own_rows // 4, 4 * D)

    def merge(groups):
        return jnp.dot(groups, merge_weight, preferred_element_type=jnp.float32).astype(
            jnp.bfloat16
        )

    merged = [merge(own_groups)] + [
        merge(tp_shift(own_groups, steps)) for steps in range(1, tp_count)
    ]
    order = (me - jnp.arange(tp_count, dtype=jnp.int32)) % tp_count
    projected = jnp.take(jnp.stack(merged), order, axis=0).reshape(group_rows, -1)
    return route_to_owners(projected, starts, counts, image_slot, device, seq_count)[None]


def solution(mesh):
    return jax.shard_map(
        shards,
        mesh=mesh,
        in_specs=(
            P("seq", None),
            P("seq"),
            P(),
            P(),
            P(None, "tp"),
            P(None, "tp"),
            P(None, "tp"),
            P("tp", None),
            P(),
            P(None, "tp"),
            P("tp", None),
            P(),
            P(None, "tp"),
        ),
        out_specs=P("seq", None, "tp"),
        check_vma=False,
    )
```

```python
import jax
import jax.numpy as jnp
from jax import lax
from jax.sharding import PartitionSpec as P
from jax.experimental import pallas as pl
from jax.experimental.pallas import tpu as pltpu

D = 1408
HD = 88
REACH = 4


epsilon = 1e-06
masked_score = -1e30


def shifted(value, axis, steps):
    count = lax.axis_size(axis)
    initial, last = (max(0, -steps), min(count, count - steps))
    return lax.ppermute(value, axis, [(source, source + steps) for source in range(initial, last)])


def finish_norm(hidden, row_mean, square, norm_gain):
    return (
        (hidden - row_mean) * lax.rsqrt(square - row_mean * row_mean + epsilon) * norm_gain
    ).astype(jnp.bfloat16)


def full_norm(hidden, norm_gain):
    row_mean = jnp.mean(hidden, axis=1, keepdims=True)
    square = jnp.mean(hidden * hidden, axis=1, keepdims=True)
    return finish_norm(hidden, row_mean, square, norm_gain)


def tp_shift(value, steps):
    count = lax.axis_size("tp")
    return lax.ppermute(value, "tp", [(u, (u + steps) % count) for u in range(count)])


def sum_rows(partial_value):
    tp_count = lax.axis_size("tp")
    me = lax.axis_index("tp")
    rows, cols = partial_value.shape
    pieces = partial_value.astype(jnp.bfloat16).reshape(tp_count, rows // tp_count, cols)
    total = lax.dynamic_index_in_dim(pieces, me, 0, keepdims=False).astype(jnp.float32)
    for steps in range(1, tp_count):
        outgoing = lax.dynamic_index_in_dim(pieces, (me + steps) % tp_count, 0, keepdims=False)
        total = total + tp_shift(outgoing, steps).astype(jnp.float32)
    return total


def gather_rows(row_block):
    tp_count = lax.axis_size("tp")
    me = lax.axis_index("tp")
    arrived = [row_block] + [tp_shift(row_block, steps) for steps in range(1, tp_count)]
    order = (me - jnp.arange(tp_count, dtype=jnp.int32)) % tp_count
    placed = jnp.take(jnp.stack(arrived), order, axis=0)
    return placed.reshape(tp_count * row_block.shape[0], row_block.shape[1])


def block_scores(query_heads, key_heads, query_image, key_image):
    scores = jnp.einsum(
        "qhd,khd->hqk", query_heads, key_heads, preferred_element_type=jnp.float32
    ) * HD ** (-0.5)
    same_image = query_image[:, None] == key_image[None, :]
    return jnp.where(same_image[None], scores, masked_score)


def block_values(weights, value_heads):
    return jnp.einsum(
        "hqk,khd->hqd",
        weights.astype(jnp.bfloat16),
        value_heads,
        preferred_element_type=jnp.float32,
    )


def attend_own_block(query_heads, key_heads, value_heads, query_image, key_image):
    scores = block_scores(query_heads, key_heads, query_image, key_image)
    row_best = jnp.max(scores, axis=2, keepdims=True)
    weights = jnp.exp(scores - row_best)
    row_total = jnp.sum(weights, axis=2, keepdims=True)
    return row_best, row_total, block_values(weights, value_heads)


def more_kernel(q_ref, k_ref, v_ref, qi_ref, ki_ref, m_ref, l_ref, a_ref, m_out, l_out, a_out):
    same_image = qi_ref[...] == ki_ref[...]
    for head in range(m_ref.shape[0]):
        cols = slice(head * HD, (head + 1) * HD)
        scores = lax.dot_general(
            q_ref[:, cols],
            k_ref[:, cols],
            (((1,), (1,)), ((), ())),
            preferred_element_type=jnp.float32,
        ) * HD ** (-0.5)
        scores = jnp.where(same_image, scores, masked_score)
        row_best = m_ref[head]
        new_best = jnp.maximum(row_best, jnp.max(scores, axis=1, keepdims=True))
        rescale = jnp.exp(row_best - new_best)
        weights = jnp.exp(scores - new_best)
        l_out[head] = l_ref[head] * rescale + jnp.sum(weights, axis=1, keepdims=True)
        a_out[head] = a_ref[head] * rescale + jnp.dot(
            weights.astype(jnp.bfloat16), v_ref[:, cols], preferred_element_type=jnp.float32
        )
        m_out[head] = new_best


def attend_more(state, query_rows, key_rows, value_rows, query_image, key_image):
    row_best, row_total, weighted = state
    rows = query_rows.shape[0]
    keys = key_rows.shape[0]
    heads = row_best.shape[0]
    flops = 4 * heads * rows * keys * HD
    return pl.pallas_call(
        more_kernel,
        out_shape=(
            jax.ShapeDtypeStruct(row_best.shape, jnp.float32),
            jax.ShapeDtypeStruct(row_total.shape, jnp.float32),
            jax.ShapeDtypeStruct(weighted.shape, jnp.float32),
        ),
        cost_estimate=pl.CostEstimate(
            flops=flops, transcendentals=heads * rows * keys, bytes_accessed=3 * rows * 704 * 2
        ),
    )(
        query_rows,
        key_rows,
        value_rows,
        query_image.reshape(rows, 1),
        key_image.reshape(1, keys),
        row_best,
        row_total,
        weighted,
    )


def image_of_groups(groups, starts, group_total):
    inside = (groups >= 0) & (groups < group_total)
    image = jnp.sum((starts[None, :] <= groups[:, None]).astype(jnp.int32), axis=1) - 1
    return jnp.where(inside, image, -1)


def route_to_owners(projected, starts, counts, image_slot, device, seq_count):
    group_rows, out_cols = projected.shape
    per_pair = group_rows // seq_count
    spread = projected.reshape(per_pair, seq_count, out_cols).transpose(1, 0, 2)
    spread = lax.all_to_all(spread, "seq", split_axis=0, concat_axis=0, tiled=True)
    held = spread.reshape(group_rows, out_cols)
    image_count = image_slot.shape[0]
    most_rows = REACH * group_rows
    per_owner = most_rows // seq_count
    image_ids = jnp.arange(image_count, dtype=jnp.int32)
    owners = jnp.arange(seq_count, dtype=jnp.int32)
    owned_image = jnp.sum(
        jnp.where(image_slot[None, :] == owners[:, None], image_ids[None, :], 0), axis=1
    )
    owner_start = starts[owned_image]
    owner_count = counts[owned_image]
    first_pos = jnp.mod(device - owner_start, seq_count)
    first_row = (owner_start + first_pos - device) // seq_count
    steps = jnp.arange(per_owner, dtype=jnp.int32)
    rows = first_row[:, None] + steps[None, :]
    valid = (first_pos[:, None] + seq_count * steps[None, :]) < owner_count[:, None]
    rows = jnp.clip(rows, 0, group_rows - 1)
    outgoing = jnp.take(held, rows.reshape(-1), axis=0).reshape(seq_count, per_owner, out_cols)
    outgoing = jnp.where(valid[:, :, None], outgoing, jnp.zeros((), outgoing.dtype))
    received = lax.all_to_all(outgoing, "seq", split_axis=0, concat_axis=0, tiled=True)
    own_image = jnp.sum(jnp.where(image_slot == device, image_ids, 0))
    own_start = starts[own_image]
    order = jnp.mod(own_start + jnp.arange(seq_count, dtype=jnp.int32), seq_count)
    placed = jnp.take(received, order, axis=0).transpose(1, 0, 2)
    return placed.reshape(most_rows, out_cols)


def shards(
    tokens,
    group_image,
    image_slot,
    attention_gain,
    query_weight,
    key_weight,
    value_weight,
    output_weight,
    feedforward_gain,
    up_weight,
    down_weight,
    merge_gain,
    merge_weight,
):
    device = lax.axis_index("seq")
    seq_count = lax.axis_size("seq")
    token_rows = tokens.shape[0]
    group_rows = group_image.shape[0]
    group_total = group_rows * seq_count
    image_count = image_slot.shape[0]
    image_ids = jnp.arange(image_count, dtype=jnp.int32)
    local_counts = jnp.sum(
        (group_image[:, None] == image_ids[None, :]).astype(jnp.int32), axis=0
    )
    every_count = lax.all_to_all(
        jnp.broadcast_to(local_counts[None, :], (seq_count, image_count)),
        "seq",
        split_axis=0,
        concat_axis=0,
        tiled=True,
    )
    counts = jnp.sum(every_count, axis=0)
    query_image = jnp.repeat(group_image, 4)
    residual = tokens.astype(jnp.float32)
    normed = full_norm(residual, attention_gain)
    head_count = query_weight.shape[1] // HD
    queries = jnp.dot(normed, query_weight, preferred_element_type=jnp.float32).astype(jnp.bfloat16)
    key_rows = jnp.dot(normed, key_weight, preferred_element_type=jnp.float32).astype(jnp.bfloat16)
    value_rows = jnp.dot(normed, value_weight, preferred_element_type=jnp.float32).astype(
        jnp.bfloat16
    )
    query_heads = queries.reshape(token_rows, head_count, HD)
    key_value = jnp.stack([key_rows, value_rows])
    counts, key_value = lax.optimization_barrier((counts, key_value))
    starts = jnp.cumsum(counts) - counts

    def images_of_block(source):
        groups = source * group_rows + jnp.arange(group_rows, dtype=jnp.int32)
        return jnp.repeat(image_of_groups(groups, starts, group_total), 4)

    state = attend_own_block(
        query_heads,
        key_value[0].reshape(token_rows, head_count, HD),
        key_value[1].reshape(token_rows, head_count, HD),
        query_image,
        query_image,
    )
    near = {step: shifted(key_value, "seq", step) for step in (1, -1, 2, -2)}
    far = {
        3: shifted(near[2], "seq", 1),
        -3: shifted(near[-2], "seq", -1),
        4: shifted(near[2], "seq", 2),
        -4: shifted(near[-2], "seq", -2),
    }
    arrived = {**near, **far}
    for step in (1, -1, 2, -2, 3, -3, 4, -4):
        block = arrived[step]
        source = device - step
        if step > 0:
            needed = lambda k: k[-1] == query_image[0]
        else:
            needed = lambda k: k[0] == query_image[-1]
        key_image = images_of_block(source)
        state = lax.cond(
            needed(key_image),
            lambda st, blk, kim: attend_more(st, queries, blk[0], blk[1], query_image, kim),
            lambda st, blk, kim: st,
            state,
            block,
            key_image,
        )
    row_best, row_total, weighted = state
    context = jnp.transpose(weighted / row_total, (1, 0, 2))
    context = context.astype(jnp.bfloat16).reshape(token_rows, head_count * HD)
    attention_part = jnp.dot(context, output_weight, preferred_element_type=jnp.float32)
    tp_count = lax.axis_size("tp")
    own_rows = token_rows // tp_count
    own_residual = lax.dynamic_slice_in_dim(residual, lax.axis_index("tp") * own_rows, own_rows, 0)
    after_attention = own_residual + sum_rows(attention_part)
    me = lax.axis_index("tp")

    def feed_forward(rows):
        hidden = jax.nn.gelu(
            jnp.dot(rows, up_weight, preferred_element_type=jnp.float32), approximate=False
        ).astype(jnp.bfloat16)
        return jnp.dot(hidden, down_weight, preferred_element_type=jnp.float32)

    normed_two = full_norm(after_attention, feedforward_gain)
    visiting = [tp_shift(normed_two, steps) for steps in range(1, tp_count)]
    ff_total = feed_forward(normed_two)
    for steps, rows in zip(range(1, tp_count), visiting):
        returned = tp_shift(feed_forward(rows).astype(jnp.bfloat16), -steps)
        ff_total = ff_total + returned.astype(jnp.float32)
    after_feedforward = after_attention + ff_total
    normed_three = full_norm(after_feedforward, merge_gain)
    own_groups = normed_three.reshape(own_rows // 4, 4 * D)

    def merge(groups):
        return jnp.dot(groups, merge_weight, preferred_element_type=jnp.float32).astype(
            jnp.bfloat16
        )

    merged = [merge(own_groups)] + [
        merge(tp_shift(own_groups, steps)) for steps in range(1, tp_count)
    ]
    order = (me - jnp.arange(tp_count, dtype=jnp.int32)) % tp_count
    projected = jnp.take(jnp.stack(merged), order, axis=0).reshape(group_rows, -1)
    return route_to_owners(projected, starts, counts, image_slot, device, seq_count)[None]


def solution(mesh):
    return jax.shard_map(
        shards,
        mesh=mesh,
        in_specs=(
            P("seq", None),
            P("seq"),
            P(),
            P(),
            P(None, "tp"),
            P(None, "tp"),
            P(None, "tp"),
            P("tp", None),
            P(),
            P(None, "tp"),
            P("tp", None),
            P(),
            P(None, "tp"),
        ),
        out_specs=P("seq", None, "tp"),
        check_vma=False,
    )
```

```python
import jax
import jax.numpy as jnp
from jax import lax
from jax.sharding import PartitionSpec as P

D = 1408
HD = 88
REACH = 4


epsilon = 1e-06
masked_score = -1e30


def shifted(value, axis, steps):
    count = lax.axis_size(axis)
    initial, last = (max(0, -steps), min(count, count - steps))
    return lax.ppermute(value, axis, [(source, source + steps) for source in range(initial, last)])


def finish_norm(hidden, row_mean, square, norm_gain):
    return (
        (hidden - row_mean) * lax.rsqrt(square - row_mean * row_mean + epsilon) * norm_gain
    ).astype(jnp.bfloat16)


def full_norm(hidden, norm_gain):
    row_mean = jnp.mean(hidden, axis=1, keepdims=True)
    square = jnp.mean(hidden * hidden, axis=1, keepdims=True)
    return finish_norm(hidden, row_mean, square, norm_gain)


def tp_shift(value, steps):
    count = lax.axis_size("tp")
    return lax.ppermute(value, "tp", [(u, (u + steps) % count) for u in range(count)])


def sum_rows(partial_value):
    tp_count = lax.axis_size("tp")
    me = lax.axis_index("tp")
    rows, cols = partial_value.shape
    pieces = partial_value.astype(jnp.bfloat16).reshape(tp_count, rows // tp_count, cols)
    total = lax.dynamic_index_in_dim(pieces, me, 0, keepdims=False).astype(jnp.float32)
    for steps in range(1, tp_count):
        outgoing = lax.dynamic_index_in_dim(pieces, (me + steps) % tp_count, 0, keepdims=False)
        total = total + tp_shift(outgoing, steps).astype(jnp.float32)
    return total


def gather_rows(row_block):
    tp_count = lax.axis_size("tp")
    me = lax.axis_index("tp")
    arrived = [row_block] + [tp_shift(row_block, steps) for steps in range(1, tp_count)]
    order = (me - jnp.arange(tp_count, dtype=jnp.int32)) % tp_count
    placed = jnp.take(jnp.stack(arrived), order, axis=0)
    return placed.reshape(tp_count * row_block.shape[0], row_block.shape[1])


def block_scores(query_heads, key_heads, query_image, key_image):
    scores = jnp.einsum(
        "qhd,khd->hqk", query_heads, key_heads, preferred_element_type=jnp.float32
    ) * HD ** (-0.5)
    same_image = query_image[:, None] == key_image[None, :]
    return jnp.where(same_image[None], scores, masked_score)


def block_values(weights, value_heads):
    return jnp.einsum(
        "hqk,khd->hqd",
        weights.astype(jnp.bfloat16),
        value_heads,
        preferred_element_type=jnp.float32,
    )


def attend_own_block(query_heads, key_heads, value_heads, query_image, key_image):
    scores = block_scores(query_heads, key_heads, query_image, key_image)
    row_best = jnp.max(scores, axis=2, keepdims=True)
    weights = jnp.exp(scores - row_best)
    row_total = jnp.sum(weights, axis=2, keepdims=True)
    return row_best, row_total, block_values(weights, value_heads)


def attend_more(state, query_heads, key_heads, value_heads, query_image, key_image):
    row_best, row_total, weighted = state
    scores = block_scores(query_heads, key_heads, query_image, key_image)
    new_best = jnp.maximum(row_best, jnp.max(scores, axis=2, keepdims=True))
    rescale = jnp.exp(row_best - new_best)
    weights = jnp.exp(scores - new_best)
    row_total = row_total * rescale + jnp.sum(weights, axis=2, keepdims=True)
    weighted = weighted * rescale + block_values(weights, value_heads)
    return new_best, row_total, weighted


def image_of_groups(groups, starts, group_total):
    inside = (groups >= 0) & (groups < group_total)
    image = jnp.sum((starts[None, :] <= groups[:, None]).astype(jnp.int32), axis=1) - 1
    return jnp.where(inside, image, -1)


def route_to_owners(projected, starts, counts, image_slot, device, seq_count):
    group_rows, out_cols = projected.shape
    per_pair = group_rows // seq_count
    spread = projected.reshape(per_pair, seq_count, out_cols).transpose(1, 0, 2)
    spread = lax.all_to_all(spread, "seq", split_axis=0, concat_axis=0, tiled=True)
    held = spread.reshape(group_rows, out_cols)
    image_count = image_slot.shape[0]
    most_rows = REACH * group_rows
    per_owner = most_rows // seq_count
    image_ids = jnp.arange(image_count, dtype=jnp.int32)
    owners = jnp.arange(seq_count, dtype=jnp.int32)
    owned_image = jnp.sum(
        jnp.where(image_slot[None, :] == owners[:, None], image_ids[None, :], 0), axis=1
    )
    owner_start = starts[owned_image]
    owner_count = counts[owned_image]
    first_pos = jnp.mod(device - owner_start, seq_count)
    first_row = (owner_start + first_pos - device) // seq_count
    steps = jnp.arange(per_owner, dtype=jnp.int32)
    rows = first_row[:, None] + steps[None, :]
    valid = (first_pos[:, None] + seq_count * steps[None, :]) < owner_count[:, None]
    rows = jnp.clip(rows, 0, group_rows - 1)
    outgoing = jnp.take(held, rows.reshape(-1), axis=0).reshape(seq_count, per_owner, out_cols)
    outgoing = jnp.where(valid[:, :, None], outgoing, jnp.zeros((), outgoing.dtype))
    received = lax.all_to_all(outgoing, "seq", split_axis=0, concat_axis=0, tiled=True)
    own_image = jnp.sum(jnp.where(image_slot == device, image_ids, 0))
    own_start = starts[own_image]
    order = jnp.mod(own_start + jnp.arange(seq_count, dtype=jnp.int32), seq_count)
    placed = jnp.take(received, order, axis=0).transpose(1, 0, 2)
    return placed.reshape(most_rows, out_cols)


def shards(
    tokens,
    group_image,
    image_slot,
    attention_gain,
    query_weight,
    key_weight,
    value_weight,
    output_weight,
    feedforward_gain,
    up_weight,
    down_weight,
    merge_gain,
    merge_weight,
):
    device = lax.axis_index("seq")
    seq_count = lax.axis_size("seq")
    token_rows = tokens.shape[0]
    group_rows = group_image.shape[0]
    group_total = group_rows * seq_count
    image_count = image_slot.shape[0]
    image_ids = jnp.arange(image_count, dtype=jnp.int32)
    local_counts = jnp.sum(
        (group_image[:, None] == image_ids[None, :]).astype(jnp.int32), axis=0
    )
    every_count = lax.all_to_all(
        jnp.broadcast_to(local_counts[None, :], (seq_count, image_count)),
        "seq",
        split_axis=0,
        concat_axis=0,
        tiled=True,
    )
    counts = jnp.sum(every_count, axis=0)
    query_image = jnp.repeat(group_image, 4)
    residual = tokens.astype(jnp.float32)
    normed = full_norm(residual, attention_gain)
    head_count = query_weight.shape[1] // HD
    queries = jnp.dot(normed, query_weight, preferred_element_type=jnp.float32).astype(jnp.bfloat16)
    key_rows = jnp.dot(normed, key_weight, preferred_element_type=jnp.float32).astype(jnp.bfloat16)
    value_rows = jnp.dot(normed, value_weight, preferred_element_type=jnp.float32).astype(
        jnp.bfloat16
    )
    query_heads = queries.reshape(token_rows, head_count, HD)
    key_value = jnp.stack([key_rows, value_rows])
    starts = jnp.cumsum(counts) - counts

    def images_of_block(source):
        groups = source * group_rows + jnp.arange(group_rows, dtype=jnp.int32)
        return jnp.repeat(image_of_groups(groups, starts, group_total), 4)

    state = attend_own_block(
        query_heads,
        key_value[0].reshape(token_rows, head_count, HD),
        key_value[1].reshape(token_rows, head_count, HD),
        query_image,
        query_image,
    )
    near = {step: shifted(key_value, "seq", step) for step in (1, -1, 2, -2)}
    far = {
        3: shifted(near[2], "seq", 1),
        -3: shifted(near[-2], "seq", -1),
        4: shifted(near[2], "seq", 2),
        -4: shifted(near[-2], "seq", -2),
    }
    arrived = {**near, **far}
    for step in (1, -1, 2, -2, 3, -3, 4, -4):
        block = arrived[step]
        source = device - step
        if step > 0:
            needed = lambda k: k[-1] == query_image[0]
        else:
            needed = lambda k: k[0] == query_image[-1]
        key_image = images_of_block(source)
        state = lax.cond(
            needed(key_image),
            lambda st, blk, kim: attend_more(
                st,
                query_heads,
                blk[0].reshape(token_rows, head_count, HD),
                blk[1].reshape(token_rows, head_count, HD),
                query_image,
                kim,
            ),
            lambda st, blk, kim: st,
            state,
            block,
            key_image,
        )
    row_best, row_total, weighted = state
    context = jnp.transpose(weighted / row_total, (1, 0, 2))
    context = context.astype(jnp.bfloat16).reshape(token_rows, head_count * HD)
    attention_part = jnp.dot(context, output_weight, preferred_element_type=jnp.float32)
    tp_count = lax.axis_size("tp")
    own_rows = token_rows // tp_count
    own_residual = lax.dynamic_slice_in_dim(residual, lax.axis_index("tp") * own_rows, own_rows, 0)
    after_attention = own_residual + sum_rows(attention_part)
    me = lax.axis_index("tp")

    def feed_forward(rows):
        hidden = jax.nn.gelu(
            jnp.dot(rows, up_weight, preferred_element_type=jnp.float32), approximate=False
        ).astype(jnp.bfloat16)
        return jnp.dot(hidden, down_weight, preferred_element_type=jnp.float32)

    normed_two = full_norm(after_attention, feedforward_gain)
    visiting = [tp_shift(normed_two, steps) for steps in range(1, tp_count)]
    ff_total = feed_forward(normed_two)
    for steps, rows in zip(range(1, tp_count), visiting):
        returned = tp_shift(feed_forward(rows).astype(jnp.bfloat16), -steps)
        ff_total = ff_total + returned.astype(jnp.float32)
    after_feedforward = after_attention + ff_total
    normed_three = full_norm(after_feedforward, merge_gain)
    own_groups = normed_three.reshape(own_rows // 4, 4 * D)

    def merge(groups):
        return jnp.dot(groups, merge_weight, preferred_element_type=jnp.float32).astype(
            jnp.bfloat16
        )

    merged = [merge(own_groups)] + [
        merge(tp_shift(own_groups, steps)) for steps in range(1, tp_count)
    ]
    order = (me - jnp.arange(tp_count, dtype=jnp.int32)) % tp_count
    projected = jnp.take(jnp.stack(merged), order, axis=0).reshape(group_rows, -1)
    return route_to_owners(projected, starts, counts, image_slot, device, seq_count)[None]


def solution(mesh):
    return jax.shard_map(
        shards,
        mesh=mesh,
        in_specs=(
            P("seq", None),
            P("seq"),
            P(),
            P(),
            P(None, "tp"),
            P(None, "tp"),
            P(None, "tp"),
            P("tp", None),
            P(),
            P(None, "tp"),
            P("tp", None),
            P(),
            P(None, "tp"),
        ),
        out_specs=P("seq", None, "tp"),
        check_vma=False,
    )
```

```python
import jax
import jax.numpy as jnp
from jax import lax
from jax.sharding import PartitionSpec as P

D = 1408
HD = 88
REACH = 4


epsilon = 1e-06
masked_score = -1e30


def shifted(value, axis, steps):
    count = lax.axis_size(axis)
    initial, last = (max(0, -steps), min(count, count - steps))
    return lax.ppermute(value, axis, [(source, source + steps) for source in range(initial, last)])


def finish_norm(hidden, row_mean, square, norm_gain):
    return (
        (hidden - row_mean) * lax.rsqrt(square - row_mean * row_mean + epsilon) * norm_gain
    ).astype(jnp.bfloat16)


def full_norm(hidden, norm_gain):
    row_mean = jnp.mean(hidden, axis=1, keepdims=True)
    square = jnp.mean(hidden * hidden, axis=1, keepdims=True)
    return finish_norm(hidden, row_mean, square, norm_gain)


def tp_shift(value, steps):
    count = lax.axis_size("tp")
    return lax.ppermute(value, "tp", [(u, (u + steps) % count) for u in range(count)])


def sum_rows(partial_value):
    tp_count = lax.axis_size("tp")
    me = lax.axis_index("tp")
    rows, cols = partial_value.shape
    pieces = partial_value.astype(jnp.bfloat16).reshape(tp_count, rows // tp_count, cols)
    total = lax.dynamic_index_in_dim(pieces, me, 0, keepdims=False).astype(jnp.float32)
    for steps in range(1, tp_count):
        outgoing = lax.dynamic_index_in_dim(pieces, (me + steps) % tp_count, 0, keepdims=False)
        total = total + tp_shift(outgoing, steps).astype(jnp.float32)
    return total


def gather_rows(row_block):
    tp_count = lax.axis_size("tp")
    me = lax.axis_index("tp")
    arrived = [row_block] + [tp_shift(row_block, steps) for steps in range(1, tp_count)]
    order = (me - jnp.arange(tp_count, dtype=jnp.int32)) % tp_count
    placed = jnp.take(jnp.stack(arrived), order, axis=0)
    return placed.reshape(tp_count * row_block.shape[0], row_block.shape[1])


def block_scores(query_heads, key_heads, query_image, key_image):
    scores = jnp.einsum(
        "qhd,khd->hqk", query_heads, key_heads, preferred_element_type=jnp.float32
    ) * HD ** (-0.5)
    same_image = query_image[:, None] == key_image[None, :]
    return jnp.where(same_image[None], scores, masked_score)


def block_values(weights, value_heads):
    return jnp.einsum(
        "hqk,khd->hqd",
        weights.astype(jnp.bfloat16),
        value_heads,
        preferred_element_type=jnp.float32,
    )


def attend_own_block(query_heads, key_heads, value_heads, query_image, key_image):
    scores = block_scores(query_heads, key_heads, query_image, key_image)
    row_best = jnp.max(scores, axis=2, keepdims=True)
    weights = jnp.exp(scores - row_best)
    row_total = jnp.sum(weights, axis=2, keepdims=True)
    return row_best, row_total, block_values(weights, value_heads)


def attend_more(state, query_heads, key_heads, value_heads, query_image, key_image):
    row_best, row_total, weighted = state
    scores = block_scores(query_heads, key_heads, query_image, key_image)
    new_best = jnp.maximum(row_best, jnp.max(scores, axis=2, keepdims=True))
    rescale = jnp.exp(row_best - new_best)
    weights = jnp.exp(scores - new_best)
    row_total = row_total * rescale + jnp.sum(weights, axis=2, keepdims=True)
    weighted = weighted * rescale + block_values(weights, value_heads)
    return new_best, row_total, weighted


def image_of_groups(groups, starts, group_total):
    inside = (groups >= 0) & (groups < group_total)
    image = jnp.sum((starts[None, :] <= groups[:, None]).astype(jnp.int32), axis=1) - 1
    return jnp.where(inside, image, -1)


def route_to_owners(projected, starts, counts, image_slot, device, seq_count):
    group_rows, out_cols = projected.shape
    per_pair = group_rows // seq_count
    spread = projected.reshape(per_pair, seq_count, out_cols).transpose(1, 0, 2)
    spread = lax.all_to_all(spread, "seq", split_axis=0, concat_axis=0, tiled=True)
    held = spread.reshape(group_rows, out_cols)
    image_count = image_slot.shape[0]
    most_rows = REACH * group_rows
    per_owner = most_rows // seq_count
    image_ids = jnp.arange(image_count, dtype=jnp.int32)
    owners = jnp.arange(seq_count, dtype=jnp.int32)
    owned_image = jnp.sum(
        jnp.where(image_slot[None, :] == owners[:, None], image_ids[None, :], 0), axis=1
    )
    owner_start = starts[owned_image]
    owner_count = counts[owned_image]
    first_pos = jnp.mod(device - owner_start, seq_count)
    first_row = (owner_start + first_pos - device) // seq_count
    steps = jnp.arange(per_owner, dtype=jnp.int32)
    rows = first_row[:, None] + steps[None, :]
    valid = (first_pos[:, None] + seq_count * steps[None, :]) < owner_count[:, None]
    rows = jnp.clip(rows, 0, group_rows - 1)
    outgoing = jnp.take(held, rows.reshape(-1), axis=0).reshape(seq_count, per_owner, out_cols)
    outgoing = jnp.where(valid[:, :, None], outgoing, jnp.zeros((), outgoing.dtype))
    received = lax.all_to_all(outgoing, "seq", split_axis=0, concat_axis=0, tiled=True)
    own_image = jnp.sum(jnp.where(image_slot == device, image_ids, 0))
    own_start = starts[own_image]
    order = jnp.mod(own_start + jnp.arange(seq_count, dtype=jnp.int32), seq_count)
    placed = jnp.take(received, order, axis=0).transpose(1, 0, 2)
    return placed.reshape(most_rows, out_cols)


def shards(
    tokens,
    group_image,
    image_slot,
    attention_gain,
    query_weight,
    key_weight,
    value_weight,
    output_weight,
    feedforward_gain,
    up_weight,
    down_weight,
    merge_gain,
    merge_weight,
):
    device = lax.axis_index("seq")
    seq_count = lax.axis_size("seq")
    token_rows = tokens.shape[0]
    group_rows = group_image.shape[0]
    group_total = group_rows * seq_count
    image_count = image_slot.shape[0]
    image_ids = jnp.arange(image_count, dtype=jnp.int32)
    local_counts = jnp.sum(
        (group_image[:, None] == image_ids[None, :]).astype(jnp.int32), axis=0
    )
    every_count = lax.all_to_all(
        jnp.broadcast_to(local_counts[None, :], (seq_count, image_count)),
        "seq",
        split_axis=0,
        concat_axis=0,
        tiled=True,
    )
    counts = jnp.sum(every_count, axis=0)
    query_image = jnp.repeat(group_image, 4)
    residual = tokens.astype(jnp.float32)
    normed = full_norm(residual, attention_gain)
    head_count = query_weight.shape[1] // HD
    queries = jnp.dot(normed, query_weight, preferred_element_type=jnp.float32).astype(jnp.bfloat16)
    key_rows = jnp.dot(normed, key_weight, preferred_element_type=jnp.float32).astype(jnp.bfloat16)
    value_rows = jnp.dot(normed, value_weight, preferred_element_type=jnp.float32).astype(
        jnp.bfloat16
    )
    query_heads = queries.reshape(token_rows, head_count, HD)
    key_value = jnp.stack([key_rows, value_rows])
    counts, key_value = lax.optimization_barrier((counts, key_value))
    starts = jnp.cumsum(counts) - counts

    def images_of_block(source):
        groups = source * group_rows + jnp.arange(group_rows, dtype=jnp.int32)
        return jnp.repeat(image_of_groups(groups, starts, group_total), 4)

    state = attend_own_block(
        query_heads,
        key_value[0].reshape(token_rows, head_count, HD),
        key_value[1].reshape(token_rows, head_count, HD),
        query_image,
        query_image,
    )
    near = {step: shifted(key_value, "seq", step) for step in (1, -1, 2, -2)}
    far = {
        3: shifted(near[2], "seq", 1),
        -3: shifted(near[-2], "seq", -1),
        4: shifted(near[2], "seq", 2),
        -4: shifted(near[-2], "seq", -2),
    }
    arrived = {**near, **far}
    for step in (1, -1, 2, -2, 3, -3, 4, -4):
        block = arrived[step]
        source = device - step
        if step > 0:
            needed = lambda k: k[-1] == query_image[0]
        else:
            needed = lambda k: k[0] == query_image[-1]
        key_image = images_of_block(source)
        state = lax.cond(
            needed(key_image),
            lambda st, blk, kim: attend_more(
                st,
                query_heads,
                blk[0].reshape(token_rows, head_count, HD),
                blk[1].reshape(token_rows, head_count, HD),
                query_image,
                kim,
            ),
            lambda st, blk, kim: st,
            state,
            block,
            key_image,
        )
    row_best, row_total, weighted = state
    context = jnp.transpose(weighted / row_total, (1, 0, 2))
    context = context.astype(jnp.bfloat16).reshape(token_rows, head_count * HD)
    attention_part = jnp.dot(context, output_weight, preferred_element_type=jnp.float32)
    tp_count = lax.axis_size("tp")
    own_rows = token_rows // tp_count
    own_residual = lax.dynamic_slice_in_dim(residual, lax.axis_index("tp") * own_rows, own_rows, 0)
    after_attention = own_residual + sum_rows(attention_part)
    me = lax.axis_index("tp")

    def feed_forward(rows):
        hidden = jax.nn.gelu(
            jnp.dot(rows, up_weight, preferred_element_type=jnp.float32), approximate=False
        ).astype(jnp.bfloat16)
        return jnp.dot(hidden, down_weight, preferred_element_type=jnp.float32)

    normed_two = full_norm(after_attention, feedforward_gain)
    distances = sorted(range(1, tp_count), key=lambda k: (min(k, tp_count - k), k))
    visiting = [tp_shift(normed_two, steps) for steps in distances]
    ff_total = feed_forward(normed_two)
    for steps, rows in zip(distances, visiting):
        returned = tp_shift(feed_forward(rows).astype(jnp.bfloat16), -steps)
        ff_total = ff_total + returned.astype(jnp.float32)
    after_feedforward = after_attention + ff_total
    normed_three = full_norm(after_feedforward, merge_gain)
    own_groups = normed_three.reshape(own_rows // 4, 4 * D)

    def merge(groups):
        return jnp.dot(groups, merge_weight, preferred_element_type=jnp.float32).astype(
            jnp.bfloat16
        )

    merged = [merge(own_groups)] + [
        merge(tp_shift(own_groups, steps)) for steps in range(1, tp_count)
    ]
    order = (me - jnp.arange(tp_count, dtype=jnp.int32)) % tp_count
    projected = jnp.take(jnp.stack(merged), order, axis=0).reshape(group_rows, -1)
    return route_to_owners(projected, starts, counts, image_slot, device, seq_count)[None]


def solution(mesh):
    return jax.shard_map(
        shards,
        mesh=mesh,
        in_specs=(
            P("seq", None),
            P("seq"),
            P(),
            P(),
            P(None, "tp"),
            P(None, "tp"),
            P(None, "tp"),
            P("tp", None),
            P(),
            P(None, "tp"),
            P("tp", None),
            P(),
            P(None, "tp"),
        ),
        out_specs=P("seq", None, "tp"),
        check_vma=False,
    )
```

```python
import jax
import jax.numpy as jnp
from jax import lax
from jax.sharding import PartitionSpec as P

D = 1408
HD = 88
REACH = 4


epsilon = 1e-06
masked_score = -1e30


def shifted(value, axis, steps):
    count = lax.axis_size(axis)
    initial, last = (max(0, -steps), min(count, count - steps))
    return lax.ppermute(value, axis, [(source, source + steps) for source in range(initial, last)])


def finish_norm(hidden, row_mean, square, norm_gain):
    return (
        (hidden - row_mean) * lax.rsqrt(square - row_mean * row_mean + epsilon) * norm_gain
    ).astype(jnp.bfloat16)


def full_norm(hidden, norm_gain):
    row_mean = jnp.mean(hidden, axis=1, keepdims=True)
    square = jnp.mean(hidden * hidden, axis=1, keepdims=True)
    return finish_norm(hidden, row_mean, square, norm_gain)


def tp_shift(value, steps):
    count = lax.axis_size("tp")
    return lax.ppermute(value, "tp", [(u, (u + steps) % count) for u in range(count)])


def sum_rows(partial_value):
    tp_count = lax.axis_size("tp")
    me = lax.axis_index("tp")
    rows, cols = partial_value.shape
    pieces = partial_value.astype(jnp.bfloat16).reshape(tp_count, rows // tp_count, cols)
    total = lax.dynamic_index_in_dim(pieces, me, 0, keepdims=False).astype(jnp.float32)
    for steps in range(1, tp_count):
        outgoing = lax.dynamic_index_in_dim(pieces, (me + steps) % tp_count, 0, keepdims=False)
        total = total + tp_shift(outgoing, steps).astype(jnp.float32)
    return total


def gather_rows(row_block):
    tp_count = lax.axis_size("tp")
    me = lax.axis_index("tp")
    arrived = [row_block] + [tp_shift(row_block, steps) for steps in range(1, tp_count)]
    order = (me - jnp.arange(tp_count, dtype=jnp.int32)) % tp_count
    placed = jnp.take(jnp.stack(arrived), order, axis=0)
    return placed.reshape(tp_count * row_block.shape[0], row_block.shape[1])


def block_scores(query_heads, key_heads, query_image, key_image):
    scores = jnp.einsum(
        "qhd,khd->hqk", query_heads, key_heads, preferred_element_type=jnp.float32
    ) * HD ** (-0.5)
    same_image = query_image[:, None] == key_image[None, :]
    return jnp.where(same_image[None], scores, masked_score)


def block_values(weights, value_heads):
    return jnp.einsum(
        "hqk,khd->hqd",
        weights.astype(jnp.bfloat16),
        value_heads,
        preferred_element_type=jnp.float32,
    )


def attend_own_block(query_heads, key_heads, value_heads, query_image, key_image):
    scores = block_scores(query_heads, key_heads, query_image, key_image)
    row_best = jnp.max(scores, axis=2, keepdims=True)
    weights = jnp.exp(scores - row_best)
    row_total = jnp.sum(weights, axis=2, keepdims=True)
    return row_best, row_total, block_values(weights, value_heads)


def attend_more(state, query_heads, key_heads, value_heads, query_image, key_image):
    row_best, row_total, weighted = state
    scores = block_scores(query_heads, key_heads, query_image, key_image)
    new_best = jnp.maximum(row_best, jnp.max(scores, axis=2, keepdims=True))
    rescale = jnp.exp(row_best - new_best)
    weights = jnp.exp(scores - new_best)
    row_total = row_total * rescale + jnp.sum(weights, axis=2, keepdims=True)
    weighted = weighted * rescale + block_values(weights, value_heads)
    return new_best, row_total, weighted


def image_of_groups(groups, starts, group_total):
    inside = (groups >= 0) & (groups < group_total)
    image = jnp.sum((starts[None, :] <= groups[:, None]).astype(jnp.int32), axis=1) - 1
    return jnp.where(inside, image, -1)


def route_to_owners(projected, starts, counts, image_slot, device, seq_count):
    group_rows, out_cols = projected.shape
    per_pair = group_rows // seq_count
    spread = projected.reshape(per_pair, seq_count, out_cols).transpose(1, 0, 2)
    spread = lax.all_to_all(spread, "seq", split_axis=0, concat_axis=0, tiled=True)
    held = spread.reshape(group_rows, out_cols)
    image_count = image_slot.shape[0]
    most_rows = REACH * group_rows
    per_owner = most_rows // seq_count
    image_ids = jnp.arange(image_count, dtype=jnp.int32)
    owners = jnp.arange(seq_count, dtype=jnp.int32)
    owned_image = jnp.sum(
        jnp.where(image_slot[None, :] == owners[:, None], image_ids[None, :], 0), axis=1
    )
    owner_start = starts[owned_image]
    owner_count = counts[owned_image]
    first_pos = jnp.mod(device - owner_start, seq_count)
    first_row = (owner_start + first_pos - device) // seq_count
    steps = jnp.arange(per_owner, dtype=jnp.int32)
    rows = first_row[:, None] + steps[None, :]
    valid = (first_pos[:, None] + seq_count * steps[None, :]) < owner_count[:, None]
    rows = jnp.clip(rows, 0, group_rows - 1)
    outgoing = jnp.take(held, rows.reshape(-1), axis=0).reshape(seq_count, per_owner, out_cols)
    outgoing = jnp.where(valid[:, :, None], outgoing, jnp.zeros((), outgoing.dtype))
    received = lax.all_to_all(outgoing, "seq", split_axis=0, concat_axis=0, tiled=True)
    own_image = jnp.sum(jnp.where(image_slot == device, image_ids, 0))
    own_start = starts[own_image]
    order = jnp.mod(own_start + jnp.arange(seq_count, dtype=jnp.int32), seq_count)
    placed = jnp.take(received, order, axis=0).transpose(1, 0, 2)
    return placed.reshape(most_rows, out_cols)


def shards(
    tokens,
    group_image,
    image_slot,
    attention_gain,
    query_weight,
    key_weight,
    value_weight,
    output_weight,
    feedforward_gain,
    up_weight,
    down_weight,
    merge_gain,
    merge_weight,
):
    device = lax.axis_index("seq")
    seq_count = lax.axis_size("seq")
    token_rows = tokens.shape[0]
    group_rows = group_image.shape[0]
    group_total = group_rows * seq_count
    image_count = image_slot.shape[0]
    image_ids = jnp.arange(image_count, dtype=jnp.int32)
    local_counts = jnp.sum(
        (group_image[:, None] == image_ids[None, :]).astype(jnp.int32), axis=0
    )
    query_image = jnp.repeat(group_image, 4)
    residual = tokens.astype(jnp.float32)
    normed = full_norm(residual, attention_gain)
    head_count = query_weight.shape[1] // HD
    queries = jnp.dot(normed, query_weight, preferred_element_type=jnp.float32).astype(jnp.bfloat16)
    key_rows = jnp.dot(normed, key_weight, preferred_element_type=jnp.float32).astype(jnp.bfloat16)
    value_rows = jnp.dot(normed, value_weight, preferred_element_type=jnp.float32).astype(
        jnp.bfloat16
    )
    query_heads = queries.reshape(token_rows, head_count, HD)
    key_value = jnp.stack([key_rows, value_rows])
    projected_yet = (key_value[0, 0, 0] != key_value[0, 0, 0]).astype(jnp.int32)
    every_count = lax.all_to_all(
        jnp.broadcast_to(local_counts[None, :] + projected_yet, (seq_count, image_count)),
        "seq",
        split_axis=0,
        concat_axis=0,
        tiled=True,
    )
    counts = jnp.sum(every_count, axis=0)
    counts, key_value = lax.optimization_barrier((counts, key_value))
    starts = jnp.cumsum(counts) - counts

    def images_of_block(source):
        groups = source * group_rows + jnp.arange(group_rows, dtype=jnp.int32)
        return jnp.repeat(image_of_groups(groups, starts, group_total), 4)

    state = attend_own_block(
        query_heads,
        key_value[0].reshape(token_rows, head_count, HD),
        key_value[1].reshape(token_rows, head_count, HD),
        query_image,
        query_image,
    )
    near = {step: shifted(key_value, "seq", step) for step in (1, -1, 2, -2)}
    far = {
        3: shifted(near[2], "seq", 1),
        -3: shifted(near[-2], "seq", -1),
        4: shifted(near[2], "seq", 2),
        -4: shifted(near[-2], "seq", -2),
    }
    arrived = {**near, **far}
    for step in (1, -1, 2, -2, 3, -3, 4, -4):
        block = arrived[step]
        source = device - step
        if step > 0:
            needed = lambda k: k[-1] == query_image[0]
        else:
            needed = lambda k: k[0] == query_image[-1]
        key_image = images_of_block(source)
        state = lax.cond(
            needed(key_image),
            lambda st, blk, kim: attend_more(
                st,
                query_heads,
                blk[0].reshape(token_rows, head_count, HD),
                blk[1].reshape(token_rows, head_count, HD),
                query_image,
                kim,
            ),
            lambda st, blk, kim: st,
            state,
            block,
            key_image,
        )
    row_best, row_total, weighted = state
    context = jnp.transpose(weighted / row_total, (1, 0, 2))
    context = context.astype(jnp.bfloat16).reshape(token_rows, head_count * HD)
    attention_part = jnp.dot(context, output_weight, preferred_element_type=jnp.float32)
    tp_count = lax.axis_size("tp")
    own_rows = token_rows // tp_count
    own_residual = lax.dynamic_slice_in_dim(residual, lax.axis_index("tp") * own_rows, own_rows, 0)
    after_attention = own_residual + sum_rows(attention_part)
    me = lax.axis_index("tp")

    def feed_forward(rows):
        hidden = jax.nn.gelu(
            jnp.dot(rows, up_weight, preferred_element_type=jnp.float32), approximate=False
        ).astype(jnp.bfloat16)
        return jnp.dot(hidden, down_weight, preferred_element_type=jnp.float32)

    normed_two = full_norm(after_attention, feedforward_gain)
    visiting = [tp_shift(normed_two, steps) for steps in range(1, tp_count)]
    ff_total = feed_forward(normed_two)
    for steps, rows in zip(range(1, tp_count), visiting):
        returned = tp_shift(feed_forward(rows).astype(jnp.bfloat16), -steps)
        ff_total = ff_total + returned.astype(jnp.float32)
    after_feedforward = after_attention + ff_total
    normed_three = full_norm(after_feedforward, merge_gain)
    own_groups = normed_three.reshape(own_rows // 4, 4 * D)

    def merge(groups):
        return jnp.dot(groups, merge_weight, preferred_element_type=jnp.float32).astype(
            jnp.bfloat16
        )

    merged = [merge(own_groups)] + [
        merge(tp_shift(own_groups, steps)) for steps in range(1, tp_count)
    ]
    order = (me - jnp.arange(tp_count, dtype=jnp.int32)) % tp_count
    projected = jnp.take(jnp.stack(merged), order, axis=0).reshape(group_rows, -1)
    return route_to_owners(projected, starts, counts, image_slot, device, seq_count)[None]


def solution(mesh):
    return jax.shard_map(
        shards,
        mesh=mesh,
        in_specs=(
            P("seq", None),
            P("seq"),
            P(),
            P(),
            P(None, "tp"),
            P(None, "tp"),
            P(None, "tp"),
            P("tp", None),
            P(),
            P(None, "tp"),
            P("tp", None),
            P(),
            P(None, "tp"),
        ),
        out_specs=P("seq", None, "tp"),
        check_vma=False,
    )
```

```python
import jax
import jax.numpy as jnp
from jax import lax
from jax.sharding import PartitionSpec as P

D = 1408
HD = 88
REACH = 4


epsilon = 1e-06
masked_score = -1e30


def shifted(value, axis, steps):
    count = lax.axis_size(axis)
    initial, last = (max(0, -steps), min(count, count - steps))
    return lax.ppermute(value, axis, [(source, source + steps) for source in range(initial, last)])


def finish_norm(hidden, row_mean, square, norm_gain):
    return (
        (hidden - row_mean) * lax.rsqrt(square - row_mean * row_mean + epsilon) * norm_gain
    ).astype(jnp.bfloat16)


def full_norm(hidden, norm_gain):
    row_mean = jnp.mean(hidden, axis=1, keepdims=True)
    square = jnp.mean(hidden * hidden, axis=1, keepdims=True)
    return finish_norm(hidden, row_mean, square, norm_gain)


def tp_shift(value, steps):
    count = lax.axis_size("tp")
    return lax.ppermute(value, "tp", [(u, (u + steps) % count) for u in range(count)])


def sum_rows(partial_value):
    tp_count = lax.axis_size("tp")
    me = lax.axis_index("tp")
    rows, cols = partial_value.shape
    pieces = partial_value.astype(jnp.bfloat16).reshape(tp_count, rows // tp_count, cols)
    total = lax.dynamic_index_in_dim(pieces, me, 0, keepdims=False).astype(jnp.float32)
    for steps in range(1, tp_count):
        outgoing = lax.dynamic_index_in_dim(pieces, (me + steps) % tp_count, 0, keepdims=False)
        total = total + tp_shift(outgoing, steps).astype(jnp.float32)
    return total


def gather_rows(row_block):
    tp_count = lax.axis_size("tp")
    me = lax.axis_index("tp")
    arrived = [row_block] + [tp_shift(row_block, steps) for steps in range(1, tp_count)]
    order = (me - jnp.arange(tp_count, dtype=jnp.int32)) % tp_count
    placed = jnp.take(jnp.stack(arrived), order, axis=0)
    return placed.reshape(tp_count * row_block.shape[0], row_block.shape[1])


def block_scores(query_heads, key_heads, query_image, key_image):
    scores = jnp.einsum(
        "qhd,khd->hqk", query_heads, key_heads, preferred_element_type=jnp.float32
    ) * HD ** (-0.5)
    same_image = query_image[:, None] == key_image[None, :]
    return jnp.where(same_image[None], scores, masked_score)


def block_values(weights, value_heads):
    return jnp.einsum(
        "hqk,khd->hqd",
        weights.astype(jnp.bfloat16),
        value_heads,
        preferred_element_type=jnp.float32,
    )


def attend_own_block(query_heads, key_heads, value_heads, query_image, key_image):
    scores = block_scores(query_heads, key_heads, query_image, key_image)
    row_best = jnp.max(scores, axis=2, keepdims=True)
    weights = jnp.exp(scores - row_best)
    row_total = jnp.sum(weights, axis=2, keepdims=True)
    return row_best, row_total, block_values(weights, value_heads)


def attend_more(state, query_heads, key_heads, value_heads, query_image, key_image):
    row_best, row_total, weighted = state
    scores = block_scores(query_heads, key_heads, query_image, key_image)
    new_best = jnp.maximum(row_best, jnp.max(scores, axis=2, keepdims=True))
    rescale = jnp.exp(row_best - new_best)
    weights = jnp.exp(scores - new_best)
    row_total = row_total * rescale + jnp.sum(weights, axis=2, keepdims=True)
    weighted = weighted * rescale + block_values(weights, value_heads)
    return new_best, row_total, weighted


def image_of_groups(groups, starts, group_total):
    inside = (groups >= 0) & (groups < group_total)
    image = jnp.sum((starts[None, :] <= groups[:, None]).astype(jnp.int32), axis=1) - 1
    return jnp.where(inside, image, -1)


def route_to_owners(projected, starts, counts, image_slot, device, seq_count):
    group_rows, out_cols = projected.shape
    per_pair = group_rows // seq_count
    spread = projected.reshape(per_pair, seq_count, out_cols).transpose(1, 0, 2)
    spread = lax.all_to_all(spread, "seq", split_axis=0, concat_axis=0, tiled=True)
    held = spread.reshape(group_rows, out_cols)
    image_count = image_slot.shape[0]
    most_rows = REACH * group_rows
    per_owner = most_rows // seq_count
    image_ids = jnp.arange(image_count, dtype=jnp.int32)
    owners = jnp.arange(seq_count, dtype=jnp.int32)
    owned_image = jnp.sum(
        jnp.where(image_slot[None, :] == owners[:, None], image_ids[None, :], 0), axis=1
    )
    owner_start = starts[owned_image]
    owner_count = counts[owned_image]
    first_pos = jnp.mod(device - owner_start, seq_count)
    first_row = (owner_start + first_pos - device) // seq_count
    steps = jnp.arange(per_owner, dtype=jnp.int32)
    rows = first_row[:, None] + steps[None, :]
    valid = (first_pos[:, None] + seq_count * steps[None, :]) < owner_count[:, None]
    rows = jnp.clip(rows, 0, group_rows - 1)
    outgoing = jnp.take(held, rows.reshape(-1), axis=0).reshape(seq_count, per_owner, out_cols)
    outgoing = jnp.where(valid[:, :, None], outgoing, jnp.zeros((), outgoing.dtype))
    received = lax.all_to_all(outgoing, "seq", split_axis=0, concat_axis=0, tiled=True)
    own_image = jnp.sum(jnp.where(image_slot == device, image_ids, 0))
    own_start = starts[own_image]
    order = jnp.mod(own_start + jnp.arange(seq_count, dtype=jnp.int32), seq_count)
    placed = jnp.take(received, order, axis=0).transpose(1, 0, 2)
    return placed.reshape(most_rows, out_cols)


def shards(
    tokens,
    group_image,
    image_slot,
    attention_gain,
    query_weight,
    key_weight,
    value_weight,
    output_weight,
    feedforward_gain,
    up_weight,
    down_weight,
    merge_gain,
    merge_weight,
):
    device = lax.axis_index("seq")
    seq_count = lax.axis_size("seq")
    token_rows = tokens.shape[0]
    group_rows = group_image.shape[0]
    group_total = group_rows * seq_count
    image_count = image_slot.shape[0]
    image_ids = jnp.arange(image_count, dtype=jnp.int32)
    local_counts = jnp.sum(
        (group_image[:, None] == image_ids[None, :]).astype(jnp.int32), axis=0
    )
    every_count = lax.all_to_all(
        jnp.broadcast_to(local_counts[None, :], (seq_count, image_count)),
        "seq",
        split_axis=0,
        concat_axis=0,
        tiled=True,
    )
    counts = jnp.sum(every_count, axis=0)
    query_image = jnp.repeat(group_image, 4)
    residual = tokens.astype(jnp.float32)
    normed = full_norm(residual, attention_gain)
    head_count = query_weight.shape[1] // HD
    queries = jnp.dot(normed, query_weight, preferred_element_type=jnp.float32).astype(jnp.bfloat16)
    key_rows = jnp.dot(normed, key_weight, preferred_element_type=jnp.float32).astype(jnp.bfloat16)
    value_rows = jnp.dot(normed, value_weight, preferred_element_type=jnp.float32).astype(
        jnp.bfloat16
    )
    query_heads = queries.reshape(token_rows, head_count, HD)
    key_value = jnp.stack([key_rows, value_rows])
    counts, key_value = lax.optimization_barrier((counts, key_value))
    starts = jnp.cumsum(counts) - counts

    def images_of_block(source):
        groups = source * group_rows + jnp.arange(group_rows, dtype=jnp.int32)
        return jnp.repeat(image_of_groups(groups, starts, group_total), 4)

    state = attend_own_block(
        query_heads,
        key_value[0].reshape(token_rows, head_count, HD),
        key_value[1].reshape(token_rows, head_count, HD),
        query_image,
        query_image,
    )
    near = {step: shifted(key_value, "seq", step) for step in (1, -1, 2, -2)}
    far = {
        3: shifted(near[2], "seq", 1),
        -3: shifted(near[-2], "seq", -1),
        4: shifted(near[2], "seq", 2),
        -4: shifted(near[-2], "seq", -2),
    }
    arrived = {**near, **far}
    for step in (1, -1, 2, -2, 3, -3, 4, -4):
        block = arrived[step]
        source = device - step
        if step > 0:
            needed = lambda k: k[-1] == query_image[0]
        else:
            needed = lambda k: k[0] == query_image[-1]
        key_image = images_of_block(source)
        state = lax.cond(
            needed(key_image),
            lambda st, blk, kim: attend_more(
                st,
                query_heads,
                blk[0].reshape(token_rows, head_count, HD),
                blk[1].reshape(token_rows, head_count, HD),
                query_image,
                kim,
            ),
            lambda st, blk, kim: st,
            state,
            block,
            key_image,
        )
    row_best, row_total, weighted = state
    context = jnp.transpose(weighted / row_total, (1, 0, 2))
    context = context.astype(jnp.bfloat16).reshape(token_rows, head_count * HD)
    tp_count = lax.axis_size("tp")
    own_rows = token_rows // tp_count
    me = lax.axis_index("tp")
    own_residual = lax.dynamic_slice_in_dim(residual, me * own_rows, own_rows, 0)
    context_pieces = context.reshape(tp_count, own_rows, head_count * HD)
    attention_out = jnp.dot(context_pieces[me], output_weight, preferred_element_type=jnp.float32)
    for steps in range(1, tp_count):
        outgoing = jnp.dot(
            lax.dynamic_index_in_dim(context_pieces, (me + steps) % tp_count, 0, keepdims=False),
            output_weight,
            preferred_element_type=jnp.float32,
        ).astype(jnp.bfloat16)
        attention_out = attention_out + tp_shift(outgoing, steps).astype(jnp.float32)
    after_attention = own_residual + attention_out

    def feed_forward(rows):
        hidden = jax.nn.gelu(
            jnp.dot(rows, up_weight, preferred_element_type=jnp.float32), approximate=False
        ).astype(jnp.bfloat16)
        return jnp.dot(hidden, down_weight, preferred_element_type=jnp.float32)

    normed_two = full_norm(after_attention, feedforward_gain)
    visiting = [tp_shift(normed_two, steps) for steps in range(1, tp_count)]
    ff_total = feed_forward(normed_two)
    for steps, rows in zip(range(1, tp_count), visiting):
        returned = tp_shift(feed_forward(rows).astype(jnp.bfloat16), -steps)
        ff_total = ff_total + returned.astype(jnp.float32)
    after_feedforward = after_attention + ff_total
    normed_three = full_norm(after_feedforward, merge_gain)
    own_groups = normed_three.reshape(own_rows // 4, 4 * D)

    def merge(groups):
        return jnp.dot(groups, merge_weight, preferred_element_type=jnp.float32).astype(
            jnp.bfloat16
        )

    merged = [merge(own_groups)] + [
        merge(tp_shift(own_groups, steps)) for steps in range(1, tp_count)
    ]
    order = (me - jnp.arange(tp_count, dtype=jnp.int32)) % tp_count
    projected = jnp.take(jnp.stack(merged), order, axis=0).reshape(group_rows, -1)
    return route_to_owners(projected, starts, counts, image_slot, device, seq_count)[None]


def solution(mesh):
    return jax.shard_map(
        shards,
        mesh=mesh,
        in_specs=(
            P("seq", None),
            P("seq"),
            P(),
            P(),
            P(None, "tp"),
            P(None, "tp"),
            P(None, "tp"),
            P("tp", None),
            P(),
            P(None, "tp"),
            P("tp", None),
            P(),
            P(None, "tp"),
        ),
        out_specs=P("seq", None, "tp"),
        check_vma=False,
    )
```

```python
import jax
import jax.numpy as jnp
from jax import lax
from jax.sharding import PartitionSpec as P

D = 1408
HD = 88
REACH = 4


epsilon = 1e-06
masked_score = -1e30


def shifted(value, axis, steps):
    count = lax.axis_size(axis)
    initial, last = (max(0, -steps), min(count, count - steps))
    return lax.ppermute(value, axis, [(source, source + steps) for source in range(initial, last)])


def finish_norm(hidden, row_mean, square, norm_gain):
    return (
        (hidden - row_mean) * lax.rsqrt(square - row_mean * row_mean + epsilon) * norm_gain
    ).astype(jnp.bfloat16)


def full_norm(hidden, norm_gain):
    row_mean = jnp.mean(hidden, axis=1, keepdims=True)
    square = jnp.mean(hidden * hidden, axis=1, keepdims=True)
    return finish_norm(hidden, row_mean, square, norm_gain)


def tp_shift(value, steps):
    count = lax.axis_size("tp")
    return lax.ppermute(value, "tp", [(u, (u + steps) % count) for u in range(count)])


def sum_rows(partial_value):
    tp_count = lax.axis_size("tp")
    me = lax.axis_index("tp")
    rows, cols = partial_value.shape
    pieces = partial_value.astype(jnp.bfloat16).reshape(tp_count, rows // tp_count, cols)
    total = lax.dynamic_index_in_dim(pieces, me, 0, keepdims=False).astype(jnp.float32)
    for steps in range(1, tp_count):
        outgoing = lax.dynamic_index_in_dim(pieces, (me + steps) % tp_count, 0, keepdims=False)
        total = total + tp_shift(outgoing, steps).astype(jnp.float32)
    return total


def gather_rows(row_block):
    tp_count = lax.axis_size("tp")
    me = lax.axis_index("tp")
    arrived = [row_block] + [tp_shift(row_block, steps) for steps in range(1, tp_count)]
    order = (me - jnp.arange(tp_count, dtype=jnp.int32)) % tp_count
    placed = jnp.take(jnp.stack(arrived), order, axis=0)
    return placed.reshape(tp_count * row_block.shape[0], row_block.shape[1])


def block_scores(query_heads, key_heads, query_image, key_image):
    scores = jnp.einsum(
        "qhd,khd->hqk", query_heads, key_heads, preferred_element_type=jnp.float32
    ) * HD ** (-0.5)
    same_image = query_image[:, None] == key_image[None, :]
    return jnp.where(same_image[None], scores, masked_score)


def block_values(weights, value_heads):
    return jnp.einsum(
        "hqk,khd->hqd",
        weights.astype(jnp.bfloat16),
        value_heads,
        preferred_element_type=jnp.float32,
    )


def attend_own_block(query_heads, key_heads, value_heads, query_image, key_image):
    scores = block_scores(query_heads, key_heads, query_image, key_image)
    row_best = jnp.max(scores, axis=2, keepdims=True)
    weights = jnp.exp(scores - row_best)
    row_total = jnp.sum(weights, axis=2, keepdims=True)
    return row_best, row_total, block_values(weights, value_heads)


def attend_more(state, query_heads, key_heads, value_heads, query_image, key_image):
    row_best, row_total, weighted = state
    scores = block_scores(query_heads, key_heads, query_image, key_image)
    new_best = jnp.maximum(row_best, jnp.max(scores, axis=2, keepdims=True))
    rescale = jnp.exp(row_best - new_best)
    weights = jnp.exp(scores - new_best)
    row_total = row_total * rescale + jnp.sum(weights, axis=2, keepdims=True)
    weighted = weighted * rescale + block_values(weights, value_heads)
    return new_best, row_total, weighted


def image_of_groups(groups, starts, group_total):
    inside = (groups >= 0) & (groups < group_total)
    image = jnp.sum((starts[None, :] <= groups[:, None]).astype(jnp.int32), axis=1) - 1
    return jnp.where(inside, image, -1)


def route_to_owners(projected, starts, counts, image_slot, device, seq_count):
    group_rows, out_cols = projected.shape
    per_pair = group_rows // seq_count
    spread = projected.reshape(per_pair, seq_count, out_cols).transpose(1, 0, 2)
    spread = lax.all_to_all(spread, "seq", split_axis=0, concat_axis=0, tiled=True)
    held = spread.reshape(group_rows, out_cols)
    image_count = image_slot.shape[0]
    most_rows = REACH * group_rows
    per_owner = most_rows // seq_count
    image_ids = jnp.arange(image_count, dtype=jnp.int32)
    owners = jnp.arange(seq_count, dtype=jnp.int32)
    owned_image = jnp.sum(
        jnp.where(image_slot[None, :] == owners[:, None], image_ids[None, :], 0), axis=1
    )
    owner_start = starts[owned_image]
    owner_count = counts[owned_image]
    first_pos = jnp.mod(device - owner_start, seq_count)
    first_row = (owner_start + first_pos - device) // seq_count
    steps = jnp.arange(per_owner, dtype=jnp.int32)
    rows = first_row[:, None] + steps[None, :]
    valid = (first_pos[:, None] + seq_count * steps[None, :]) < owner_count[:, None]
    rows = jnp.clip(rows, 0, group_rows - 1)
    outgoing = jnp.take(held, rows.reshape(-1), axis=0).reshape(seq_count, per_owner, out_cols)
    outgoing = jnp.where(valid[:, :, None], outgoing, jnp.zeros((), outgoing.dtype))
    received = lax.all_to_all(outgoing, "seq", split_axis=0, concat_axis=0, tiled=True)
    own_image = jnp.sum(jnp.where(image_slot == device, image_ids, 0))
    own_start = starts[own_image]
    order = jnp.mod(own_start + jnp.arange(seq_count, dtype=jnp.int32), seq_count)
    placed = jnp.take(received, order, axis=0).transpose(1, 0, 2)
    return placed.reshape(most_rows, out_cols)


def shards(
    tokens,
    group_image,
    image_slot,
    attention_gain,
    query_weight,
    key_weight,
    value_weight,
    output_weight,
    feedforward_gain,
    up_weight,
    down_weight,
    merge_gain,
    merge_weight,
):
    device = lax.axis_index("seq")
    seq_count = lax.axis_size("seq")
    token_rows = tokens.shape[0]
    group_rows = group_image.shape[0]
    group_total = group_rows * seq_count
    image_count = image_slot.shape[0]
    image_ids = jnp.arange(image_count, dtype=jnp.int32)
    local_counts = jnp.sum(
        (group_image[:, None] == image_ids[None, :]).astype(jnp.int32), axis=0
    )
    every_count = lax.all_to_all(
        jnp.broadcast_to(local_counts[None, :], (seq_count, image_count)),
        "seq",
        split_axis=0,
        concat_axis=0,
        tiled=True,
    )
    counts = jnp.sum(every_count, axis=0)
    query_image = jnp.repeat(group_image, 4)
    residual = tokens.astype(jnp.float32)
    normed = full_norm(residual, attention_gain)
    head_count = query_weight.shape[1] // HD
    queries = jnp.dot(normed, query_weight, preferred_element_type=jnp.float32).astype(jnp.bfloat16)
    key_rows = jnp.dot(normed, key_weight, preferred_element_type=jnp.float32).astype(jnp.bfloat16)
    value_rows = jnp.dot(normed, value_weight, preferred_element_type=jnp.float32).astype(
        jnp.bfloat16
    )
    query_heads = queries.reshape(token_rows, head_count, HD)
    key_value = jnp.stack([key_rows, value_rows])
    counts, key_value = lax.optimization_barrier((counts, key_value))
    starts = jnp.cumsum(counts) - counts

    def images_of_block(source):
        groups = source * group_rows + jnp.arange(group_rows, dtype=jnp.int32)
        return jnp.repeat(image_of_groups(groups, starts, group_total), 4)

    state = attend_own_block(
        query_heads,
        key_value[0].reshape(token_rows, head_count, HD),
        key_value[1].reshape(token_rows, head_count, HD),
        query_image,
        query_image,
    )
    near = {step: shifted(key_value, "seq", step) for step in (1, -1, 2, -2)}
    far = {
        3: shifted(near[2], "seq", 1),
        -3: shifted(near[-2], "seq", -1),
        4: shifted(near[2], "seq", 2),
        -4: shifted(near[-2], "seq", -2),
    }
    arrived = {**near, **far}
    for step in (2, -2, 1, -1, 3, -3, 4, -4):
        block = arrived[step]
        source = device - step
        if step > 0:
            needed = lambda k: k[-1] == query_image[0]
        else:
            needed = lambda k: k[0] == query_image[-1]
        key_image = images_of_block(source)
        state = lax.cond(
            needed(key_image),
            lambda st, blk, kim: attend_more(
                st,
                query_heads,
                blk[0].reshape(token_rows, head_count, HD),
                blk[1].reshape(token_rows, head_count, HD),
                query_image,
                kim,
            ),
            lambda st, blk, kim: st,
            state,
            block,
            key_image,
        )
    row_best, row_total, weighted = state
    context = jnp.transpose(weighted / row_total, (1, 0, 2))
    context = context.astype(jnp.bfloat16).reshape(token_rows, head_count * HD)
    attention_part = jnp.dot(context, output_weight, preferred_element_type=jnp.float32)
    tp_count = lax.axis_size("tp")
    own_rows = token_rows // tp_count
    own_residual = lax.dynamic_slice_in_dim(residual, lax.axis_index("tp") * own_rows, own_rows, 0)
    after_attention = own_residual + sum_rows(attention_part)
    me = lax.axis_index("tp")

    def feed_forward(rows):
        hidden = jax.nn.gelu(
            jnp.dot(rows, up_weight, preferred_element_type=jnp.float32), approximate=False
        ).astype(jnp.bfloat16)
        return jnp.dot(hidden, down_weight, preferred_element_type=jnp.float32)

    normed_two = full_norm(after_attention, feedforward_gain)
    visiting = [tp_shift(normed_two, steps) for steps in range(1, tp_count)]
    ff_total = feed_forward(normed_two)
    for steps, rows in zip(range(1, tp_count), visiting):
        returned = tp_shift(feed_forward(rows).astype(jnp.bfloat16), -steps)
        ff_total = ff_total + returned.astype(jnp.float32)
    after_feedforward = after_attention + ff_total
    normed_three = full_norm(after_feedforward, merge_gain)
    own_groups = normed_three.reshape(own_rows // 4, 4 * D)

    def merge(groups):
        return jnp.dot(groups, merge_weight, preferred_element_type=jnp.float32).astype(
            jnp.bfloat16
        )

    merged = [merge(own_groups)] + [
        merge(tp_shift(own_groups, steps)) for steps in range(1, tp_count)
    ]
    order = (me - jnp.arange(tp_count, dtype=jnp.int32)) % tp_count
    projected = jnp.take(jnp.stack(merged), order, axis=0).reshape(group_rows, -1)
    return route_to_owners(projected, starts, counts, image_slot, device, seq_count)[None]


def solution(mesh):
    return jax.shard_map(
        shards,
        mesh=mesh,
        in_specs=(
            P("seq", None),
            P("seq"),
            P(),
            P(),
            P(None, "tp"),
            P(None, "tp"),
            P(None, "tp"),
            P("tp", None),
            P(),
            P(None, "tp"),
            P("tp", None),
            P(),
            P(None, "tp"),
        ),
        out_specs=P("seq", None, "tp"),
        check_vma=False,
    )
```
